32 devices in a mesh: real: 2 (over x), los: 8 (over z, y), sky: 2 (over core).
Axes of the slice: x: 2, y: 2, z: 4, core: 2. Of those that a mesh axis runs over, the one named last changes fastest.
Arguments:
- density: float32 [16, 2048, 2048], P(('real', 'los'), 'sky'), parts along dimension 0, may hold values from -6 to 8
- lens_weight: float32 [16], P(('real', 'los')), parts along dimension 0, may hold values from 0.05 to 0.4
- plane_count: int32 [16], P(('real', 'los')), parts along dimension 0, may hold values from 0 to 1
- ray_state: float32 [16, 12, 32, 2048], P(('real', 'los'), None, 'sky'), parts along dimension 0, may hold values from -6 to 6
Outputs:
- ray_out: float32 [16, 12, 32, 2048], P(('real', 'los'), None, 'sky'), parts along dimension 0
The draws below stay inside these ranges and needn't reach their ends.
There are 2 independent parts, one for each index of `real`. The reference program is written for one: setup_inputs(seed, part) draws one part's arguments, and reference() takes and returns one part's arrays. A program takes and returns all parts, laid end to end along the dimension named above; each array names one. Nothing has to cross between parts.
All inputs are finite; a program needn't handle non-finite values.
Results may differ from the reference program's by a relative error of at most 0.00012.
Values sent between devices are 32-bit elements; how exact they have to be, the bound alone decides.
No kernel may reach another device: no remote copies, remote signals or barrier semaphores. Data moves between devices by JAX's collectives and lax.ppermute only.
A program may use at most 128 MiB of HBM per device.

```python
import math
import jax
import jax.numpy as jnp
from jax import lax

G = 2048
RAY_ROWS = 32
HOPS = 4
SLABS = 8


def draw_density(key, part):
    key_rough = jax.random.fold_in(key, 0)
    return jnp.clip(jax.random.normal(key_rough, (SLABS, G, G), jnp.float32), -6.0, 6.0)


def with_ends(result, own_key, smallest, high):
    extent = result.shape
    index_at = [jax.random.randint(jax.random.fold_in(own_key, axis), (), 0, extent[axis]) for axis in range(len(extent))]
    result = result.at[tuple(index_at)].set(smallest)
    longest = extent.index(max(extent))
    index_at[longest] = (index_at[longest] + 1) % extent[longest]
    return result.at[tuple(index_at)].set(high)


def shard_levels(own_key, dims, cuts, low, largest):
    factor_of, own = 1.0, jax.random.fold_in(own_key, 6)
    for position, shards_of in cuts:
        heights = jnp.exp(jax.random.uniform(jax.random.fold_in(own, position), (shards_of,), jnp.float32, low / len(cuts), largest / len(cuts)))
        factor_of = factor_of * jnp.repeat(heights, dims[position] // shards_of).reshape([-1 if axis == position else 1 for axis in range(len(dims))])
    return factor_of


def bell_draw(rng, dims, deviation, limit, shards=(), kind=jnp.bfloat16):
    values = jax.random.normal(rng, dims, jnp.float32) * deviation
    if len(shards) > 0:
        values = shard_levels(rng, dims, shards, -0.22, 0.18) * values
    return jnp.clip(values, min=-limit, max=limit).astype(kind)


def setup_inputs(seed: int = 0, part: int = 0) -> dict:
    arg_keys = jax.random.split(jax.random.key(seed), 5)
    own_keys = jax.random.split(jax.random.fold_in(arg_keys[4], part), 5)
    density = draw_density(jax.random.fold_in(jax.random.fold_in(arg_keys[4], part), 71), part)
    lens_weight = jnp.clip(jnp.exp(math.log(0.4) - 2.0794415 * jax.random.uniform(own_keys[1], (SLABS,), jnp.float32) ** shard_levels(own_keys[1], (SLABS,), ((0, 8),), -0.2, 0.2)), 0.05, 0.4)
    plane_count = with_ends(jax.random.randint(own_keys[2], (SLABS,), 0, 2), jax.random.fold_in(own_keys[2], 1), 0, 1).astype(jnp.int32)
    ray_state = bell_draw(own_keys[3], (SLABS, 12, RAY_ROWS, G), 1.0, 6.0, ((0, 8), (2, 2)), jnp.float32)
    return dict(density=density, lens_weight=lens_weight, plane_count=plane_count, ray_state=ray_state)


two_pi = 2.0 * math.pi


def lens_step(ray_tile, fields):
    disp_x = ray_tile[..., 0, :, :]
    disp_y = ray_tile[..., 1, :, :]
    tilt_x = ray_tile[..., 2, :, :]
    tilt_y = ray_tile[..., 3, :, :]
    jac_xx = ray_tile[..., 4, :, :]
    jac_xy = ray_tile[..., 5, :, :]
    jac_yx = ray_tile[..., 6, :, :]
    jac_yy = ray_tile[..., 7, :, :]
    rate_xx = ray_tile[..., 8, :, :]
    rate_xy = ray_tile[..., 9, :, :]
    rate_yx = ray_tile[..., 10, :, :]
    rate_yy = ray_tile[..., 11, :, :]
    bend_x = fields[..., 0, :, :]
    bend_y = fields[..., 1, :, :]
    hess_xx = fields[..., 2, :, :]
    hess_yy = fields[..., 3, :, :]
    hess_xy = fields[..., 4, :, :]
    push_x = bend_x + hess_xx * disp_x + hess_xy * disp_y
    push_y = bend_y + hess_xy * disp_x + hess_yy * disp_y
    new_tilt_x = tilt_x - push_x
    new_tilt_y = tilt_y - push_y
    new_disp_x = disp_x + new_tilt_x
    new_disp_y = disp_y + new_tilt_y
    new_rate_xx = rate_xx - (hess_xx * jac_xx + hess_xy * jac_yx)
    new_rate_xy = rate_xy - (hess_xx * jac_xy + hess_xy * jac_yy)
    new_rate_yx = rate_yx - (hess_xy * jac_xx + hess_yy * jac_yx)
    new_rate_yy = rate_yy - (hess_xy * jac_xy + hess_yy * jac_yy)
    new_jac_xx = jac_xx + new_rate_xx
    new_jac_xy = jac_xy + new_rate_xy
    new_jac_yx = jac_yx + new_rate_yx
    new_jac_yy = jac_yy + new_rate_yy
    return jnp.stack([new_disp_x, new_disp_y, new_tilt_x, new_tilt_y,
                      new_jac_xx, new_jac_xy, new_jac_yx, new_jac_yy,
                      new_rate_xx, new_rate_xy, new_rate_yx, new_rate_yy], axis=-3)


def plane_fields(packed_args):
    plane_cells, strength = packed_args
    length = plane_cells.shape[-1]
    spectrum = jnp.fft.fft2(plane_cells)
    indices = jnp.arange(length, dtype=jnp.int32)
    signed = jnp.where(indices < length // 2, indices, indices - length)
    waves = (two_pi / length) * signed.astype(jnp.float32)
    retain_one = indices != length // 2
    wave_row = waves[:, None]
    wave_col = waves[None, :]
    squared = wave_col * wave_col + wave_row * wave_row
    retain = retain_one[:, None] & retain_one[None, :] & (squared > 0.0)
    safe_sq = jnp.where(retain, squared, 1.0)
    potential = jnp.where(retain, -2.0 / safe_sq, 0.0) * spectrum
    first_pair = jnp.fft.ifft2((1j * wave_col - wave_row) * potential)
    second_pair = jnp.fft.ifft2((-wave_col * wave_col - 1j * (wave_row * wave_row)) * potential)
    third_pair = jnp.fft.ifft2((-wave_col * wave_row) * potential)
    ray_rows = jnp.arange(RAY_ROWS, dtype=jnp.int32) * (length // RAY_ROWS)
    stacked = jnp.stack([first_pair.real, first_pair.imag, second_pair.real,
                         second_pair.imag, third_pair.real])
    return stacked[:, ray_rows, :] * strength


def reference(density, lens_weight, plane_count, ray_state):
    strength = lens_weight * plane_count.astype(jnp.float32)
    fields = lax.map(plane_fields, (density, strength))
    ray_tile = ray_state
    for step_index in range(HOPS):
        ray_tile = lens_step(ray_tile, fields)
        ray_tile = jnp.roll(ray_tile, 1, axis=0)
    return ray_tile
```

```python
import math

import jax
import jax.numpy as jnp
from jax import lax
from jax.sharding import PartitionSpec as P

HOPS = 4


two_pi = 2.0 * math.pi
highest = lax.Precision.HIGHEST
first_radix = 16


def shifted(block, axis, distance):
    devices = range(lax.axis_size(axis))
    route = [((i - distance) % len(devices), i) for i in devices]
    return lax.ppermute(block, axis, route)


def lens_step(ray_tile, fields):
    disp_x = ray_tile[..., 0, :, :]
    disp_y = ray_tile[..., 1, :, :]
    tilt_x = ray_tile[..., 2, :, :]
    tilt_y = ray_tile[..., 3, :, :]
    jac_xx = ray_tile[..., 4, :, :]
    jac_xy = ray_tile[..., 5, :, :]
    jac_yx = ray_tile[..., 6, :, :]
    jac_yy = ray_tile[..., 7, :, :]
    rate_xx = ray_tile[..., 8, :, :]
    rate_xy = ray_tile[..., 9, :, :]
    rate_yx = ray_tile[..., 10, :, :]
    rate_yy = ray_tile[..., 11, :, :]
    bend_x = fields[..., 0, :, :]
    bend_y = fields[..., 1, :, :]
    hess_xx = fields[..., 2, :, :]
    hess_yy = fields[..., 3, :, :]
    hess_xy = fields[..., 4, :, :]
    push_x = bend_x + hess_xx * disp_x + hess_xy * disp_y
    push_y = bend_y + hess_xy * disp_x + hess_yy * disp_y
    new_tilt_x = tilt_x - push_x
    new_tilt_y = tilt_y - push_y
    new_disp_x = disp_x + new_tilt_x
    new_disp_y = disp_y + new_tilt_y
    new_rate_xx = rate_xx - (hess_xx * jac_xx + hess_xy * jac_yx)
    new_rate_xy = rate_xy - (hess_xx * jac_xy + hess_xy * jac_yy)
    new_rate_yx = rate_yx - (hess_xy * jac_xx + hess_yy * jac_yx)
    new_rate_yy = rate_yy - (hess_xy * jac_xy + hess_yy * jac_yy)
    new_jac_xx = jac_xx + new_rate_xx
    new_jac_xy = jac_xy + new_rate_xy
    new_jac_yx = jac_yx + new_rate_yx
    new_jac_yy = jac_yy + new_rate_yy
    return jnp.stack(
        [
            new_disp_x,
            new_disp_y,
            new_tilt_x,
            new_tilt_y,
            new_jac_xx,
            new_jac_xy,
            new_jac_yx,
            new_jac_yy,
            new_rate_xx,
            new_rate_xy,
            new_rate_yx,
            new_rate_yy,
        ],
        axis=-3,
    )


def phase_table(left_idx, right_idx, modulus, orient):
    product = left_idx[:, None] * right_idx[None, :] % modulus
    angle = orient * two_pi / modulus * product.astype(jnp.float32)
    return (jnp.cos(angle), jnp.sin(angle))


def block_table(left_idx, right_idx, modulus, orient):
    t_re, t_im = phase_table(left_idx, right_idx, modulus, orient)
    top = jnp.concatenate([t_re, t_im], axis=1)
    bottom = jnp.concatenate([-t_im, t_re], axis=1)
    return jnp.concatenate([top, bottom], axis=0)


def mixed(form, left_op, right_op):
    return jnp.einsum(
        form, left_op, right_op, precision=highest, preferred_element_type=jnp.float32
    )


def complex_product(form, real_in, imag_in, table_re, table_im):
    if imag_in is None:
        return (mixed(form, real_in, table_re), mixed(form, real_in, table_im))
    out_re = mixed(form, real_in, table_re) - mixed(form, imag_in, table_im)
    out_im = mixed(form, real_in, table_im) + mixed(form, imag_in, table_re)
    return (out_re, out_im)


def first_factor_of(length):
    factor_one = 1
    while factor_one * factor_one < length and length % (factor_one * 2) == 0:
        factor_one = factor_one * 2
    return factor_one


def rows_forward(cells):
    row_count, length = cells.shape
    second = length // first_radix
    half = second // 2
    shaped = cells.reshape(row_count, first_radix, second)
    v_idx = jnp.arange(first_radix, dtype=jnp.int32)
    u_idx = jnp.arange(second, dtype=jnp.int32)
    m_idx = jnp.arange(half, dtype=jnp.int32)
    section_re, section_im = phase_table(v_idx, v_idx, first_radix, -1.0)
    section = jnp.concatenate([section_re, section_im], axis=1)
    part = mixed("rvu,vk->rku", shaped, section)
    part_re = part[:, :first_radix]
    part_im = part[:, first_radix:]
    twist_re, twist_im = phase_table(v_idx, u_idx, length, -1.0)
    turned_re = part_re * twist_re - part_im * twist_im
    turned_im = part_re * twist_im + part_im * twist_re
    turned = jnp.concatenate([turned_re, turned_im], axis=2)
    final = block_table(u_idx, m_idx, second, -1.0)
    return mixed("rkj,jn->rkn", turned, final)


def columns_forward(spread_re, spread_im):
    length, col_count = spread_re.shape
    factor_one = first_factor_of(length)
    second = length // factor_one
    first_idx = jnp.arange(factor_one, dtype=jnp.int32)
    second_idx = jnp.arange(second, dtype=jnp.int32)
    stacked = jnp.concatenate(
        [
            spread_re.reshape(factor_one, second * col_count),
            spread_im.reshape(factor_one, second * col_count),
        ],
        axis=0,
    )
    section = block_table(first_idx, first_idx, factor_one, -1.0)
    part = mixed("jn,jc->nc", section, stacked).reshape(2, factor_one, second, col_count)
    twist_re, twist_im = phase_table(first_idx, second_idx, length, -1.0)
    twist_re = twist_re[:, :, None]
    twist_im = twist_im[:, :, None]
    turned_re = part[0] * twist_re - part[1] * twist_im
    turned_im = part[0] * twist_im + part[1] * twist_re
    turned = jnp.stack([turned_re, turned_im], axis=1).reshape(
        factor_one, 2 * second, col_count
    )
    final = block_table(second_idx, second_idx, second, -1.0)
    done = mixed("jn,kjc->nkc", final, turned)
    return done.reshape(2, length, col_count)


def rows_inverse(spec_re, spec_im, length, m_count):
    row_count = spec_re.shape[0]
    second = length // first_radix
    shaped_re = spec_re.reshape(row_count, first_radix, m_count)
    shaped_im = spec_im.reshape(row_count, first_radix, m_count)
    k_idx = jnp.arange(first_radix, dtype=jnp.int32)
    u_idx = jnp.arange(second, dtype=jnp.int32)
    m_idx = jnp.arange(m_count, dtype=jnp.int32)
    section_re, section_im = phase_table(m_idx, u_idx, second, 1.0)
    part_re, part_im = complex_product("rkm,mu->rku", shaped_re, shaped_im, section_re, section_im)
    twist_re, twist_im = phase_table(k_idx, u_idx, length, 1.0)
    turned_re = part_re * twist_re - part_im * twist_im
    turned_im = part_re * twist_im + part_im * twist_re
    final_re, final_im = phase_table(k_idx, k_idx, first_radix, 1.0)
    done_re, done_im = complex_product("rku,kv->rvu", turned_re, turned_im, final_re, final_im)
    return (done_re.reshape(row_count, length), done_im.reshape(row_count, length))


def wavenumbers(indices, length):
    signed = jnp.where(indices < length // 2, indices, indices - length)
    return (two_pi / length * signed.astype(jnp.float32), indices != length // 2)


def folded_spectra(spectrum, col_idx, ray_all):
    _, length, col_count = spectrum.shape
    norm_factor = float(length * length)
    wave_col, retain_col = wavenumbers(col_idx, length)
    weight = jnp.where(col_idx == 0, 1.0, 2.0).astype(jnp.float32)
    row_idx = jnp.arange(length, dtype=jnp.int32)
    wave_row, retain_row = wavenumbers(row_idx, length)
    wave_row = wave_row[:, None]
    squared = wave_col[None, :] * wave_col[None, :] + wave_row * wave_row
    retain = retain_row[:, None] & retain_col[None, :] & (squared > 0.0)
    safe_sq = jnp.where(retain, squared, 1.0)
    kernel = jnp.where(retain, -2.0 / (safe_sq * norm_factor), 0.0) * weight[None, :]
    phi = kernel[None] * spectrum
    terms = jnp.stack([phi, wave_row[None] * phi, (wave_row * wave_row)[None] * phi])
    terms = terms.reshape(3, 2, length // ray_all, ray_all, col_count)
    return jnp.sum(terms, axis=2)


def per_device(density, lens_weight, plane_count, ray_state):
    sky_count = lax.axis_size("sky")
    sky_index = lax.axis_index("sky")
    ray_tile = shifted(ray_state, "los", HOPS)
    plane_cells = density[0]
    length = plane_cells.shape[1]
    second = length // first_radix
    half = second // 2
    ray_dev = ray_state.shape[2]
    ray_all = ray_dev * sky_count
    strength = lens_weight[0] * plane_count[0].astype(jnp.float32)
    rows = rows_forward(plane_cells)
    spread = lax.all_to_all(rows, "sky", split_axis=1, concat_axis=0, tiled=True)
    k_local = spread.shape[1]
    spread_re = spread[:, :, :half].reshape(length, k_local * half)
    spread_im = spread[:, :, half:].reshape(length, k_local * half)
    spectrum = columns_forward(spread_re, spread_im)
    position = jnp.arange(k_local * half, dtype=jnp.int32)
    col_idx = sky_index * k_local + position // half + first_radix * (position % half)
    folds = folded_spectra(spectrum, col_idx, ray_all)
    q_idx = jnp.arange(ray_all, dtype=jnp.int32)
    back = block_table(q_idx, q_idx, ray_all, 1.0)
    at_rows = mixed("pjc,jn->pnc", folds.reshape(3, 2 * ray_all, k_local * half), back)
    at_rows = at_rows.reshape(3, 2, ray_all, k_local, half)
    returned = lax.all_to_all(at_rows, "sky", split_axis=2, concat_axis=3, tiled=True)
    k_all = returned.shape[3]
    kx_idx = jnp.arange(k_all, dtype=jnp.int32)[:, None] + first_radix * jnp.arange(
        half, dtype=jnp.int32
    )[None, :]
    wave_col = wavenumbers(kx_idx, length)[0]
    f0_re, f0_im = returned[0, 0], returned[0, 1]
    f1_re, f1_im = returned[1, 0], returned[1, 1]
    f2_re, f2_im = returned[2, 0], returned[2, 1]
    col_sq = wave_col * wave_col
    all_re = jnp.stack(
        [-wave_col * f0_im, -f1_im, -col_sq * f0_re, -f2_re, -wave_col * f1_re]
    )
    all_im = jnp.stack(
        [wave_col * f0_re, f1_re, -col_sq * f0_im, -f2_im, -wave_col * f1_im]
    )
    flat_re = all_re.reshape(5 * ray_dev, k_all * half)
    flat_im = all_im.reshape(5 * ray_dev, k_all * half)
    field_re, _ = rows_inverse(flat_re, flat_im, length, half)
    fields = field_re.reshape(5, ray_dev, length) * strength
    for step_index in range(HOPS):
        current = shifted(fields, "los", HOPS - step_index)
        ray_tile = lens_step(ray_tile, current[None])
    return ray_tile


def solution(mesh):
    return jax.shard_map(
        per_device,
        mesh=mesh,
        in_specs=(
            P(("real", "los"), "sky", None),
            P(("real", "los")),
            P(("real", "los")),
            P(("real", "los"), None, "sky", None),
        ),
        out_specs=P(("real", "los"), None, "sky", None),
        check_vma=False,
    )
```

```python
import math

import jax
import jax.numpy as jnp
from jax import lax
from jax.sharding import PartitionSpec as P

HOPS = 4


two_pi = 2.0 * math.pi
highest = lax.Precision.HIGHEST
first_radix = 16


def shifted(block, axis, distance):
    devices = range(lax.axis_size(axis))
    route = [((i - distance) % len(devices), i) for i in devices]
    return lax.ppermute(block, axis, route)


def lens_step(ray_tile, fields):
    disp_x = ray_tile[..., 0, :, :]
    disp_y = ray_tile[..., 1, :, :]
    tilt_x = ray_tile[..., 2, :, :]
    tilt_y = ray_tile[..., 3, :, :]
    jac_xx = ray_tile[..., 4, :, :]
    jac_xy = ray_tile[..., 5, :, :]
    jac_yx = ray_tile[..., 6, :, :]
    jac_yy = ray_tile[..., 7, :, :]
    rate_xx = ray_tile[..., 8, :, :]
    rate_xy = ray_tile[..., 9, :, :]
    rate_yx = ray_tile[..., 10, :, :]
    rate_yy = ray_tile[..., 11, :, :]
    bend_x = fields[..., 0, :, :]
    bend_y = fields[..., 1, :, :]
    hess_xx = fields[..., 2, :, :]
    hess_yy = fields[..., 3, :, :]
    hess_xy = fields[..., 4, :, :]
    push_x = bend_x + hess_xx * disp_x + hess_xy * disp_y
    push_y = bend_y + hess_xy * disp_x + hess_yy * disp_y
    new_tilt_x = tilt_x - push_x
    new_tilt_y = tilt_y - push_y
    new_disp_x = disp_x + new_tilt_x
    new_disp_y = disp_y + new_tilt_y
    new_rate_xx = rate_xx - (hess_xx * jac_xx + hess_xy * jac_yx)
    new_rate_xy = rate_xy - (hess_xx * jac_xy + hess_xy * jac_yy)
    new_rate_yx = rate_yx - (hess_xy * jac_xx + hess_yy * jac_yx)
    new_rate_yy = rate_yy - (hess_xy * jac_xy + hess_yy * jac_yy)
    new_jac_xx = jac_xx + new_rate_xx
    new_jac_xy = jac_xy + new_rate_xy
    new_jac_yx = jac_yx + new_rate_yx
    new_jac_yy = jac_yy + new_rate_yy
    return jnp.stack(
        [
            new_disp_x,
            new_disp_y,
            new_tilt_x,
            new_tilt_y,
            new_jac_xx,
            new_jac_xy,
            new_jac_yx,
            new_jac_yy,
            new_rate_xx,
            new_rate_xy,
            new_rate_yx,
            new_rate_yy,
        ],
        axis=-3,
    )


def phase_table(left_idx, right_idx, modulus, orient):
    product = left_idx[:, None] * right_idx[None, :] % modulus
    angle = orient * two_pi / modulus * product.astype(jnp.float32)
    return (jnp.cos(angle), jnp.sin(angle))


def block_table(left_idx, right_idx, modulus, orient):
    t_re, t_im = phase_table(left_idx, right_idx, modulus, orient)
    top = jnp.concatenate([t_re, t_im], axis=1)
    bottom = jnp.concatenate([-t_im, t_re], axis=1)
    return jnp.concatenate([top, bottom], axis=0)


def mixed(form, left_op, right_op):
    return jnp.einsum(
        form, left_op, right_op, precision=highest, preferred_element_type=jnp.float32
    )


def complex_product(form, real_in, imag_in, table_re, table_im):
    if imag_in is None:
        return (mixed(form, real_in, table_re), mixed(form, real_in, table_im))
    out_re = mixed(form, real_in, table_re) - mixed(form, imag_in, table_im)
    out_im = mixed(form, real_in, table_im) + mixed(form, imag_in, table_re)
    return (out_re, out_im)


def first_factor_of(length):
    factor_one = 1
    while factor_one * factor_one < length and length % (factor_one * 2) == 0:
        factor_one = factor_one * 2
    return factor_one


def rows_forward(cells):
    row_count, length = cells.shape
    second = length // first_radix
    half = second // 2
    shaped = cells.reshape(row_count, first_radix, second)
    v_idx = jnp.arange(first_radix, dtype=jnp.int32)
    u_idx = jnp.arange(second, dtype=jnp.int32)
    m_idx = jnp.arange(half, dtype=jnp.int32)
    section_re, section_im = phase_table(v_idx, v_idx, first_radix, -1.0)
    section = jnp.concatenate([section_re, section_im], axis=1)
    part = mixed("rvu,vk->rku", shaped, section)
    part_re = part[:, :first_radix]
    part_im = part[:, first_radix:]
    twist_re, twist_im = phase_table(v_idx, u_idx, length, -1.0)
    turned_re = part_re * twist_re - part_im * twist_im
    turned_im = part_re * twist_im + part_im * twist_re
    turned = jnp.concatenate([turned_re, turned_im], axis=2)
    final = block_table(u_idx, m_idx, second, -1.0)
    return mixed("rkj,jn->rkn", turned, final)


def columns_forward(spread_re, spread_im):
    length, col_count = spread_re.shape
    factor_one = first_factor_of(length)
    second = length // factor_one
    first_idx = jnp.arange(factor_one, dtype=jnp.int32)
    second_idx = jnp.arange(second, dtype=jnp.int32)
    stacked = jnp.concatenate(
        [
            spread_re.reshape(factor_one, second * col_count),
            spread_im.reshape(factor_one, second * col_count),
        ],
        axis=0,
    )
    section = block_table(first_idx, first_idx, factor_one, -1.0)
    part = mixed("jn,jc->nc", section, stacked).reshape(2, factor_one, second, col_count)
    twist_re, twist_im = phase_table(first_idx, second_idx, length, -1.0)
    twist_re = twist_re[:, :, None]
    twist_im = twist_im[:, :, None]
    turned_re = part[0] * twist_re - part[1] * twist_im
    turned_im = part[0] * twist_im + part[1] * twist_re
    turned = jnp.stack([turned_re, turned_im], axis=1).reshape(
        factor_one, 2 * second, col_count
    )
    final = block_table(second_idx, second_idx, second, -1.0)
    done = mixed("jn,kjc->nkc", final, turned)
    return done.reshape(2, length, col_count)


def rows_inverse(spec_re, spec_im, length, m_count):
    row_count = spec_re.shape[0]
    second = length // first_radix
    shaped_re = spec_re.reshape(row_count, first_radix, m_count)
    shaped_im = spec_im.reshape(row_count, first_radix, m_count)
    k_idx = jnp.arange(first_radix, dtype=jnp.int32)
    u_idx = jnp.arange(second, dtype=jnp.int32)
    m_idx = jnp.arange(m_count, dtype=jnp.int32)
    section_re, section_im = phase_table(m_idx, u_idx, second, 1.0)
    part_re, part_im = complex_product("rkm,mu->rku", shaped_re, shaped_im, section_re, section_im)
    twist_re, twist_im = phase_table(k_idx, u_idx, length, 1.0)
    turned_re = part_re * twist_re - part_im * twist_im
    turned_im = part_re * twist_im + part_im * twist_re
    final_re, final_im = phase_table(k_idx, k_idx, first_radix, 1.0)
    done_re, done_im = complex_product("rku,kv->rvu", turned_re, turned_im, final_re, final_im)
    return (done_re.reshape(row_count, length), done_im.reshape(row_count, length))


def wavenumbers(indices, length):
    signed = jnp.where(indices < length // 2, indices, indices - length)
    return (two_pi / length * signed.astype(jnp.float32), indices != length // 2)


def folded_spectra(spectrum, col_idx, ray_all):
    _, length, col_count = spectrum.shape
    norm_factor = float(length * length)
    wave_col, retain_col = wavenumbers(col_idx, length)
    weight = jnp.where(col_idx == 0, 1.0, 2.0).astype(jnp.float32)
    row_idx = jnp.arange(length, dtype=jnp.int32)
    wave_row, retain_row = wavenumbers(row_idx, length)
    wave_row = wave_row[:, None]
    squared = wave_col[None, :] * wave_col[None, :] + wave_row * wave_row
    retain = retain_row[:, None] & retain_col[None, :] & (squared > 0.0)
    safe_sq = jnp.where(retain, squared, 1.0)
    kernel = jnp.where(retain, -2.0 / (safe_sq * norm_factor), 0.0) * weight[None, :]
    phi = kernel[None] * spectrum
    terms = jnp.stack([phi, wave_row[None] * phi, (wave_row * wave_row)[None] * phi])
    terms = terms.reshape(3, 2, length // ray_all, ray_all, col_count)
    return jnp.sum(terms, axis=2)


def per_device(density, lens_weight, plane_count, ray_state):
    sky_count = lax.axis_size("sky")
    sky_index = lax.axis_index("sky")
    ray_tile = shifted(ray_state, "los", HOPS)
    plane_cells = density[0]
    length = plane_cells.shape[1]
    second = length // first_radix
    half = second // 2
    ray_dev = ray_state.shape[2]
    ray_all = ray_dev * sky_count
    strength = lens_weight[0] * plane_count[0].astype(jnp.float32)
    rows = rows_forward(plane_cells)
    spread = lax.all_to_all(rows, "sky", split_axis=1, concat_axis=0, tiled=True)
    k_local = spread.shape[1]
    spread_re = spread[:, :, :half].reshape(length, k_local * half)
    spread_im = spread[:, :, half:].reshape(length, k_local * half)
    spectrum = columns_forward(spread_re, spread_im)
    ray_tile, spectrum = lax.optimization_barrier((ray_tile, spectrum))
    position = jnp.arange(k_local * half, dtype=jnp.int32)
    col_idx = sky_index * k_local + position // half + first_radix * (position % half)
    folds = folded_spectra(spectrum, col_idx, ray_all)
    q_idx = jnp.arange(ray_all, dtype=jnp.int32)
    back = block_table(q_idx, q_idx, ray_all, 1.0)
    at_rows = mixed("pjc,jn->pnc", folds.reshape(3, 2 * ray_all, k_local * half), back)
    at_rows = at_rows.reshape(3, 2, ray_all, k_local, half)
    returned = lax.all_to_all(at_rows, "sky", split_axis=2, concat_axis=3, tiled=True)
    returned = returned * strength
    arrived = jnp.stack(
        [shifted(returned, "los", HOPS - step_index) for step_index in range(HOPS)]
    )
    k_all = returned.shape[3]
    kx_idx = jnp.arange(k_all, dtype=jnp.int32)[:, None] + first_radix * jnp.arange(
        half, dtype=jnp.int32
    )[None, :]
    wave_col = wavenumbers(kx_idx, length)[0]
    f0_re, f0_im = arrived[:, 0, 0], arrived[:, 0, 1]
    f1_re, f1_im = arrived[:, 1, 0], arrived[:, 1, 1]
    f2_re, f2_im = arrived[:, 2, 0], arrived[:, 2, 1]
    col_sq = wave_col * wave_col
    all_re = jnp.stack(
        [-wave_col * f0_im, -f1_im, -col_sq * f0_re, -f2_re, -wave_col * f1_re], axis=1
    )
    all_im = jnp.stack(
        [wave_col * f0_re, f1_re, -col_sq * f0_im, -f2_im, -wave_col * f1_im], axis=1
    )
    flat_re = all_re.reshape(HOPS * 5 * ray_dev, k_all * half)
    flat_im = all_im.reshape(HOPS * 5 * ray_dev, k_all * half)
    field_re, _ = rows_inverse(flat_re, flat_im, length, half)
    fields = field_re.reshape(HOPS, 5, ray_dev, length)
    for step_index in range(HOPS):
        ray_tile = lens_step(ray_tile, fields[step_index][None])
    return ray_tile


def solution(mesh):
    return jax.shard_map(
        per_device,
        mesh=mesh,
        in_specs=(
            P(("real", "los"), "sky", None),
            P(("real", "los")),
            P(("real", "los")),
            P(("real", "los"), None, "sky", None),
        ),
        out_specs=P(("real", "los"), None, "sky", None),
        check_vma=False,
    )
```

```python
import math

import jax
import jax.numpy as jnp
from jax import lax
from jax.sharding import PartitionSpec as P

HOPS = 4


two_pi = 2.0 * math.pi
highest = lax.Precision.HIGH
first_radix = 16


def shifted(block, axis, distance):
    devices = range(lax.axis_size(axis))
    route = [((i - distance) % len(devices), i) for i in devices]
    return lax.ppermute(block, axis, route)


def lens_step(ray_tile, fields):
    disp_x = ray_tile[..., 0, :, :]
    disp_y = ray_tile[..., 1, :, :]
    tilt_x = ray_tile[..., 2, :, :]
    tilt_y = ray_tile[..., 3, :, :]
    jac_xx = ray_tile[..., 4, :, :]
    jac_xy = ray_tile[..., 5, :, :]
    jac_yx = ray_tile[..., 6, :, :]
    jac_yy = ray_tile[..., 7, :, :]
    rate_xx = ray_tile[..., 8, :, :]
    rate_xy = ray_tile[..., 9, :, :]
    rate_yx = ray_tile[..., 10, :, :]
    rate_yy = ray_tile[..., 11, :, :]
    bend_x = fields[..., 0, :, :]
    bend_y = fields[..., 1, :, :]
    hess_xx = fields[..., 2, :, :]
    hess_yy = fields[..., 3, :, :]
    hess_xy = fields[..., 4, :, :]
    push_x = bend_x + hess_xx * disp_x + hess_xy * disp_y
    push_y = bend_y + hess_xy * disp_x + hess_yy * disp_y
    new_tilt_x = tilt_x - push_x
    new_tilt_y = tilt_y - push_y
    new_disp_x = disp_x + new_tilt_x
    new_disp_y = disp_y + new_tilt_y
    new_rate_xx = rate_xx - (hess_xx * jac_xx + hess_xy * jac_yx)
    new_rate_xy = rate_xy - (hess_xx * jac_xy + hess_xy * jac_yy)
    new_rate_yx = rate_yx - (hess_xy * jac_xx + hess_yy * jac_yx)
    new_rate_yy = rate_yy - (hess_xy * jac_xy + hess_yy * jac_yy)
    new_jac_xx = jac_xx + new_rate_xx
    new_jac_xy = jac_xy + new_rate_xy
    new_jac_yx = jac_yx + new_rate_yx
    new_jac_yy = jac_yy + new_rate_yy
    return jnp.stack(
        [
            new_disp_x,
            new_disp_y,
            new_tilt_x,
            new_tilt_y,
            new_jac_xx,
            new_jac_xy,
            new_jac_yx,
            new_jac_yy,
            new_rate_xx,
            new_rate_xy,
            new_rate_yx,
            new_rate_yy,
        ],
        axis=-3,
    )


def phase_table(left_idx, right_idx, modulus, orient):
    product = left_idx[:, None] * right_idx[None, :] % modulus
    angle = orient * two_pi / modulus * product.astype(jnp.float32)
    return (jnp.cos(angle), jnp.sin(angle))


def block_table(left_idx, right_idx, modulus, orient):
    t_re, t_im = phase_table(left_idx, right_idx, modulus, orient)
    top = jnp.concatenate([t_re, t_im], axis=1)
    bottom = jnp.concatenate([-t_im, t_re], axis=1)
    return jnp.concatenate([top, bottom], axis=0)


def mixed(form, left_op, right_op):
    return jnp.einsum(
        form, left_op, right_op, precision=highest, preferred_element_type=jnp.float32
    )


def complex_product(form, real_in, imag_in, table_re, table_im):
    if imag_in is None:
        return (mixed(form, real_in, table_re), mixed(form, real_in, table_im))
    out_re = mixed(form, real_in, table_re) - mixed(form, imag_in, table_im)
    out_im = mixed(form, real_in, table_im) + mixed(form, imag_in, table_re)
    return (out_re, out_im)


def first_factor_of(length):
    factor_one = 1
    while factor_one * factor_one < length and length % (factor_one * 2) == 0:
        factor_one = factor_one * 2
    return factor_one


def rows_forward(cells):
    row_count, length = cells.shape
    second = length // first_radix
    half = second // 2
    shaped = cells.reshape(row_count, first_radix, second)
    v_idx = jnp.arange(first_radix, dtype=jnp.int32)
    u_idx = jnp.arange(second, dtype=jnp.int32)
    m_idx = jnp.arange(half, dtype=jnp.int32)
    section_re, section_im = phase_table(v_idx, v_idx, first_radix, -1.0)
    section = jnp.concatenate([section_re, section_im], axis=1)
    part = mixed("rvu,vk->rku", shaped, section)
    part_re = part[:, :first_radix]
    part_im = part[:, first_radix:]
    twist_re, twist_im = phase_table(v_idx, u_idx, length, -1.0)
    turned_re = part_re * twist_re - part_im * twist_im
    turned_im = part_re * twist_im + part_im * twist_re
    turned = jnp.concatenate([turned_re, turned_im], axis=2)
    final = block_table(u_idx, m_idx, second, -1.0)
    return mixed("rkj,jn->rkn", turned, final)


def columns_forward(spread_re, spread_im):
    length, col_count = spread_re.shape
    factor_one = first_factor_of(length)
    second = length // factor_one
    first_idx = jnp.arange(factor_one, dtype=jnp.int32)
    second_idx = jnp.arange(second, dtype=jnp.int32)
    stacked = jnp.concatenate(
        [
            spread_re.reshape(factor_one, second * col_count),
            spread_im.reshape(factor_one, second * col_count),
        ],
        axis=0,
    )
    section = block_table(first_idx, first_idx, factor_one, -1.0)
    part = mixed("jn,jc->nc", section, stacked).reshape(2, factor_one, second, col_count)
    twist_re, twist_im = phase_table(first_idx, second_idx, length, -1.0)
    twist_re = twist_re[:, :, None]
    twist_im = twist_im[:, :, None]
    turned_re = part[0] * twist_re - part[1] * twist_im
    turned_im = part[0] * twist_im + part[1] * twist_re
    turned = jnp.stack([turned_re, turned_im], axis=1).reshape(
        factor_one, 2 * second, col_count
    )
    final = block_table(second_idx, second_idx, second, -1.0)
    done = mixed("jn,kjc->nkc", final, turned)
    return done.reshape(2, length, col_count)


def rows_inverse(spec_re, spec_im, length, m_count):
    row_count = spec_re.shape[0]
    second = length // first_radix
    shaped_re = spec_re.reshape(row_count, first_radix, m_count)
    shaped_im = spec_im.reshape(row_count, first_radix, m_count)
    k_idx = jnp.arange(first_radix, dtype=jnp.int32)
    u_idx = jnp.arange(second, dtype=jnp.int32)
    m_idx = jnp.arange(m_count, dtype=jnp.int32)
    section_re, section_im = phase_table(m_idx, u_idx, second, 1.0)
    part_re, part_im = complex_product("rkm,mu->rku", shaped_re, shaped_im, section_re, section_im)
    twist_re, twist_im = phase_table(k_idx, u_idx, length, 1.0)
    turned_re = part_re * twist_re - part_im * twist_im
    turned_im = part_re * twist_im + part_im * twist_re
    final_re, final_im = phase_table(k_idx, k_idx, first_radix, 1.0)
    done_re, done_im = complex_product("rku,kv->rvu", turned_re, turned_im, final_re, final_im)
    return (done_re.reshape(row_count, length), done_im.reshape(row_count, length))


def wavenumbers(indices, length):
    signed = jnp.where(indices < length // 2, indices, indices - length)
    return (two_pi / length * signed.astype(jnp.float32), indices != length // 2)


def folded_spectra(spectrum, col_idx, ray_all):
    _, length, col_count = spectrum.shape
    norm_factor = float(length * length)
    wave_col, retain_col = wavenumbers(col_idx, length)
    weight = jnp.where(col_idx == 0, 1.0, 2.0).astype(jnp.float32)
    row_idx = jnp.arange(length, dtype=jnp.int32)
    wave_row, retain_row = wavenumbers(row_idx, length)
    wave_row = wave_row[:, None]
    squared = wave_col[None, :] * wave_col[None, :] + wave_row * wave_row
    retain = retain_row[:, None] & retain_col[None, :] & (squared > 0.0)
    safe_sq = jnp.where(retain, squared, 1.0)
    kernel = jnp.where(retain, -2.0 / (safe_sq * norm_factor), 0.0) * weight[None, :]
    phi = kernel[None] * spectrum
    terms = jnp.stack([phi, wave_row[None] * phi, (wave_row * wave_row)[None] * phi])
    terms = terms.reshape(3, 2, length // ray_all, ray_all, col_count)
    return jnp.sum(terms, axis=2)


def per_device(density, lens_weight, plane_count, ray_state):
    sky_count = lax.axis_size("sky")
    sky_index = lax.axis_index("sky")
    ray_tile = shifted(ray_state, "los", HOPS)
    plane_cells = density[0]
    length = plane_cells.shape[1]
    second = length // first_radix
    half = second // 2
    ray_dev = ray_state.shape[2]
    ray_all = ray_dev * sky_count
    strength = lens_weight[0] * plane_count[0].astype(jnp.float32)
    rows = rows_forward(plane_cells)
    spread = lax.all_to_all(rows, "sky", split_axis=1, concat_axis=0, tiled=True)
    k_local = spread.shape[1]
    spread_re = spread[:, :, :half].reshape(length, k_local * half)
    spread_im = spread[:, :, half:].reshape(length, k_local * half)
    spectrum = columns_forward(spread_re, spread_im)
    ray_tile, spectrum = lax.optimization_barrier((ray_tile, spectrum))
    position = jnp.arange(k_local * half, dtype=jnp.int32)
    col_idx = sky_index * k_local + position // half + first_radix * (position % half)
    folds = folded_spectra(spectrum, col_idx, ray_all)
    q_idx = jnp.arange(ray_all, dtype=jnp.int32)
    back = block_table(q_idx, q_idx, ray_all, 1.0)
    at_rows = mixed("pjc,jn->pnc", folds.reshape(3, 2 * ray_all, k_local * half), back)
    at_rows = at_rows.reshape(3, 2, ray_all, k_local, half)
    returned = lax.all_to_all(at_rows, "sky", split_axis=2, concat_axis=3, tiled=True)
    returned = returned * strength
    arrived = jnp.stack(
        [shifted(returned, "los", HOPS - step_index) for step_index in range(HOPS)]
    )
    k_all = returned.shape[3]
    kx_idx = jnp.arange(k_all, dtype=jnp.int32)[:, None] + first_radix * jnp.arange(
        half, dtype=jnp.int32
    )[None, :]
    wave_col = wavenumbers(kx_idx, length)[0]
    f0_re, f0_im = arrived[:, 0, 0], arrived[:, 0, 1]
    f1_re, f1_im = arrived[:, 1, 0], arrived[:, 1, 1]
    f2_re, f2_im = arrived[:, 2, 0], arrived[:, 2, 1]
    col_sq = wave_col * wave_col
    all_re = jnp.stack(
        [-wave_col * f0_im, -f1_im, -col_sq * f0_re, -f2_re, -wave_col * f1_re], axis=1
    )
    all_im = jnp.stack(
        [wave_col * f0_re, f1_re, -col_sq * f0_im, -f2_im, -wave_col * f1_im], axis=1
    )
    flat_re = all_re.reshape(HOPS * 5 * ray_dev, k_all * half)
    flat_im = all_im.reshape(HOPS * 5 * ray_dev, k_all * half)
    field_re, _ = rows_inverse(flat_re, flat_im, length, half)
    fields = field_re.reshape(HOPS, 5, ray_dev, length)
    for step_index in range(HOPS):
        ray_tile = lens_step(ray_tile, fields[step_index][None])
    return ray_tile


def solution(mesh):
    return jax.shard_map(
        per_device,
        mesh=mesh,
        in_specs=(
            P(("real", "los"), "sky", None),
            P(("real", "los")),
            P(("real", "los")),
            P(("real", "los"), None, "sky", None),
        ),
        out_specs=P(("real", "los"), None, "sky", None),
        check_vma=False,
    )
```

```python
import math

import jax
import jax.numpy as jnp
from jax import lax
from jax.sharding import PartitionSpec as P

HOPS = 4


two_pi = 2.0 * math.pi
highest = lax.Precision.HIGH
first_radix = 16


def shifted(block, axis, distance):
    devices = range(lax.axis_size(axis))
    route = [((i - distance) % len(devices), i) for i in devices]
    return lax.ppermute(block, axis, route)


def lens_step(ray_tile, fields):
    disp_x = ray_tile[..., 0, :, :]
    disp_y = ray_tile[..., 1, :, :]
    tilt_x = ray_tile[..., 2, :, :]
    tilt_y = ray_tile[..., 3, :, :]
    jac_xx = ray_tile[..., 4, :, :]
    jac_xy = ray_tile[..., 5, :, :]
    jac_yx = ray_tile[..., 6, :, :]
    jac_yy = ray_tile[..., 7, :, :]
    rate_xx = ray_tile[..., 8, :, :]
    rate_xy = ray_tile[..., 9, :, :]
    rate_yx = ray_tile[..., 10, :, :]
    rate_yy = ray_tile[..., 11, :, :]
    bend_x = fields[..., 0, :, :]
    bend_y = fields[..., 1, :, :]
    hess_xx = fields[..., 2, :, :]
    hess_yy = fields[..., 3, :, :]
    hess_xy = fields[..., 4, :, :]
    push_x = bend_x + hess_xx * disp_x + hess_xy * disp_y
    push_y = bend_y + hess_xy * disp_x + hess_yy * disp_y
    new_tilt_x = tilt_x - push_x
    new_tilt_y = tilt_y - push_y
    new_disp_x = disp_x + new_tilt_x
    new_disp_y = disp_y + new_tilt_y
    new_rate_xx = rate_xx - (hess_xx * jac_xx + hess_xy * jac_yx)
    new_rate_xy = rate_xy - (hess_xx * jac_xy + hess_xy * jac_yy)
    new_rate_yx = rate_yx - (hess_xy * jac_xx + hess_yy * jac_yx)
    new_rate_yy = rate_yy - (hess_xy * jac_xy + hess_yy * jac_yy)
    new_jac_xx = jac_xx + new_rate_xx
    new_jac_xy = jac_xy + new_rate_xy
    new_jac_yx = jac_yx + new_rate_yx
    new_jac_yy = jac_yy + new_rate_yy
    return jnp.stack(
        [
            new_disp_x,
            new_disp_y,
            new_tilt_x,
            new_tilt_y,
            new_jac_xx,
            new_jac_xy,
            new_jac_yx,
            new_jac_yy,
            new_rate_xx,
            new_rate_xy,
            new_rate_yx,
            new_rate_yy,
        ],
        axis=-3,
    )


def phase_table(left_idx, right_idx, modulus, orient):
    product = left_idx[:, None] * right_idx[None, :] % modulus
    angle = orient * two_pi / modulus * product.astype(jnp.float32)
    return (jnp.cos(angle), jnp.sin(angle))


def block_table(left_idx, right_idx, modulus, orient):
    t_re, t_im = phase_table(left_idx, right_idx, modulus, orient)
    top = jnp.concatenate([t_re, t_im], axis=1)
    bottom = jnp.concatenate([-t_im, t_re], axis=1)
    return jnp.concatenate([top, bottom], axis=0)


def mixed(form, left_op, right_op):
    return jnp.einsum(
        form, left_op, right_op, precision=highest, preferred_element_type=jnp.float32
    )


def complex_product(form, real_in, imag_in, table_re, table_im):
    if imag_in is None:
        return (mixed(form, real_in, table_re), mixed(form, real_in, table_im))
    out_re = mixed(form, real_in, table_re) - mixed(form, imag_in, table_im)
    out_im = mixed(form, real_in, table_im) + mixed(form, imag_in, table_re)
    return (out_re, out_im)


def first_factor_of(length):
    factor_one = 1
    while factor_one * factor_one < length and length % (factor_one * 2) == 0:
        factor_one = factor_one * 2
    return factor_one


def rows_forward(cells):
    row_count, length = cells.shape
    second = length // first_radix
    half = second // 2
    shaped = cells.reshape(row_count, first_radix, second)
    v_idx = jnp.arange(first_radix, dtype=jnp.int32)
    u_idx = jnp.arange(second, dtype=jnp.int32)
    m_idx = jnp.arange(half, dtype=jnp.int32)
    section_re, section_im = phase_table(v_idx, v_idx, first_radix, -1.0)
    section = jnp.concatenate([section_re, section_im], axis=1)
    part = mixed("rvu,vk->rku", shaped, section)
    part_re = part[:, :first_radix]
    part_im = part[:, first_radix:]
    twist_re, twist_im = phase_table(v_idx, u_idx, length, -1.0)
    turned_re = part_re * twist_re - part_im * twist_im
    turned_im = part_re * twist_im + part_im * twist_re
    turned = jnp.concatenate([turned_re, turned_im], axis=2)
    final = block_table(u_idx, m_idx, second, -1.0)
    return mixed("rkj,jn->rkn", turned, final)


def columns_forward(spread_re, spread_im):
    length, col_count = spread_re.shape
    factor_one = first_factor_of(length)
    second = length // factor_one
    first_idx = jnp.arange(factor_one, dtype=jnp.int32)
    second_idx = jnp.arange(second, dtype=jnp.int32)
    stacked = jnp.concatenate(
        [
            spread_re.reshape(factor_one, second * col_count),
            spread_im.reshape(factor_one, second * col_count),
        ],
        axis=0,
    )
    section = block_table(first_idx, first_idx, factor_one, -1.0)
    part = mixed("jn,jc->nc", section, stacked).reshape(2, factor_one, second, col_count)
    twist_re, twist_im = phase_table(first_idx, second_idx, length, -1.0)
    twist_re = twist_re[:, :, None]
    twist_im = twist_im[:, :, None]
    turned_re = part[0] * twist_re - part[1] * twist_im
    turned_im = part[0] * twist_im + part[1] * twist_re
    turned = jnp.stack([turned_re, turned_im], axis=1).reshape(
        factor_one, 2 * second, col_count
    )
    final = block_table(second_idx, second_idx, second, -1.0)
    done = mixed("jn,kjc->nkc", final, turned)
    return done.reshape(2, length, col_count)


def rows_inverse(spec_re, spec_im, length, m_count):
    row_count = spec_re.shape[0]
    second = length // first_radix
    shaped_re = spec_re.reshape(row_count, first_radix, m_count)
    shaped_im = spec_im.reshape(row_count, first_radix, m_count)
    k_idx = jnp.arange(first_radix, dtype=jnp.int32)
    u_idx = jnp.arange(second, dtype=jnp.int32)
    m_idx = jnp.arange(m_count, dtype=jnp.int32)
    section_re, section_im = phase_table(m_idx, u_idx, second, 1.0)
    part_re, part_im = complex_product("rkm,mu->rku", shaped_re, shaped_im, section_re, section_im)
    twist_re, twist_im = phase_table(k_idx, u_idx, length, 1.0)
    turned_re = part_re * twist_re - part_im * twist_im
    turned_im = part_re * twist_im + part_im * twist_re
    final_re, final_im = phase_table(k_idx, k_idx, first_radix, 1.0)
    done_re, done_im = complex_product("rku,kv->rvu", turned_re, turned_im, final_re, final_im)
    return (done_re.reshape(row_count, length), done_im.reshape(row_count, length))


def wavenumbers(indices, length):
    signed = jnp.where(indices < length // 2, indices, indices - length)
    return (two_pi / length * signed.astype(jnp.float32), indices != length // 2)


def folded_spectra(spectrum, col_idx, ray_all):
    _, length, col_count = spectrum.shape
    norm_factor = float(length * length)
    wave_col, retain_col = wavenumbers(col_idx, length)
    weight = jnp.where(col_idx == 0, 1.0, 2.0).astype(jnp.float32)
    row_idx = jnp.arange(length, dtype=jnp.int32)
    wave_row, retain_row = wavenumbers(row_idx, length)
    wave_row = wave_row[:, None]
    squared = wave_col[None, :] * wave_col[None, :] + wave_row * wave_row
    retain = retain_row[:, None] & retain_col[None, :] & (squared > 0.0)
    safe_sq = jnp.where(retain, squared, 1.0)
    kernel = jnp.where(retain, -2.0 / (safe_sq * norm_factor), 0.0) * weight[None, :]
    phi = kernel[None] * spectrum
    terms = jnp.stack([phi, wave_row[None] * phi, (wave_row * wave_row)[None] * phi])
    terms = terms.reshape(3, 2, length // ray_all, ray_all, col_count)
    return jnp.sum(terms, axis=2)


def per_device(density, lens_weight, plane_count, ray_state):
    sky_count = lax.axis_size("sky")
    sky_index = lax.axis_index("sky")
    ray_tile = shifted(ray_state, "los", HOPS)
    plane_cells = density[0]
    length = plane_cells.shape[1]
    second = length // first_radix
    half = second // 2
    ray_dev = ray_state.shape[2]
    ray_all = ray_dev * sky_count
    strength = lens_weight[0] * plane_count[0].astype(jnp.float32)
    rows = rows_forward(plane_cells)
    spread = lax.all_to_all(rows, "sky", split_axis=1, concat_axis=0, tiled=True)
    k_local = spread.shape[1]
    spread_re = spread[:, :, :half].reshape(length, k_local * half)
    spread_im = spread[:, :, half:].reshape(length, k_local * half)
    spectrum = columns_forward(spread_re, spread_im)
    ray_tile, spectrum = lax.optimization_barrier((ray_tile, spectrum))
    position = jnp.arange(k_local * half, dtype=jnp.int32)
    col_idx = sky_index * k_local + position // half + first_radix * (position % half)
    folds = folded_spectra(spectrum, col_idx, ray_all)
    q_idx = jnp.arange(ray_all, dtype=jnp.int32)
    back = block_table(q_idx, q_idx, ray_all, 1.0)
    at_rows = mixed("pjc,jn->pnc", folds.reshape(3, 2 * ray_all, k_local * half), back)
    at_rows = at_rows.reshape(3, 2, ray_all, k_local, half)
    returned = lax.all_to_all(at_rows, "sky", split_axis=2, concat_axis=3, tiled=True)
    k_all = returned.shape[3]
    dense = returned.reshape(3 * 2 * ray_dev, k_all * half) * strength
    arrived = jnp.stack(
        [shifted(dense, "los", HOPS - step_index) for step_index in range(HOPS)]
    ).reshape(HOPS, 3, 2, ray_dev, k_all, half)
    kx_idx = jnp.arange(k_all, dtype=jnp.int32)[:, None] + first_radix * jnp.arange(
        half, dtype=jnp.int32
    )[None, :]
    wave_col = wavenumbers(kx_idx, length)[0]
    f0_re, f0_im = arrived[:, 0, 0], arrived[:, 0, 1]
    f1_re, f1_im = arrived[:, 1, 0], arrived[:, 1, 1]
    f2_re, f2_im = arrived[:, 2, 0], arrived[:, 2, 1]
    col_sq = wave_col * wave_col
    all_re = jnp.stack(
        [-wave_col * f0_im, -f1_im, -col_sq * f0_re, -f2_re, -wave_col * f1_re], axis=1
    )
    all_im = jnp.stack(
        [wave_col * f0_re, f1_re, -col_sq * f0_im, -f2_im, -wave_col * f1_im], axis=1
    )
    flat_re = all_re.reshape(HOPS * 5 * ray_dev, k_all * half)
    flat_im = all_im.reshape(HOPS * 5 * ray_dev, k_all * half)
    field_re, _ = rows_inverse(flat_re, flat_im, length, half)
    fields = field_re.reshape(HOPS, 5, ray_dev, length)
    for step_index in range(HOPS):
        ray_tile = lens_step(ray_tile, fields[step_index][None])
    return ray_tile


def solution(mesh):
    return jax.shard_map(
        per_device,
        mesh=mesh,
        in_specs=(
            P(("real", "los"), "sky", None),
            P(("real", "los")),
            P(("real", "los")),
            P(("real", "los"), None, "sky", None),
        ),
        out_specs=P(("real", "los"), None, "sky", None),
        check_vma=False,
    )
```

```python
import math

import jax
import jax.numpy as jnp
from jax import lax
from jax.sharding import PartitionSpec as P

HOPS = 4


two_pi = 2.0 * math.pi
highest = lax.Precision.HIGH
first_radix = 16


def shifted(block, axis, distance):
    devices = range(lax.axis_size(axis))
    route = [((i - distance) % len(devices), i) for i in devices]
    return lax.ppermute(block, axis, route)


def lens_step(ray_tile, fields):
    disp_x = ray_tile[..., 0, :, :]
    disp_y = ray_tile[..., 1, :, :]
    tilt_x = ray_tile[..., 2, :, :]
    tilt_y = ray_tile[..., 3, :, :]
    jac_xx = ray_tile[..., 4, :, :]
    jac_xy = ray_tile[..., 5, :, :]
    jac_yx = ray_tile[..., 6, :, :]
    jac_yy = ray_tile[..., 7, :, :]
    rate_xx = ray_tile[..., 8, :, :]
    rate_xy = ray_tile[..., 9, :, :]
    rate_yx = ray_tile[..., 10, :, :]
    rate_yy = ray_tile[..., 11, :, :]
    bend_x = fields[..., 0, :, :]
    bend_y = fields[..., 1, :, :]
    hess_xx = fields[..., 2, :, :]
    hess_yy = fields[..., 3, :, :]
    hess_xy = fields[..., 4, :, :]
    push_x = bend_x + hess_xx * disp_x + hess_xy * disp_y
    push_y = bend_y + hess_xy * disp_x + hess_yy * disp_y
    new_tilt_x = tilt_x - push_x
    new_tilt_y = tilt_y - push_y
    new_disp_x = disp_x + new_tilt_x
    new_disp_y = disp_y + new_tilt_y
    new_rate_xx = rate_xx - (hess_xx * jac_xx + hess_xy * jac_yx)
    new_rate_xy = rate_xy - (hess_xx * jac_xy + hess_xy * jac_yy)
    new_rate_yx = rate_yx - (hess_xy * jac_xx + hess_yy * jac_yx)
    new_rate_yy = rate_yy - (hess_xy * jac_xy + hess_yy * jac_yy)
    new_jac_xx = jac_xx + new_rate_xx
    new_jac_xy = jac_xy + new_rate_xy
    new_jac_yx = jac_yx + new_rate_yx
    new_jac_yy = jac_yy + new_rate_yy
    return jnp.stack(
        [
            new_disp_x,
            new_disp_y,
            new_tilt_x,
            new_tilt_y,
            new_jac_xx,
            new_jac_xy,
            new_jac_yx,
            new_jac_yy,
            new_rate_xx,
            new_rate_xy,
            new_rate_yx,
            new_rate_yy,
        ],
        axis=-3,
    )


def phase_table(left_idx, right_idx, modulus, orient):
    product = left_idx[:, None] * right_idx[None, :] % modulus
    angle = orient * two_pi / modulus * product.astype(jnp.float32)
    return (jnp.cos(angle), jnp.sin(angle))


def block_table(left_idx, right_idx, modulus, orient):
    t_re, t_im = phase_table(left_idx, right_idx, modulus, orient)
    top = jnp.concatenate([t_re, t_im], axis=1)
    bottom = jnp.concatenate([-t_im, t_re], axis=1)
    return jnp.concatenate([top, bottom], axis=0)


def mixed(form, left_op, right_op):
    return jnp.einsum(
        form, left_op, right_op, precision=highest, preferred_element_type=jnp.float32
    )


def complex_product(form, real_in, imag_in, table_re, table_im):
    if imag_in is None:
        return (mixed(form, real_in, table_re), mixed(form, real_in, table_im))
    out_re = mixed(form, real_in, table_re) - mixed(form, imag_in, table_im)
    out_im = mixed(form, real_in, table_im) + mixed(form, imag_in, table_re)
    return (out_re, out_im)


def first_factor_of(length):
    factor_one = 1
    while factor_one * factor_one < length and length % (factor_one * 2) == 0:
        factor_one = factor_one * 2
    return factor_one


def rows_forward(cells):
    row_count, length = cells.shape
    second = length // first_radix
    half = second // 2
    shaped = cells.reshape(row_count, first_radix, second)
    v_idx = jnp.arange(first_radix, dtype=jnp.int32)
    u_idx = jnp.arange(second, dtype=jnp.int32)
    m_idx = jnp.arange(half, dtype=jnp.int32)
    section_re, section_im = phase_table(v_idx, v_idx, first_radix, -1.0)
    section = jnp.concatenate([section_re, section_im], axis=1)
    part = mixed("rvu,vk->rku", shaped, section)
    part_re = part[:, :first_radix]
    part_im = part[:, first_radix:]
    twist_re, twist_im = phase_table(v_idx, u_idx, length, -1.0)
    turned_re = part_re * twist_re - part_im * twist_im
    turned_im = part_re * twist_im + part_im * twist_re
    turned = jnp.concatenate([turned_re, turned_im], axis=2)
    final = block_table(u_idx, m_idx, second, -1.0)
    return mixed("rkj,jn->rkn", turned, final)


def columns_forward(spread_re, spread_im):
    length, col_count = spread_re.shape
    factor_one = first_factor_of(length)
    second = length // factor_one
    first_idx = jnp.arange(factor_one, dtype=jnp.int32)
    second_idx = jnp.arange(second, dtype=jnp.int32)
    stacked = jnp.concatenate(
        [
            spread_re.reshape(factor_one, second * col_count),
            spread_im.reshape(factor_one, second * col_count),
        ],
        axis=0,
    )
    section = block_table(first_idx, first_idx, factor_one, -1.0)
    part = mixed("jn,jc->nc", section, stacked).reshape(2, factor_one, second, col_count)
    twist_re, twist_im = phase_table(first_idx, second_idx, length, -1.0)
    twist_re = twist_re[:, :, None]
    twist_im = twist_im[:, :, None]
    turned_re = part[0] * twist_re - part[1] * twist_im
    turned_im = part[0] * twist_im + part[1] * twist_re
    turned = jnp.stack([turned_re, turned_im], axis=1).reshape(
        factor_one, 2 * second, col_count
    )
    final = block_table(second_idx, second_idx, second, -1.0)
    done = mixed("jn,kjc->nkc", final, turned)
    return done.reshape(2, length, col_count)


def rows_inverse(spec_re, spec_im, length, m_count):
    row_count = spec_re.shape[0]
    second = length // first_radix
    shaped_re = spec_re.reshape(row_count, first_radix, m_count)
    shaped_im = spec_im.reshape(row_count, first_radix, m_count)
    k_idx = jnp.arange(first_radix, dtype=jnp.int32)
    u_idx = jnp.arange(second, dtype=jnp.int32)
    m_idx = jnp.arange(m_count, dtype=jnp.int32)
    section_re, section_im = phase_table(m_idx, u_idx, second, 1.0)
    part_re, part_im = complex_product("rkm,mu->rku", shaped_re, shaped_im, section_re, section_im)
    twist_re, twist_im = phase_table(k_idx, u_idx, length, 1.0)
    turned_re = part_re * twist_re - part_im * twist_im
    turned_im = part_re * twist_im + part_im * twist_re
    final_re, final_im = phase_table(k_idx, k_idx, first_radix, 1.0)
    done_re, done_im = complex_product("rku,kv->rvu", turned_re, turned_im, final_re, final_im)
    return (done_re.reshape(row_count, length), done_im.reshape(row_count, length))


def wavenumbers(indices, length):
    signed = jnp.where(indices < length // 2, indices, indices - length)
    return (two_pi / length * signed.astype(jnp.float32), indices != length // 2)


def folded_spectra(spectrum, col_idx, ray_all):
    _, length, col_count = spectrum.shape
    norm_factor = float(length * length)
    wave_col, retain_col = wavenumbers(col_idx, length)
    weight = jnp.where(col_idx == 0, 1.0, 2.0).astype(jnp.float32)
    row_idx = jnp.arange(length, dtype=jnp.int32)
    wave_row, retain_row = wavenumbers(row_idx, length)
    wave_row = wave_row[:, None]
    squared = wave_col[None, :] * wave_col[None, :] + wave_row * wave_row
    retain = retain_row[:, None] & retain_col[None, :] & (squared > 0.0)
    safe_sq = jnp.where(retain, squared, 1.0)
    kernel = jnp.where(retain, -2.0 / (safe_sq * norm_factor), 0.0) * weight[None, :]
    phi = kernel[None] * spectrum
    terms = jnp.stack([phi, wave_row[None] * phi, (wave_row * wave_row)[None] * phi])
    terms = terms.reshape(3, 2, length // ray_all, ray_all, col_count)
    return jnp.sum(terms, axis=2)


def per_device(density, lens_weight, plane_count, ray_state):
    sky_count = lax.axis_size("sky")
    sky_index = lax.axis_index("sky")
    ray_split = ray_state.shape[1] // 2
    ray_first = shifted(ray_state[:, :ray_split], "los", HOPS)
    ray_second = shifted(ray_state[:, ray_split:], "los", HOPS)
    plane_cells = density[0]
    length = plane_cells.shape[1]
    second = length // first_radix
    half = second // 2
    ray_dev = ray_state.shape[2]
    ray_all = ray_dev * sky_count
    strength = lens_weight[0] * plane_count[0].astype(jnp.float32)
    rows = rows_forward(plane_cells)
    ray_first, rows = lax.optimization_barrier((ray_first, rows))
    spread = lax.all_to_all(rows, "sky", split_axis=1, concat_axis=0, tiled=True)
    k_local = spread.shape[1]
    spread_re = spread[:, :, :half].reshape(length, k_local * half)
    spread_im = spread[:, :, half:].reshape(length, k_local * half)
    chunks = 2
    chunk_cols = k_local * half // chunks
    q_idx = jnp.arange(ray_all, dtype=jnp.int32)
    back = block_table(q_idx, q_idx, ray_all, 1.0)
    pieces = []
    for chunk in range(chunks):
        cols = slice(chunk * chunk_cols, (chunk + 1) * chunk_cols)
        spectrum = columns_forward(spread_re[:, cols], spread_im[:, cols])
        if chunk == 0:
            ray_second, spectrum = lax.optimization_barrier((ray_second, spectrum))
        position = chunk * chunk_cols + jnp.arange(chunk_cols, dtype=jnp.int32)
        col_idx = sky_index * k_local + position // half + first_radix * (position % half)
        folds = folded_spectra(spectrum, col_idx, ray_all)
        at_rows = mixed("pjc,jn->pnc", folds.reshape(3, 2 * ray_all, chunk_cols), back)
        at_rows = at_rows.reshape(3, 2, ray_all, chunk_cols // half, half)
        returned = lax.all_to_all(at_rows, "sky", split_axis=2, concat_axis=3, tiled=True)
        dense = returned.reshape(3 * 2 * ray_dev, returned.shape[3] * half) * strength
        moved = jnp.stack(
            [shifted(dense, "los", HOPS - step_index) for step_index in range(HOPS)]
        )
        pieces.append(moved.reshape(HOPS, 3, 2, ray_dev, sky_count, chunk_cols // half, half))
    arrived = jnp.stack(pieces, axis=5)
    k_all = sky_count * k_local
    arrived = arrived.reshape(HOPS, 3, 2, ray_dev, k_all, half)
    kx_idx = jnp.arange(k_all, dtype=jnp.int32)[:, None] + first_radix * jnp.arange(
        half, dtype=jnp.int32
    )[None, :]
    wave_col = wavenumbers(kx_idx, length)[0]
    f0_re, f0_im = arrived[:, 0, 0], arrived[:, 0, 1]
    f1_re, f1_im = arrived[:, 1, 0], arrived[:, 1, 1]
    f2_re, f2_im = arrived[:, 2, 0], arrived[:, 2, 1]
    col_sq = wave_col * wave_col
    all_re = jnp.stack(
        [-wave_col * f0_im, -f1_im, -col_sq * f0_re, -f2_re, -wave_col * f1_re], axis=1
    )
    all_im = jnp.stack(
        [wave_col * f0_re, f1_re, -col_sq * f0_im, -f2_im, -wave_col * f1_im], axis=1
    )
    flat_re = all_re.reshape(HOPS * 5 * ray_dev, k_all * half)
    flat_im = all_im.reshape(HOPS * 5 * ray_dev, k_all * half)
    field_re, _ = rows_inverse(flat_re, flat_im, length, half)
    fields = field_re.reshape(HOPS, 5, ray_dev, length)
    ray_tile = jnp.concatenate([ray_first, ray_second], axis=1)
    for step_index in range(HOPS):
        ray_tile = lens_step(ray_tile, fields[step_index][None])
    return ray_tile


def solution(mesh):
    return jax.shard_map(
        per_device,
        mesh=mesh,
        in_specs=(
            P(("real", "los"), "sky", None),
            P(("real", "los")),
            P(("real", "los")),
            P(("real", "los"), None, "sky", None),
        ),
        out_specs=P(("real", "los"), None, "sky", None),
        check_vma=False,
    )
```

```python
import math

import jax
import jax.numpy as jnp
from jax import lax
from jax.sharding import PartitionSpec as P

HOPS = 4


two_pi = 2.0 * math.pi
highest = lax.Precision.HIGH
first_radix = 16


def shifted(block, axis, distance):
    devices = range(lax.axis_size(axis))
    route = [((i - distance) % len(devices), i) for i in devices]
    return lax.ppermute(block, axis, route)


def lens_step(ray_tile, fields):
    disp_x = ray_tile[..., 0, :, :]
    disp_y = ray_tile[..., 1, :, :]
    tilt_x = ray_tile[..., 2, :, :]
    tilt_y = ray_tile[..., 3, :, :]
    jac_xx = ray_tile[..., 4, :, :]
    jac_xy = ray_tile[..., 5, :, :]
    jac_yx = ray_tile[..., 6, :, :]
    jac_yy = ray_tile[..., 7, :, :]
    rate_xx = ray_tile[..., 8, :, :]
    rate_xy = ray_tile[..., 9, :, :]
    rate_yx = ray_tile[..., 10, :, :]
    rate_yy = ray_tile[..., 11, :, :]
    bend_x = fields[..., 0, :, :]
    bend_y = fields[..., 1, :, :]
    hess_xx = fields[..., 2, :, :]
    hess_yy = fields[..., 3, :, :]
    hess_xy = fields[..., 4, :, :]
    push_x = bend_x + hess_xx * disp_x + hess_xy * disp_y
    push_y = bend_y + hess_xy * disp_x + hess_yy * disp_y
    new_tilt_x = tilt_x - push_x
    new_tilt_y = tilt_y - push_y
    new_disp_x = disp_x + new_tilt_x
    new_disp_y = disp_y + new_tilt_y
    new_rate_xx = rate_xx - (hess_xx * jac_xx + hess_xy * jac_yx)
    new_rate_xy = rate_xy - (hess_xx * jac_xy + hess_xy * jac_yy)
    new_rate_yx = rate_yx - (hess_xy * jac_xx + hess_yy * jac_yx)
    new_rate_yy = rate_yy - (hess_xy * jac_xy + hess_yy * jac_yy)
    new_jac_xx = jac_xx + new_rate_xx
    new_jac_xy = jac_xy + new_rate_xy
    new_jac_yx = jac_yx + new_rate_yx
    new_jac_yy = jac_yy + new_rate_yy
    return jnp.stack(
        [
            new_disp_x,
            new_disp_y,
            new_tilt_x,
            new_tilt_y,
            new_jac_xx,
            new_jac_xy,
            new_jac_yx,
            new_jac_yy,
            new_rate_xx,
            new_rate_xy,
            new_rate_yx,
            new_rate_yy,
        ],
        axis=-3,
    )


def phase_table(left_idx, right_idx, modulus, orient):
    product = left_idx[:, None] * right_idx[None, :] % modulus
    angle = orient * two_pi / modulus * product.astype(jnp.float32)
    return (jnp.cos(angle), jnp.sin(angle))


def block_table(left_idx, right_idx, modulus, orient):
    t_re, t_im = phase_table(left_idx, right_idx, modulus, orient)
    top = jnp.concatenate([t_re, t_im], axis=1)
    bottom = jnp.concatenate([-t_im, t_re], axis=1)
    return jnp.concatenate([top, bottom], axis=0)


def mixed(form, left_op, right_op):
    return jnp.einsum(
        form, left_op, right_op, precision=highest, preferred_element_type=jnp.float32
    )


def complex_product(form, real_in, imag_in, table_re, table_im):
    if imag_in is None:
        return (mixed(form, real_in, table_re), mixed(form, real_in, table_im))
    out_re = mixed(form, real_in, table_re) - mixed(form, imag_in, table_im)
    out_im = mixed(form, real_in, table_im) + mixed(form, imag_in, table_re)
    return (out_re, out_im)


def first_factor_of(length):
    factor_one = 1
    while factor_one * factor_one < length and length % (factor_one * 2) == 0:
        factor_one = factor_one * 2
    return factor_one


def rows_forward(cells):
    row_count, length = cells.shape
    second = length // first_radix
    half = second // 2
    shaped = cells.reshape(row_count, first_radix, second)
    v_idx = jnp.arange(first_radix, dtype=jnp.int32)
    u_idx = jnp.arange(second, dtype=jnp.int32)
    m_idx = jnp.arange(half, dtype=jnp.int32)
    section_re, section_im = phase_table(v_idx, v_idx, first_radix, -1.0)
    section = jnp.concatenate([section_re, section_im], axis=1)
    part = mixed("rvu,vk->rku", shaped, section)
    part_re = part[:, :first_radix]
    part_im = part[:, first_radix:]
    twist_re, twist_im = phase_table(v_idx, u_idx, length, -1.0)
    turned_re = part_re * twist_re - part_im * twist_im
    turned_im = part_re * twist_im + part_im * twist_re
    turned = jnp.concatenate([turned_re, turned_im], axis=2)
    final = block_table(u_idx, m_idx, second, -1.0)
    return mixed("rkj,jn->rkn", turned, final)


def columns_forward(spread_re, spread_im):
    length, col_count = spread_re.shape
    factor_one = first_factor_of(length)
    second = length // factor_one
    first_idx = jnp.arange(factor_one, dtype=jnp.int32)
    second_idx = jnp.arange(second, dtype=jnp.int32)
    stacked = jnp.concatenate(
        [
            spread_re.reshape(factor_one, second * col_count),
            spread_im.reshape(factor_one, second * col_count),
        ],
        axis=0,
    )
    section = block_table(first_idx, first_idx, factor_one, -1.0)
    part = mixed("jn,jc->nc", section, stacked).reshape(2, factor_one, second, col_count)
    twist_re, twist_im = phase_table(first_idx, second_idx, length, -1.0)
    twist_re = twist_re[:, :, None]
    twist_im = twist_im[:, :, None]
    turned_re = part[0] * twist_re - part[1] * twist_im
    turned_im = part[0] * twist_im + part[1] * twist_re
    turned = jnp.stack([turned_re, turned_im], axis=1).reshape(
        factor_one, 2 * second, col_count
    )
    final = block_table(second_idx, second_idx, second, -1.0)
    done = mixed("jn,kjc->nkc", final, turned)
    return done.reshape(2, length, col_count)


def rows_inverse(spec_re, spec_im, length, m_count):
    row_count = spec_re.shape[0]
    second = length // first_radix
    shaped_re = spec_re.reshape(row_count, first_radix, m_count)
    shaped_im = spec_im.reshape(row_count, first_radix, m_count)
    k_idx = jnp.arange(first_radix, dtype=jnp.int32)
    u_idx = jnp.arange(second, dtype=jnp.int32)
    m_idx = jnp.arange(m_count, dtype=jnp.int32)
    section_re, section_im = phase_table(m_idx, u_idx, second, 1.0)
    part_re, part_im = complex_product("rkm,mu->rku", shaped_re, shaped_im, section_re, section_im)
    twist_re, twist_im = phase_table(k_idx, u_idx, length, 1.0)
    turned_re = part_re * twist_re - part_im * twist_im
    turned_im = part_re * twist_im + part_im * twist_re
    final_re, final_im = phase_table(k_idx, k_idx, first_radix, 1.0)
    done_re, done_im = complex_product("rku,kv->rvu", turned_re, turned_im, final_re, final_im)
    return (done_re.reshape(row_count, length), done_im.reshape(row_count, length))


def wavenumbers(indices, length):
    signed = jnp.where(indices < length // 2, indices, indices - length)
    return (two_pi / length * signed.astype(jnp.float32), indices != length // 2)


def folded_spectra(spectrum, col_idx, ray_all):
    _, length, col_count = spectrum.shape
    norm_factor = float(length * length)
    wave_col, retain_col = wavenumbers(col_idx, length)
    weight = jnp.where(col_idx == 0, 1.0, 2.0).astype(jnp.float32)
    row_idx = jnp.arange(length, dtype=jnp.int32)
    wave_row, retain_row = wavenumbers(row_idx, length)
    wave_row = wave_row[:, None]
    squared = wave_col[None, :] * wave_col[None, :] + wave_row * wave_row
    retain = retain_row[:, None] & retain_col[None, :] & (squared > 0.0)
    safe_sq = jnp.where(retain, squared, 1.0)
    kernel = jnp.where(retain, -2.0 / (safe_sq * norm_factor), 0.0) * weight[None, :]
    phi = kernel[None] * spectrum
    terms = jnp.stack([phi, wave_row[None] * phi, (wave_row * wave_row)[None] * phi])
    terms = terms.reshape(3, 2, length // ray_all, ray_all, col_count)
    return jnp.sum(terms, axis=2)


def dense_tables(length, count, offset):
    low = first_factor_of(length)
    high = length // low
    k_idx = jnp.arange(count, dtype=jnp.int32) + offset
    low_re, low_im = phase_table(jnp.arange(low, dtype=jnp.int32), k_idx, length, -1.0)
    high_re, high_im = phase_table(
        jnp.arange(high, dtype=jnp.int32) * low, k_idx, length, -1.0
    )
    table_re = high_re[:, None] * low_re[None] - high_im[:, None] * low_im[None]
    table_im = high_re[:, None] * low_im[None] + high_im[:, None] * low_re[None]
    return (table_re.reshape(length, count), table_im.reshape(length, count))


def per_device(density, lens_weight, plane_count, ray_state):
    sky_count = lax.axis_size("sky")
    sky_index = lax.axis_index("sky")
    ray_tile = shifted(ray_state, "los", HOPS)
    plane_cells = density[0]
    length = plane_cells.shape[1]
    second = length // first_radix
    half = second // 2
    ray_dev = ray_state.shape[2]
    ray_all = ray_dev * sky_count
    strength = lens_weight[0] * plane_count[0].astype(jnp.float32)
    half_len = length // 2
    offset = jnp.minimum(sky_index, 0)
    table_re, table_im = dense_tables(length, half_len, offset)
    rows = jnp.stack(
        [
            mixed("rx,xk->rk", plane_cells, table_re),
            mixed("rx,xk->rk", plane_cells, table_im),
        ]
    )
    spread = lax.all_to_all(rows, "sky", split_axis=2, concat_axis=1, tiled=True)
    col_count = spread.shape[2]
    spread_re = spread[0]
    spread_im = spread[1]
    spectrum = columns_forward(spread_re, spread_im)
    ray_tile, spectrum = lax.optimization_barrier((ray_tile, spectrum))
    col_idx = sky_index * col_count + jnp.arange(col_count, dtype=jnp.int32)
    folds = folded_spectra(spectrum, col_idx, ray_all)
    q_idx = jnp.arange(ray_all, dtype=jnp.int32)
    back = block_table(q_idx, q_idx, ray_all, 1.0)
    at_rows = mixed("pjc,jn->pnc", folds.reshape(3, 2 * ray_all, col_count), back)
    at_rows = at_rows.reshape(3, 2, ray_all, col_count)
    returned = lax.all_to_all(at_rows, "sky", split_axis=2, concat_axis=3, tiled=True)
    dense = returned.reshape(3 * 2 * ray_dev, half_len) * strength
    arrived = jnp.stack(
        [shifted(dense, "los", HOPS - step_index) for step_index in range(HOPS)]
    ).reshape(HOPS, 3, 2, ray_dev, half_len)
    wave_col = wavenumbers(jnp.arange(half_len, dtype=jnp.int32), length)[0]
    f0_re, f0_im = arrived[:, 0, 0], arrived[:, 0, 1]
    f1_re, f1_im = arrived[:, 1, 0], arrived[:, 1, 1]
    f2_re, f2_im = arrived[:, 2, 0], arrived[:, 2, 1]
    col_sq = wave_col * wave_col
    all_re = jnp.stack(
        [-wave_col * f0_im, -f1_im, -col_sq * f0_re, -f2_re, -wave_col * f1_re], axis=1
    )
    all_im = jnp.stack(
        [wave_col * f0_re, f1_re, -col_sq * f0_im, -f2_im, -wave_col * f1_im], axis=1
    )
    flat_re = all_re.reshape(HOPS * 5 * ray_dev, half_len)
    flat_im = all_im.reshape(HOPS * 5 * ray_dev, half_len)
    field_re = mixed("rk,xk->rx", flat_re, table_re) + mixed("rk,xk->rx", flat_im, table_im)
    fields = field_re.reshape(HOPS, 5, ray_dev, length)
    for step_index in range(HOPS):
        ray_tile = lens_step(ray_tile, fields[step_index][None])
    return ray_tile


def solution(mesh):
    return jax.shard_map(
        per_device,
        mesh=mesh,
        in_specs=(
            P(("real", "los"), "sky", None),
            P(("real", "los")),
            P(("real", "los")),
            P(("real", "los"), None, "sky", None),
        ),
        out_specs=P(("real", "los"), None, "sky", None),
        check_vma=False,
    )
```

```python
import math

import jax
import jax.numpy as jnp
from jax import lax
from jax.sharding import PartitionSpec as P

HOPS = 4


two_pi = 2.0 * math.pi
highest = lax.Precision.HIGH
first_radix = 16


def shifted(block, axis, distance):
    devices = range(lax.axis_size(axis))
    route = [((i - distance) % len(devices), i) for i in devices]
    return lax.ppermute(block, axis, route)


def lens_step(ray_tile, fields):
    disp_x = ray_tile[..., 0, :, :]
    disp_y = ray_tile[..., 1, :, :]
    tilt_x = ray_tile[..., 2, :, :]
    tilt_y = ray_tile[..., 3, :, :]
    jac_xx = ray_tile[..., 4, :, :]
    jac_xy = ray_tile[..., 5, :, :]
    jac_yx = ray_tile[..., 6, :, :]
    jac_yy = ray_tile[..., 7, :, :]
    rate_xx = ray_tile[..., 8, :, :]
    rate_xy = ray_tile[..., 9, :, :]
    rate_yx = ray_tile[..., 10, :, :]
    rate_yy = ray_tile[..., 11, :, :]
    bend_x = fields[..., 0, :, :]
    bend_y = fields[..., 1, :, :]
    hess_xx = fields[..., 2, :, :]
    hess_yy = fields[..., 3, :, :]
    hess_xy = fields[..., 4, :, :]
    push_x = bend_x + hess_xx * disp_x + hess_xy * disp_y
    push_y = bend_y + hess_xy * disp_x + hess_yy * disp_y
    new_tilt_x = tilt_x - push_x
    new_tilt_y = tilt_y - push_y
    new_disp_x = disp_x + new_tilt_x
    new_disp_y = disp_y + new_tilt_y
    new_rate_xx = rate_xx - (hess_xx * jac_xx + hess_xy * jac_yx)
    new_rate_xy = rate_xy - (hess_xx * jac_xy + hess_xy * jac_yy)
    new_rate_yx = rate_yx - (hess_xy * jac_xx + hess_yy * jac_yx)
    new_rate_yy = rate_yy - (hess_xy * jac_xy + hess_yy * jac_yy)
    new_jac_xx = jac_xx + new_rate_xx
    new_jac_xy = jac_xy + new_rate_xy
    new_jac_yx = jac_yx + new_rate_yx
    new_jac_yy = jac_yy + new_rate_yy
    return jnp.stack(
        [
            new_disp_x,
            new_disp_y,
            new_tilt_x,
            new_tilt_y,
            new_jac_xx,
            new_jac_xy,
            new_jac_yx,
            new_jac_yy,
            new_rate_xx,
            new_rate_xy,
            new_rate_yx,
            new_rate_yy,
        ],
        axis=-3,
    )


def phase_table(left_idx, right_idx, modulus, orient):
    product = left_idx[:, None] * right_idx[None, :] % modulus
    angle = orient * two_pi / modulus * product.astype(jnp.float32)
    return (jnp.cos(angle), jnp.sin(angle))


def block_table(left_idx, right_idx, modulus, orient):
    t_re, t_im = phase_table(left_idx, right_idx, modulus, orient)
    top = jnp.concatenate([t_re, t_im], axis=1)
    bottom = jnp.concatenate([-t_im, t_re], axis=1)
    return jnp.concatenate([top, bottom], axis=0)


def mixed(form, left_op, right_op):
    return jnp.einsum(
        form, left_op, right_op, precision=highest, preferred_element_type=jnp.float32
    )


def complex_product(form, real_in, imag_in, table_re, table_im):
    if imag_in is None:
        return (mixed(form, real_in, table_re), mixed(form, real_in, table_im))
    out_re = mixed(form, real_in, table_re) - mixed(form, imag_in, table_im)
    out_im = mixed(form, real_in, table_im) + mixed(form, imag_in, table_re)
    return (out_re, out_im)


def first_factor_of(length):
    factor_one = 1
    while factor_one * factor_one < length and length % (factor_one * 2) == 0:
        factor_one = factor_one * 2
    return factor_one


def rows_forward(cells):
    row_count, length = cells.shape
    second = length // first_radix
    half = second // 2
    shaped = cells.reshape(row_count, first_radix, second)
    v_idx = jnp.arange(first_radix, dtype=jnp.int32)
    u_idx = jnp.arange(second, dtype=jnp.int32)
    m_idx = jnp.arange(half, dtype=jnp.int32)
    section_re, section_im = phase_table(v_idx, v_idx, first_radix, -1.0)
    section = jnp.stack([section_re, section_im], axis=1)
    part = mixed("rvu,vik->rkiu", shaped, section).reshape(row_count, first_radix, 2 * second)
    freq = v_idx[:, None] + first_radix * m_idx[None, :]
    product = u_idx[None, :, None] * freq[:, None, :] % length
    angle = -two_pi / length * product.astype(jnp.float32)
    t_re = jnp.cos(angle)
    t_im = jnp.sin(angle)
    top = jnp.concatenate([t_re, t_im], axis=2)
    bottom = jnp.concatenate([-t_im, t_re], axis=2)
    final = jnp.concatenate([top, bottom], axis=1)
    return mixed("rkj,kjn->rkn", part, final)


def columns_forward(spread_re, spread_im):
    length, col_count = spread_re.shape
    factor_one = first_factor_of(length)
    second = length // factor_one
    first_idx = jnp.arange(factor_one, dtype=jnp.int32)
    second_idx = jnp.arange(second, dtype=jnp.int32)
    stacked = jnp.concatenate(
        [
            spread_re.reshape(factor_one, second * col_count),
            spread_im.reshape(factor_one, second * col_count),
        ],
        axis=0,
    )
    section = block_table(first_idx, first_idx, factor_one, -1.0)
    part = mixed("jn,jc->nc", section, stacked).reshape(2, factor_one, second, col_count)
    twist_re, twist_im = phase_table(first_idx, second_idx, length, -1.0)
    twist_re = twist_re[:, :, None]
    twist_im = twist_im[:, :, None]
    turned_re = part[0] * twist_re - part[1] * twist_im
    turned_im = part[0] * twist_im + part[1] * twist_re
    turned = jnp.stack([turned_re, turned_im], axis=1).reshape(
        factor_one, 2 * second, col_count
    )
    final = block_table(second_idx, second_idx, second, -1.0)
    done = mixed("jn,kjc->nkc", final, turned)
    return done.reshape(2, length, col_count)


def rows_inverse(spec_re, spec_im, length, m_count):
    row_count = spec_re.shape[0]
    second = length // first_radix
    shaped_re = spec_re.reshape(row_count, first_radix, m_count)
    shaped_im = spec_im.reshape(row_count, first_radix, m_count)
    k_idx = jnp.arange(first_radix, dtype=jnp.int32)
    u_idx = jnp.arange(second, dtype=jnp.int32)
    m_idx = jnp.arange(m_count, dtype=jnp.int32)
    section_re, section_im = phase_table(m_idx, u_idx, second, 1.0)
    part_re, part_im = complex_product("rkm,mu->rku", shaped_re, shaped_im, section_re, section_im)
    twist_re, twist_im = phase_table(k_idx, u_idx, length, 1.0)
    turned_re = part_re * twist_re - part_im * twist_im
    turned_im = part_re * twist_im + part_im * twist_re
    final_re, final_im = phase_table(k_idx, k_idx, first_radix, 1.0)
    done_re, done_im = complex_product("rku,kv->rvu", turned_re, turned_im, final_re, final_im)
    return (done_re.reshape(row_count, length), done_im.reshape(row_count, length))


def wavenumbers(indices, length):
    signed = jnp.where(indices < length // 2, indices, indices - length)
    return (two_pi / length * signed.astype(jnp.float32), indices != length // 2)


def folded_spectra(spectrum, col_idx, ray_all):
    _, length, col_count = spectrum.shape
    norm_factor = float(length * length)
    wave_col, retain_col = wavenumbers(col_idx, length)
    weight = jnp.where(col_idx == 0, 1.0, 2.0).astype(jnp.float32)
    row_idx = jnp.arange(length, dtype=jnp.int32)
    wave_row, retain_row = wavenumbers(row_idx, length)
    wave_row = wave_row[:, None]
    squared = wave_col[None, :] * wave_col[None, :] + wave_row * wave_row
    retain = retain_row[:, None] & retain_col[None, :] & (squared > 0.0)
    safe_sq = jnp.where(retain, squared, 1.0)
    kernel = jnp.where(retain, -2.0 / (safe_sq * norm_factor), 0.0) * weight[None, :]
    phi = kernel[None] * spectrum
    terms = jnp.stack([phi, wave_row[None] * phi, (wave_row * wave_row)[None] * phi])
    terms = terms.reshape(3, 2, length // ray_all, ray_all, col_count)
    return jnp.sum(terms, axis=2)


def per_device(density, lens_weight, plane_count, ray_state):
    sky_count = lax.axis_size("sky")
    sky_index = lax.axis_index("sky")
    ray_tile = shifted(ray_state, "los", HOPS)
    plane_cells = density[0]
    length = plane_cells.shape[1]
    second = length // first_radix
    half = second // 2
    ray_dev = ray_state.shape[2]
    ray_all = ray_dev * sky_count
    strength = lens_weight[0] * plane_count[0].astype(jnp.float32)
    rows = rows_forward(plane_cells)
    spread = lax.all_to_all(rows, "sky", split_axis=1, concat_axis=0, tiled=True)
    k_local = spread.shape[1]
    spread_re = spread[:, :, :half].reshape(length, k_local * half)
    spread_im = spread[:, :, half:].reshape(length, k_local * half)
    spectrum = columns_forward(spread_re, spread_im)
    ray_tile, spectrum = lax.optimization_barrier((ray_tile, spectrum))
    position = jnp.arange(k_local * half, dtype=jnp.int32)
    col_idx = sky_index * k_local + position // half + first_radix * (position % half)
    folds = folded_spectra(spectrum, col_idx, ray_all)
    q_idx = jnp.arange(ray_all, dtype=jnp.int32)
    back = block_table(q_idx, q_idx, ray_all, 1.0)
    at_rows = mixed("pjc,jn->pnc", folds.reshape(3, 2 * ray_all, k_local * half), back)
    at_rows = at_rows.reshape(3, 2, ray_all, k_local, half)
    returned = lax.all_to_all(at_rows, "sky", split_axis=2, concat_axis=3, tiled=True)
    k_all = returned.shape[3]
    dense = returned.reshape(3 * 2 * ray_dev, k_all * half) * strength
    arrived = jnp.stack(
        [shifted(dense, "los", HOPS - step_index) for step_index in range(HOPS)]
    ).reshape(HOPS, 3, 2, ray_dev, k_all, half)
    kx_idx = jnp.arange(k_all, dtype=jnp.int32)[:, None] + first_radix * jnp.arange(
        half, dtype=jnp.int32
    )[None, :]
    wave_col = wavenumbers(kx_idx, length)[0]
    f0_re, f0_im = arrived[:, 0, 0], arrived[:, 0, 1]
    f1_re, f1_im = arrived[:, 1, 0], arrived[:, 1, 1]
    f2_re, f2_im = arrived[:, 2, 0], arrived[:, 2, 1]
    col_sq = wave_col * wave_col
    all_re = jnp.stack(
        [-wave_col * f0_im, -f1_im, -col_sq * f0_re, -f2_re, -wave_col * f1_re], axis=1
    )
    all_im = jnp.stack(
        [wave_col * f0_re, f1_re, -col_sq * f0_im, -f2_im, -wave_col * f1_im], axis=1
    )
    flat_re = all_re.reshape(HOPS * 5 * ray_dev, k_all * half)
    flat_im = all_im.reshape(HOPS * 5 * ray_dev, k_all * half)
    field_re, _ = rows_inverse(flat_re, flat_im, length, half)
    fields = field_re.reshape(HOPS, 5, ray_dev, length)
    for step_index in range(HOPS):
        ray_tile = lens_step(ray_tile, fields[step_index][None])
    return ray_tile


def solution(mesh):
    return jax.shard_map(
        per_device,
        mesh=mesh,
        in_specs=(
            P(("real", "los"), "sky", None),
            P(("real", "los")),
            P(("real", "los")),
            P(("real", "los"), None, "sky", None),
        ),
        out_specs=P(("real", "los"), None, "sky", None),
        check_vma=False,
    )
```

```python
import math

import jax
import jax.numpy as jnp
from jax import lax
from jax.sharding import PartitionSpec as P

HOPS = 4


two_pi = 2.0 * math.pi
highest = lax.Precision.HIGH
first_radix = 16


def shifted(block, axis, distance):
    devices = range(lax.axis_size(axis))
    route = [((i - distance) % len(devices), i) for i in devices]
    return lax.ppermute(block, axis, route)


def lens_step(ray_tile, fields):
    disp_x = ray_tile[..., 0, :, :]
    disp_y = ray_tile[..., 1, :, :]
    tilt_x = ray_tile[..., 2, :, :]
    tilt_y = ray_tile[..., 3, :, :]
    jac_xx = ray_tile[..., 4, :, :]
    jac_xy = ray_tile[..., 5, :, :]
    jac_yx = ray_tile[..., 6, :, :]
    jac_yy = ray_tile[..., 7, :, :]
    rate_xx = ray_tile[..., 8, :, :]
    rate_xy = ray_tile[..., 9, :, :]
    rate_yx = ray_tile[..., 10, :, :]
    rate_yy = ray_tile[..., 11, :, :]
    bend_x = fields[..., 0, :, :]
    bend_y = fields[..., 1, :, :]
    hess_xx = fields[..., 2, :, :]
    hess_yy = fields[..., 3, :, :]
    hess_xy = fields[..., 4, :, :]
    push_x = bend_x + hess_xx * disp_x + hess_xy * disp_y
    push_y = bend_y + hess_xy * disp_x + hess_yy * disp_y
    new_tilt_x = tilt_x - push_x
    new_tilt_y = tilt_y - push_y
    new_disp_x = disp_x + new_tilt_x
    new_disp_y = disp_y + new_tilt_y
    new_rate_xx = rate_xx - (hess_xx * jac_xx + hess_xy * jac_yx)
    new_rate_xy = rate_xy - (hess_xx * jac_xy + hess_xy * jac_yy)
    new_rate_yx = rate_yx - (hess_xy * jac_xx + hess_yy * jac_yx)
    new_rate_yy = rate_yy - (hess_xy * jac_xy + hess_yy * jac_yy)
    new_jac_xx = jac_xx + new_rate_xx
    new_jac_xy = jac_xy + new_rate_xy
    new_jac_yx = jac_yx + new_rate_yx
    new_jac_yy = jac_yy + new_rate_yy
    return jnp.stack(
        [
            new_disp_x,
            new_disp_y,
            new_tilt_x,
            new_tilt_y,
            new_jac_xx,
            new_jac_xy,
            new_jac_yx,
            new_jac_yy,
            new_rate_xx,
            new_rate_xy,
            new_rate_yx,
            new_rate_yy,
        ],
        axis=-3,
    )


def phase_table(left_idx, right_idx, modulus, orient):
    product = left_idx[:, None] * right_idx[None, :] % modulus
    angle = orient * two_pi / modulus * product.astype(jnp.float32)
    return (jnp.cos(angle), jnp.sin(angle))


def block_table(left_idx, right_idx, modulus, orient):
    t_re, t_im = phase_table(left_idx, right_idx, modulus, orient)
    top = jnp.concatenate([t_re, t_im], axis=1)
    bottom = jnp.concatenate([-t_im, t_re], axis=1)
    return jnp.concatenate([top, bottom], axis=0)


def mixed(form, left_op, right_op):
    return jnp.einsum(
        form, left_op, right_op, precision=highest, preferred_element_type=jnp.float32
    )


def complex_product(form, real_in, imag_in, table_re, table_im):
    if imag_in is None:
        return (mixed(form, real_in, table_re), mixed(form, real_in, table_im))
    out_re = mixed(form, real_in, table_re) - mixed(form, imag_in, table_im)
    out_im = mixed(form, real_in, table_im) + mixed(form, imag_in, table_re)
    return (out_re, out_im)


def first_factor_of(length):
    factor_one = 1
    while factor_one * factor_one < length and length % (factor_one * 2) == 0:
        factor_one = factor_one * 2
    return factor_one


def rows_forward(cells):
    row_count, length = cells.shape
    second = length // first_radix
    half = second // 2
    shaped = cells.reshape(row_count, first_radix, second)
    v_idx = jnp.arange(first_radix, dtype=jnp.int32)
    u_idx = jnp.arange(second, dtype=jnp.int32)
    m_idx = jnp.arange(half, dtype=jnp.int32)
    section_re, section_im = phase_table(v_idx, v_idx, first_radix, -1.0)
    section = jnp.concatenate([section_re, section_im], axis=1)
    part = mixed("rvu,vk->rku", shaped, section)
    part_re = part[:, :first_radix]
    part_im = part[:, first_radix:]
    twist_re, twist_im = phase_table(v_idx, u_idx, length, -1.0)
    turned_re = part_re * twist_re - part_im * twist_im
    turned_im = part_re * twist_im + part_im * twist_re
    turned = jnp.concatenate([turned_re, turned_im], axis=2)
    final = block_table(u_idx, m_idx, second, -1.0)
    return mixed("rkj,jn->rkn", turned, final)


def columns_forward(spread_re, spread_im):
    length, col_count = spread_re.shape
    factor_one = first_factor_of(length)
    second = length // factor_one
    first_idx = jnp.arange(factor_one, dtype=jnp.int32)
    second_idx = jnp.arange(second, dtype=jnp.int32)
    stacked = jnp.concatenate(
        [
            spread_re.reshape(factor_one, second * col_count),
            spread_im.reshape(factor_one, second * col_count),
        ],
        axis=0,
    )
    section = block_table(first_idx, first_idx, factor_one, -1.0)
    part = mixed("jn,jc->nc", section, stacked).reshape(2, factor_one, second, col_count)
    twist_re, twist_im = phase_table(first_idx, second_idx, length, -1.0)
    sign = jnp.array([-1.0, 1.0], jnp.float32)[:, None, None, None]
    turned = part * twist_re[None, :, :, None] + part[::-1] * (sign * twist_im[None, :, :, None])
    turned = jnp.transpose(turned, (1, 0, 2, 3)).reshape(factor_one, 2 * second, col_count)
    final = block_table(second_idx, second_idx, second, -1.0)
    done = mixed("kjc,jn->knc", turned, final)
    return done.reshape(factor_one, 2, second, col_count)


def rows_inverse(spec_re, spec_im, length, m_count):
    row_count = spec_re.shape[0]
    second = length // first_radix
    shaped_re = spec_re.reshape(row_count, first_radix, m_count)
    shaped_im = spec_im.reshape(row_count, first_radix, m_count)
    k_idx = jnp.arange(first_radix, dtype=jnp.int32)
    u_idx = jnp.arange(second, dtype=jnp.int32)
    m_idx = jnp.arange(m_count, dtype=jnp.int32)
    section_re, section_im = phase_table(m_idx, u_idx, second, 1.0)
    part_re, part_im = complex_product("rkm,mu->rku", shaped_re, shaped_im, section_re, section_im)
    twist_re, twist_im = phase_table(k_idx, u_idx, length, 1.0)
    turned_re = part_re * twist_re - part_im * twist_im
    turned_im = part_re * twist_im + part_im * twist_re
    final_re, final_im = phase_table(k_idx, k_idx, first_radix, 1.0)
    done_re, done_im = complex_product("rku,kv->rvu", turned_re, turned_im, final_re, final_im)
    return (done_re.reshape(row_count, length), done_im.reshape(row_count, length))


def wavenumbers(indices, length):
    signed = jnp.where(indices < length // 2, indices, indices - length)
    return (two_pi / length * signed.astype(jnp.float32), indices != length // 2)


def folded_spectra(spectrum, col_idx, ray_all):
    k_count, _, m_count, col_count = spectrum.shape
    length = k_count * m_count
    norm_factor = float(length * length)
    wave_col, retain_col = wavenumbers(col_idx, length)
    weight = jnp.where(col_idx == 0, 1.0, 2.0).astype(jnp.float32)
    row_idx = (
        jnp.arange(k_count, dtype=jnp.int32)[:, None]
        + k_count * jnp.arange(m_count, dtype=jnp.int32)[None, :]
    )
    wave_row, retain_row = wavenumbers(row_idx, length)
    wave_row = wave_row[:, None, :, None]
    retain_row = retain_row[:, None, :, None]
    squared = wave_col * wave_col + wave_row * wave_row
    retain = retain_row & retain_col & (squared > 0.0)
    safe_sq = jnp.where(retain, squared, 1.0)
    kernel = jnp.where(retain, -2.0 / (safe_sq * norm_factor), 0.0) * weight
    phi = kernel * spectrum
    terms = jnp.stack([phi, wave_row * phi, (wave_row * wave_row) * phi])
    terms = terms.reshape(3, k_count // ray_all, ray_all, 2, m_count, col_count)
    return jnp.transpose(jnp.sum(terms, axis=(1, 4)), (0, 2, 1, 3))


def per_device(density, lens_weight, plane_count, ray_state):
    sky_count = lax.axis_size("sky")
    sky_index = lax.axis_index("sky")
    ray_tile = shifted(ray_state, "los", HOPS)
    plane_cells = density[0]
    length = plane_cells.shape[1]
    second = length // first_radix
    half = second // 2
    ray_dev = ray_state.shape[2]
    ray_all = ray_dev * sky_count
    strength = lens_weight[0] * plane_count[0].astype(jnp.float32)
    rows = rows_forward(plane_cells)
    spread = lax.all_to_all(rows, "sky", split_axis=1, concat_axis=0, tiled=True)
    k_local = spread.shape[1]
    spread_re = spread[:, :, :half].reshape(length, k_local * half)
    spread_im = spread[:, :, half:].reshape(length, k_local * half)
    spectrum = columns_forward(spread_re, spread_im)
    ray_tile, spectrum = lax.optimization_barrier((ray_tile, spectrum))
    position = jnp.arange(k_local * half, dtype=jnp.int32)
    col_idx = sky_index * k_local + position // half + first_radix * (position % half)
    folds = folded_spectra(spectrum, col_idx, ray_all)
    q_idx = jnp.arange(ray_all, dtype=jnp.int32)
    back = block_table(q_idx, q_idx, ray_all, 1.0)
    at_rows = mixed("pjc,jn->pnc", folds.reshape(3, 2 * ray_all, k_local * half), back)
    at_rows = at_rows.reshape(3, 2, ray_all, k_local, half)
    returned = lax.all_to_all(at_rows, "sky", split_axis=2, concat_axis=3, tiled=True)
    k_all = returned.shape[3]
    dense = returned.reshape(3 * 2 * ray_dev, k_all * half) * strength
    arrived = jnp.stack(
        [shifted(dense, "los", HOPS - step_index) for step_index in range(HOPS)]
    ).reshape(HOPS, 3, 2, ray_dev, k_all, half)
    kx_idx = jnp.arange(k_all, dtype=jnp.int32)[:, None] + first_radix * jnp.arange(
        half, dtype=jnp.int32
    )[None, :]
    wave_col = wavenumbers(kx_idx, length)[0]
    f0_re, f0_im = arrived[:, 0, 0], arrived[:, 0, 1]
    f1_re, f1_im = arrived[:, 1, 0], arrived[:, 1, 1]
    f2_re, f2_im = arrived[:, 2, 0], arrived[:, 2, 1]
    col_sq = wave_col * wave_col
    all_re = jnp.stack(
        [-wave_col * f0_im, -f1_im, -col_sq * f0_re, -f2_re, -wave_col * f1_re], axis=1
    )
    all_im = jnp.stack(
        [wave_col * f0_re, f1_re, -col_sq * f0_im, -f2_im, -wave_col * f1_im], axis=1
    )
    flat_re = all_re.reshape(HOPS * 5 * ray_dev, k_all * half)
    flat_im = all_im.reshape(HOPS * 5 * ray_dev, k_all * half)
    field_re, _ = rows_inverse(flat_re, flat_im, length, half)
    fields = field_re.reshape(HOPS, 5, ray_dev, length)
    for step_index in range(HOPS):
        ray_tile = lens_step(ray_tile, fields[step_index][None])
    return ray_tile


def solution(mesh):
    return jax.shard_map(
        per_device,
        mesh=mesh,
        in_specs=(
            P(("real", "los"), "sky", None),
            P(("real", "los")),
            P(("real", "los")),
            P(("real", "los"), None, "sky", None),
        ),
        out_specs=P(("real", "los"), None, "sky", None),
        check_vma=False,
    )
```

```python
import math

import jax
import jax.numpy as jnp
from jax import lax
from jax.sharding import PartitionSpec as P

HOPS = 4


two_pi = 2.0 * math.pi
highest = lax.Precision.HIGH
first_radix = 16


def shifted(block, axis, distance):
    devices = range(lax.axis_size(axis))
    route = [((i - distance) % len(devices), i) for i in devices]
    return lax.ppermute(block, axis, route)


def lens_step(ray_tile, fields):
    disp_x = ray_tile[..., 0, :, :]
    disp_y = ray_tile[..., 1, :, :]
    tilt_x = ray_tile[..., 2, :, :]
    tilt_y = ray_tile[..., 3, :, :]
    jac_xx = ray_tile[..., 4, :, :]
    jac_xy = ray_tile[..., 5, :, :]
    jac_yx = ray_tile[..., 6, :, :]
    jac_yy = ray_tile[..., 7, :, :]
    rate_xx = ray_tile[..., 8, :, :]
    rate_xy = ray_tile[..., 9, :, :]
    rate_yx = ray_tile[..., 10, :, :]
    rate_yy = ray_tile[..., 11, :, :]
    bend_x = fields[..., 0, :, :]
    bend_y = fields[..., 1, :, :]
    hess_xx = fields[..., 2, :, :]
    hess_yy = fields[..., 3, :, :]
    hess_xy = fields[..., 4, :, :]
    push_x = bend_x + hess_xx * disp_x + hess_xy * disp_y
    push_y = bend_y + hess_xy * disp_x + hess_yy * disp_y
    new_tilt_x = tilt_x - push_x
    new_tilt_y = tilt_y - push_y
    new_disp_x = disp_x + new_tilt_x
    new_disp_y = disp_y + new_tilt_y
    new_rate_xx = rate_xx - (hess_xx * jac_xx + hess_xy * jac_yx)
    new_rate_xy = rate_xy - (hess_xx * jac_xy + hess_xy * jac_yy)
    new_rate_yx = rate_yx - (hess_xy * jac_xx + hess_yy * jac_yx)
    new_rate_yy = rate_yy - (hess_xy * jac_xy + hess_yy * jac_yy)
    new_jac_xx = jac_xx + new_rate_xx
    new_jac_xy = jac_xy + new_rate_xy
    new_jac_yx = jac_yx + new_rate_yx
    new_jac_yy = jac_yy + new_rate_yy
    return jnp.stack(
        [
            new_disp_x,
            new_disp_y,
            new_tilt_x,
            new_tilt_y,
            new_jac_xx,
            new_jac_xy,
            new_jac_yx,
            new_jac_yy,
            new_rate_xx,
            new_rate_xy,
            new_rate_yx,
            new_rate_yy,
        ],
        axis=-3,
    )


def phase_table(left_idx, right_idx, modulus, orient):
    product = left_idx[:, None] * right_idx[None, :] % modulus
    angle = orient * two_pi / modulus * product.astype(jnp.float32)
    return (jnp.cos(angle), jnp.sin(angle))


def block_table(left_idx, right_idx, modulus, orient):
    t_re, t_im = phase_table(left_idx, right_idx, modulus, orient)
    top = jnp.concatenate([t_re, t_im], axis=1)
    bottom = jnp.concatenate([-t_im, t_re], axis=1)
    return jnp.concatenate([top, bottom], axis=0)


def mixed(form, left_op, right_op):
    return jnp.einsum(
        form, left_op, right_op, precision=highest, preferred_element_type=jnp.float32
    )


def complex_product(form, real_in, imag_in, table_re, table_im):
    if imag_in is None:
        return (mixed(form, real_in, table_re), mixed(form, real_in, table_im))
    out_re = mixed(form, real_in, table_re) - mixed(form, imag_in, table_im)
    out_im = mixed(form, real_in, table_im) + mixed(form, imag_in, table_re)
    return (out_re, out_im)


def first_factor_of(length):
    factor_one = 1
    while factor_one * factor_one < length and length % (factor_one * 2) == 0:
        factor_one = factor_one * 2
    return factor_one


def rows_forward(cells):
    row_count, length = cells.shape
    second = length // first_radix
    half = second // 2
    shaped = cells.reshape(row_count, first_radix, second)
    v_idx = jnp.arange(first_radix, dtype=jnp.int32)
    u_idx = jnp.arange(second, dtype=jnp.int32)
    m_idx = jnp.arange(half, dtype=jnp.int32)
    section_re, section_im = phase_table(v_idx, v_idx, first_radix, -1.0)
    section = jnp.concatenate([section_re, section_im], axis=1)
    part = mixed("rvu,vk->rku", shaped, section)
    part_re = part[:, :first_radix]
    part_im = part[:, first_radix:]
    twist_re, twist_im = phase_table(v_idx, u_idx, length, -1.0)
    turned_re = part_re * twist_re - part_im * twist_im
    turned_im = part_re * twist_im + part_im * twist_re
    turned = jnp.concatenate([turned_re, turned_im], axis=2)
    final = block_table(u_idx, m_idx, second, -1.0)
    return mixed("rkj,jn->rkn", turned, final)


def columns_forward(spread_re, spread_im):
    length, col_count = spread_re.shape
    factor_one = first_factor_of(length)
    second = length // factor_one
    first_idx = jnp.arange(factor_one, dtype=jnp.int32)
    second_idx = jnp.arange(second, dtype=jnp.int32)
    stacked = jnp.concatenate(
        [
            spread_re.reshape(factor_one, second * col_count),
            spread_im.reshape(factor_one, second * col_count),
        ],
        axis=0,
    )
    section = block_table(first_idx, first_idx, factor_one, -1.0)
    part = mixed("jn,jc->nc", section, stacked).reshape(2, factor_one, second, col_count)
    twist_re, twist_im = phase_table(first_idx, second_idx, length, -1.0)
    sign = jnp.array([-1.0, 1.0], jnp.float32)[:, None, None, None]
    turned = part * twist_re[None, :, :, None] + part[::-1] * (sign * twist_im[None, :, :, None])
    turned = jnp.transpose(turned, (1, 0, 2, 3)).reshape(factor_one, 2 * second, col_count)
    final = block_table(second_idx, second_idx, second, -1.0)
    done = mixed("kjc,jn->knc", turned, final)
    return done.reshape(factor_one, 2, second, col_count)


def rows_inverse(spec_re, spec_im, length, m_count):
    row_count = spec_re.shape[0]
    second = length // first_radix
    shaped_re = spec_re.reshape(row_count, first_radix, m_count)
    shaped_im = spec_im.reshape(row_count, first_radix, m_count)
    k_idx = jnp.arange(first_radix, dtype=jnp.int32)
    u_idx = jnp.arange(second, dtype=jnp.int32)
    m_idx = jnp.arange(m_count, dtype=jnp.int32)
    section_re, section_im = phase_table(m_idx, u_idx, second, 1.0)
    part_re, part_im = complex_product("rkm,mu->rku", shaped_re, shaped_im, section_re, section_im)
    twist_re, twist_im = phase_table(k_idx, u_idx, length, 1.0)
    turned_re = part_re * twist_re - part_im * twist_im
    turned_im = part_re * twist_im + part_im * twist_re
    final_re, final_im = phase_table(k_idx, k_idx, first_radix, 1.0)
    done_re, done_im = complex_product("rku,kv->rvu", turned_re, turned_im, final_re, final_im)
    return (done_re.reshape(row_count, length), done_im.reshape(row_count, length))


def wavenumbers(indices, length):
    signed = jnp.where(indices < length // 2, indices, indices - length)
    return (two_pi / length * signed.astype(jnp.float32), indices != length // 2)


def folded_spectra(spectrum, col_idx, ray_all):
    k_count, _, m_count, col_count = spectrum.shape
    length = k_count * m_count
    norm_factor = float(length * length)
    wave_col, retain_col = wavenumbers(col_idx, length)
    weight = jnp.where(col_idx == 0, 1.0, 2.0).astype(jnp.float32)
    row_idx = (
        jnp.arange(k_count, dtype=jnp.int32)[:, None]
        + k_count * jnp.arange(m_count, dtype=jnp.int32)[None, :]
    )
    wave_row, retain_row = wavenumbers(row_idx, length)
    wave_row = wave_row[:, None, :, None]
    retain_row = retain_row[:, None, :, None]
    squared = wave_col * wave_col + wave_row * wave_row
    retain = retain_row & retain_col & (squared > 0.0)
    safe_sq = jnp.where(retain, squared, 1.0)
    kernel = jnp.where(retain, -2.0 / (safe_sq * norm_factor), 0.0) * weight
    phi = kernel * spectrum
    terms = jnp.stack([phi, wave_row * phi, (wave_row * wave_row) * phi])
    terms = terms.reshape(3, k_count // ray_all, ray_all, 2, m_count, col_count)
    return jnp.transpose(jnp.sum(terms, axis=(1, 4)), (0, 2, 1, 3))


def per_device(density, lens_weight, plane_count, ray_state):
    sky_count = lax.axis_size("sky")
    sky_index = lax.axis_index("sky")
    ray_split = ray_state.shape[1] // 2
    ray_first = shifted(ray_state[:, :ray_split], "los", HOPS)
    ray_second = shifted(ray_state[:, ray_split:], "los", HOPS)
    plane_cells = density[0]
    length = plane_cells.shape[1]
    second = length // first_radix
    half = second // 2
    ray_dev = ray_state.shape[2]
    ray_all = ray_dev * sky_count
    strength = lens_weight[0] * plane_count[0].astype(jnp.float32)
    rows = rows_forward(plane_cells)
    ray_first, rows = lax.optimization_barrier((ray_first, rows))
    spread = lax.all_to_all(rows, "sky", split_axis=1, concat_axis=0, tiled=True)
    k_local = spread.shape[1]
    spread_re = spread[:, :, :half].reshape(length, k_local * half)
    spread_im = spread[:, :, half:].reshape(length, k_local * half)
    spectrum = columns_forward(spread_re, spread_im)
    ray_second, spectrum = lax.optimization_barrier((ray_second, spectrum))
    position = jnp.arange(k_local * half, dtype=jnp.int32)
    col_idx = sky_index * k_local + position // half + first_radix * (position % half)
    folds = folded_spectra(spectrum, col_idx, ray_all)
    q_idx = jnp.arange(ray_all, dtype=jnp.int32)
    back = block_table(q_idx, q_idx, ray_all, 1.0)
    at_rows = mixed("pjc,jn->pnc", folds.reshape(3, 2 * ray_all, k_local * half), back)
    at_rows = at_rows.reshape(3, 2, ray_all, k_local, half)
    returned = lax.all_to_all(at_rows, "sky", split_axis=2, concat_axis=3, tiled=True)
    k_all = returned.shape[3]
    dense = returned.reshape(3 * 2 * ray_dev, k_all * half) * strength
    arrived = jnp.stack(
        [shifted(dense, "los", HOPS - step_index) for step_index in range(HOPS)]
    ).reshape(HOPS, 3, 2, ray_dev, k_all, half)
    kx_idx = jnp.arange(k_all, dtype=jnp.int32)[:, None] + first_radix * jnp.arange(
        half, dtype=jnp.int32
    )[None, :]
    wave_col = wavenumbers(kx_idx, length)[0]
    f0_re, f0_im = arrived[:, 0, 0], arrived[:, 0, 1]
    f1_re, f1_im = arrived[:, 1, 0], arrived[:, 1, 1]
    f2_re, f2_im = arrived[:, 2, 0], arrived[:, 2, 1]
    col_sq = wave_col * wave_col
    all_re = jnp.stack(
        [-wave_col * f0_im, -f1_im, -col_sq * f0_re, -f2_re, -wave_col * f1_re], axis=1
    )
    all_im = jnp.stack(
        [wave_col * f0_re, f1_re, -col_sq * f0_im, -f2_im, -wave_col * f1_im], axis=1
    )
    flat_re = all_re.reshape(HOPS * 5 * ray_dev, k_all * half)
    flat_im = all_im.reshape(HOPS * 5 * ray_dev, k_all * half)
    field_re, _ = rows_inverse(flat_re, flat_im, length, half)
    fields = field_re.reshape(HOPS, 5, ray_dev, length)
    ray_tile = jnp.concatenate([ray_first, ray_second], axis=1)
    for step_index in range(HOPS):
        ray_tile = lens_step(ray_tile, fields[step_index][None])
    return ray_tile


def solution(mesh):
    return jax.shard_map(
        per_device,
        mesh=mesh,
        in_specs=(
            P(("real", "los"), "sky", None),
            P(("real", "los")),
            P(("real", "los")),
            P(("real", "los"), None, "sky", None),
        ),
        out_specs=P(("real", "los"), None, "sky", None),
        check_vma=False,
    )
```

```python
import math

import jax
import jax.numpy as jnp
from jax import lax
from jax.sharding import PartitionSpec as P

HOPS = 4


two_pi = 2.0 * math.pi
highest = lax.Precision.HIGH
first_radix = 16


def shifted(block, axis, distance):
    devices = range(lax.axis_size(axis))
    route = [((i - distance) % len(devices), i) for i in devices]
    return lax.ppermute(block, axis, route)


def lens_step(ray_tile, fields):
    disp_x = ray_tile[..., 0, :, :]
    disp_y = ray_tile[..., 1, :, :]
    tilt_x = ray_tile[..., 2, :, :]
    tilt_y = ray_tile[..., 3, :, :]
    jac_xx = ray_tile[..., 4, :, :]
    jac_xy = ray_tile[..., 5, :, :]
    jac_yx = ray_tile[..., 6, :, :]
    jac_yy = ray_tile[..., 7, :, :]
    rate_xx = ray_tile[..., 8, :, :]
    rate_xy = ray_tile[..., 9, :, :]
    rate_yx = ray_tile[..., 10, :, :]
    rate_yy = ray_tile[..., 11, :, :]
    bend_x = fields[..., 0, :, :]
    bend_y = fields[..., 1, :, :]
    hess_xx = fields[..., 2, :, :]
    hess_yy = fields[..., 3, :, :]
    hess_xy = fields[..., 4, :, :]
    push_x = bend_x + hess_xx * disp_x + hess_xy * disp_y
    push_y = bend_y + hess_xy * disp_x + hess_yy * disp_y
    new_tilt_x = tilt_x - push_x
    new_tilt_y = tilt_y - push_y
    new_disp_x = disp_x + new_tilt_x
    new_disp_y = disp_y + new_tilt_y
    new_rate_xx = rate_xx - (hess_xx * jac_xx + hess_xy * jac_yx)
    new_rate_xy = rate_xy - (hess_xx * jac_xy + hess_xy * jac_yy)
    new_rate_yx = rate_yx - (hess_xy * jac_xx + hess_yy * jac_yx)
    new_rate_yy = rate_yy - (hess_xy * jac_xy + hess_yy * jac_yy)
    new_jac_xx = jac_xx + new_rate_xx
    new_jac_xy = jac_xy + new_rate_xy
    new_jac_yx = jac_yx + new_rate_yx
    new_jac_yy = jac_yy + new_rate_yy
    return jnp.stack(
        [
            new_disp_x,
            new_disp_y,
            new_tilt_x,
            new_tilt_y,
            new_jac_xx,
            new_jac_xy,
            new_jac_yx,
            new_jac_yy,
            new_rate_xx,
            new_rate_xy,
            new_rate_yx,
            new_rate_yy,
        ],
        axis=-3,
    )


def phase_table(left_idx, right_idx, modulus, orient):
    product = left_idx[:, None] * right_idx[None, :] % modulus
    angle = orient * two_pi / modulus * product.astype(jnp.float32)
    return (jnp.cos(angle), jnp.sin(angle))


def block_table(left_idx, right_idx, modulus, orient):
    t_re, t_im = phase_table(left_idx, right_idx, modulus, orient)
    top = jnp.concatenate([t_re, t_im], axis=1)
    bottom = jnp.concatenate([-t_im, t_re], axis=1)
    return jnp.concatenate([top, bottom], axis=0)


def mixed(form, left_op, right_op):
    return jnp.einsum(
        form, left_op, right_op, precision=highest, preferred_element_type=jnp.float32
    )


def complex_product(form, real_in, imag_in, table_re, table_im):
    if imag_in is None:
        return (mixed(form, real_in, table_re), mixed(form, real_in, table_im))
    out_re = mixed(form, real_in, table_re) - mixed(form, imag_in, table_im)
    out_im = mixed(form, real_in, table_im) + mixed(form, imag_in, table_re)
    return (out_re, out_im)


def first_factor_of(length):
    factor_one = 1
    while factor_one * factor_one < length and length % (factor_one * 2) == 0:
        factor_one = factor_one * 2
    return factor_one


def rows_forward(cells):
    row_count, length = cells.shape
    second = length // first_radix
    half = second // 2
    shaped = cells.reshape(row_count, first_radix, second)
    v_idx = jnp.arange(first_radix, dtype=jnp.int32)
    u_idx = jnp.arange(second, dtype=jnp.int32)
    m_idx = jnp.arange(half, dtype=jnp.int32)
    section_re, section_im = phase_table(v_idx, v_idx, first_radix, -1.0)
    section = jnp.concatenate([section_re, section_im], axis=1)
    part = mixed("rvu,vk->rku", shaped, section)
    part_re = part[:, :first_radix]
    part_im = part[:, first_radix:]
    twist_re, twist_im = phase_table(v_idx, u_idx, length, -1.0)
    turned_re = part_re * twist_re - part_im * twist_im
    turned_im = part_re * twist_im + part_im * twist_re
    turned = jnp.concatenate([turned_re, turned_im], axis=2)
    final = block_table(u_idx, m_idx, second, -1.0)
    return mixed("rkj,jn->rkn", turned, final)


def columns_forward(spread_re, spread_im):
    length, col_count = spread_re.shape
    factor_one = first_factor_of(length)
    second = length // factor_one
    first_idx = jnp.arange(factor_one, dtype=jnp.int32)
    second_idx = jnp.arange(second, dtype=jnp.int32)
    stacked = jnp.concatenate(
        [
            spread_re.reshape(factor_one, second * col_count),
            spread_im.reshape(factor_one, second * col_count),
        ],
        axis=0,
    )
    section = block_table(first_idx, first_idx, factor_one, -1.0)
    part = mixed("jn,jc->nc", section, stacked).reshape(2, factor_one, second, col_count)
    twist_re, twist_im = phase_table(first_idx, second_idx, length, -1.0)
    twist_re = twist_re[:, :, None]
    twist_im = twist_im[:, :, None]
    turned_re = part[0] * twist_re - part[1] * twist_im
    turned_im = part[0] * twist_im + part[1] * twist_re
    turned = jnp.stack([turned_re, turned_im], axis=1).reshape(
        factor_one, 2 * second, col_count
    )
    final = block_table(second_idx, second_idx, second, -1.0)
    done = mixed("kjc,jn->knc", turned, final)
    return done.reshape(factor_one, 2, second, col_count)


def rows_inverse(spec_re, spec_im, length, m_count):
    row_count = spec_re.shape[0]
    second = length // first_radix
    shaped_re = spec_re.reshape(row_count, first_radix, m_count)
    shaped_im = spec_im.reshape(row_count, first_radix, m_count)
    k_idx = jnp.arange(first_radix, dtype=jnp.int32)
    u_idx = jnp.arange(second, dtype=jnp.int32)
    m_idx = jnp.arange(m_count, dtype=jnp.int32)
    section_re, section_im = phase_table(m_idx, u_idx, second, 1.0)
    part_re, part_im = complex_product("rkm,mu->rku", shaped_re, shaped_im, section_re, section_im)
    twist_re, twist_im = phase_table(k_idx, u_idx, length, 1.0)
    turned_re = part_re * twist_re - part_im * twist_im
    turned_im = part_re * twist_im + part_im * twist_re
    final_re, final_im = phase_table(k_idx, k_idx, first_radix, 1.0)
    done_re, done_im = complex_product("rku,kv->rvu", turned_re, turned_im, final_re, final_im)
    return (done_re.reshape(row_count, length), done_im.reshape(row_count, length))


def wavenumbers(indices, length):
    signed = jnp.where(indices < length // 2, indices, indices - length)
    return (two_pi / length * signed.astype(jnp.float32), indices != length // 2)


def folded_spectra(spectrum, col_idx, ray_all):
    k_count, _, m_count, col_count = spectrum.shape
    length = k_count * m_count
    norm_factor = float(length * length)
    wave_col, retain_col = wavenumbers(col_idx, length)
    weight = jnp.where(col_idx == 0, 1.0, 2.0).astype(jnp.float32)
    row_idx = (
        jnp.arange(k_count, dtype=jnp.int32)[:, None]
        + k_count * jnp.arange(m_count, dtype=jnp.int32)[None, :]
    )
    wave_row, retain_row = wavenumbers(row_idx, length)
    wave_row = wave_row[:, None, :, None]
    retain_row = retain_row[:, None, :, None]
    squared = wave_col * wave_col + wave_row * wave_row
    retain = retain_row & retain_col & (squared > 0.0)
    safe_sq = jnp.where(retain, squared, 1.0)
    kernel = jnp.where(retain, -2.0 / (safe_sq * norm_factor), 0.0) * weight
    phi = kernel * spectrum
    terms = jnp.stack([phi, wave_row * phi, (wave_row * wave_row) * phi])
    terms = terms.reshape(3, k_count // ray_all, ray_all, 2, m_count, col_count)
    return jnp.transpose(jnp.sum(terms, axis=(1, 4)), (0, 2, 1, 3))


def per_device(density, lens_weight, plane_count, ray_state):
    sky_count = lax.axis_size("sky")
    sky_index = lax.axis_index("sky")
    ray_split = ray_state.shape[1] // 2
    ray_first = shifted(ray_state[:, :ray_split], "los", HOPS)
    ray_second = shifted(ray_state[:, ray_split:], "los", HOPS)
    plane_cells = density[0]
    length = plane_cells.shape[1]
    second = length // first_radix
    half = second // 2
    ray_dev = ray_state.shape[2]
    ray_all = ray_dev * sky_count
    strength = lens_weight[0] * plane_count[0].astype(jnp.float32)
    rows = rows_forward(plane_cells)
    ray_first, rows = lax.optimization_barrier((ray_first, rows))
    spread = lax.all_to_all(rows, "sky", split_axis=1, concat_axis=0, tiled=True)
    k_local = spread.shape[1]
    spread_re = spread[:, :, :half].reshape(length, k_local * half)
    spread_im = spread[:, :, half:].reshape(length, k_local * half)
    spectrum = columns_forward(spread_re, spread_im)
    ray_second, spectrum = lax.optimization_barrier((ray_second, spectrum))
    position = jnp.arange(k_local * half, dtype=jnp.int32)
    col_idx = sky_index * k_local + position // half + first_radix * (position % half)
    folds = folded_spectra(spectrum, col_idx, ray_all)
    q_idx = jnp.arange(ray_all, dtype=jnp.int32)
    back = block_table(q_idx, q_idx, ray_all, 1.0)
    at_rows = mixed("pjc,jn->pnc", folds.reshape(3, 2 * ray_all, k_local * half), back)
    at_rows = at_rows.reshape(3, 2, ray_all, k_local, half)
    returned = lax.all_to_all(at_rows, "sky", split_axis=2, concat_axis=3, tiled=True)
    k_all = returned.shape[3]
    dense = returned.reshape(3 * 2 * ray_dev, k_all * half) * strength
    arrived = jnp.stack(
        [shifted(dense, "los", HOPS - step_index) for step_index in range(HOPS)]
    ).reshape(HOPS, 3, 2, ray_dev, k_all, half)
    kx_idx = jnp.arange(k_all, dtype=jnp.int32)[:, None] + first_radix * jnp.arange(
        half, dtype=jnp.int32
    )[None, :]
    wave_col = wavenumbers(kx_idx, length)[0]
    f0_re, f0_im = arrived[:, 0, 0], arrived[:, 0, 1]
    f1_re, f1_im = arrived[:, 1, 0], arrived[:, 1, 1]
    f2_re, f2_im = arrived[:, 2, 0], arrived[:, 2, 1]
    col_sq = wave_col * wave_col
    all_re = jnp.stack(
        [-wave_col * f0_im, -f1_im, -col_sq * f0_re, -f2_re, -wave_col * f1_re], axis=1
    )
    all_im = jnp.stack(
        [wave_col * f0_re, f1_re, -col_sq * f0_im, -f2_im, -wave_col * f1_im], axis=1
    )
    flat_re = all_re.reshape(HOPS * 5 * ray_dev, k_all * half)
    flat_im = all_im.reshape(HOPS * 5 * ray_dev, k_all * half)
    field_re, _ = rows_inverse(flat_re, flat_im, length, half)
    fields = field_re.reshape(HOPS, 5, ray_dev, length)
    ray_tile = jnp.concatenate([ray_first, ray_second], axis=1)
    for step_index in range(HOPS):
        ray_tile = lens_step(ray_tile, fields[step_index][None])
    return ray_tile


def solution(mesh):
    return jax.shard_map(
        per_device,
        mesh=mesh,
        in_specs=(
            P(("real", "los"), "sky", None),
            P(("real", "los")),
            P(("real", "los")),
            P(("real", "los"), None, "sky", None),
        ),
        out_specs=P(("real", "los"), None, "sky", None),
        check_vma=False,
    )
```

```python
import math

import jax
import jax.numpy as jnp
from jax import lax
from jax.sharding import PartitionSpec as P

HOPS = 4


two_pi = 2.0 * math.pi
highest = lax.Precision.HIGH
first_radix = 16


def shifted(block, axis, distance):
    devices = range(lax.axis_size(axis))
    route = [((i - distance) % len(devices), i) for i in devices]
    return lax.ppermute(block, axis, route)


def lens_step(state, fields):
    disp_x, disp_y, tilt_x, tilt_y = state[0:4]
    jac_xx, jac_xy, jac_yx, jac_yy = state[4:8]
    rate_xx, rate_xy, rate_yx, rate_yy = state[8:12]
    bend_x, bend_y, hess_xx, hess_yy, hess_xy = fields
    push_x = bend_x + hess_xx * disp_x + hess_xy * disp_y
    push_y = bend_y + hess_xy * disp_x + hess_yy * disp_y
    new_tilt_x = tilt_x - push_x
    new_tilt_y = tilt_y - push_y
    new_disp_x = disp_x + new_tilt_x
    new_disp_y = disp_y + new_tilt_y
    new_rate_xx = rate_xx - (hess_xx * jac_xx + hess_xy * jac_yx)
    new_rate_xy = rate_xy - (hess_xx * jac_xy + hess_xy * jac_yy)
    new_rate_yx = rate_yx - (hess_xy * jac_xx + hess_yy * jac_yx)
    new_rate_yy = rate_yy - (hess_xy * jac_xy + hess_yy * jac_yy)
    new_jac_xx = jac_xx + new_rate_xx
    new_jac_xy = jac_xy + new_rate_xy
    new_jac_yx = jac_yx + new_rate_yx
    new_jac_yy = jac_yy + new_rate_yy
    return [
        new_disp_x,
        new_disp_y,
        new_tilt_x,
        new_tilt_y,
        new_jac_xx,
        new_jac_xy,
        new_jac_yx,
        new_jac_yy,
        new_rate_xx,
        new_rate_xy,
        new_rate_yx,
        new_rate_yy,
    ]


def phase_table(left_idx, right_idx, modulus, orient):
    product = left_idx[:, None] * right_idx[None, :] % modulus
    angle = orient * two_pi / modulus * product.astype(jnp.float32)
    return (jnp.cos(angle), jnp.sin(angle))


def block_table(left_idx, right_idx, modulus, orient):
    t_re, t_im = phase_table(left_idx, right_idx, modulus, orient)
    top = jnp.concatenate([t_re, t_im], axis=1)
    bottom = jnp.concatenate([-t_im, t_re], axis=1)
    return jnp.concatenate([top, bottom], axis=0)


def mixed(form, left_op, right_op):
    return jnp.einsum(
        form, left_op, right_op, precision=highest, preferred_element_type=jnp.float32
    )


def complex_product(form, real_in, imag_in, table_re, table_im):
    if imag_in is None:
        return (mixed(form, real_in, table_re), mixed(form, real_in, table_im))
    out_re = mixed(form, real_in, table_re) - mixed(form, imag_in, table_im)
    out_im = mixed(form, real_in, table_im) + mixed(form, imag_in, table_re)
    return (out_re, out_im)


def first_factor_of(length):
    factor_one = 1
    while factor_one * factor_one < length and length % (factor_one * 2) == 0:
        factor_one = factor_one * 2
    return factor_one


def rows_forward(cells):
    row_count, length = cells.shape
    second = length // first_radix
    half = second // 2
    shaped = cells.reshape(row_count, first_radix, second)
    v_idx = jnp.arange(first_radix, dtype=jnp.int32)
    u_idx = jnp.arange(second, dtype=jnp.int32)
    m_idx = jnp.arange(half, dtype=jnp.int32)
    section_re, section_im = phase_table(v_idx, v_idx, first_radix, -1.0)
    section = jnp.concatenate([section_re, section_im], axis=1)
    part = mixed("rvu,vk->rku", shaped, section)
    part_re = part[:, :first_radix]
    part_im = part[:, first_radix:]
    twist_re, twist_im = phase_table(v_idx, u_idx, length, -1.0)
    turned_re = part_re * twist_re - part_im * twist_im
    turned_im = part_re * twist_im + part_im * twist_re
    turned = jnp.concatenate([turned_re, turned_im], axis=2)
    final = block_table(u_idx, m_idx, second, -1.0)
    return mixed("rkj,jn->rkn", turned, final)


def columns_forward(spread_re, spread_im):
    length, col_count = spread_re.shape
    factor_one = first_factor_of(length)
    second = length // factor_one
    first_idx = jnp.arange(factor_one, dtype=jnp.int32)
    second_idx = jnp.arange(second, dtype=jnp.int32)
    stacked = jnp.concatenate(
        [
            spread_re.reshape(factor_one, second * col_count),
            spread_im.reshape(factor_one, second * col_count),
        ],
        axis=0,
    )
    section = block_table(first_idx, first_idx, factor_one, -1.0)
    part = mixed("jn,jc->nc", section, stacked).reshape(2, factor_one, second, col_count)
    twist_re, twist_im = phase_table(first_idx, second_idx, length, -1.0)
    twist_re = twist_re[:, :, None]
    twist_im = twist_im[:, :, None]
    turned_re = part[0] * twist_re - part[1] * twist_im
    turned_im = part[0] * twist_im + part[1] * twist_re
    turned = jnp.stack([turned_re, turned_im], axis=1).reshape(
        factor_one, 2 * second, col_count
    )
    final = block_table(second_idx, second_idx, second, -1.0)
    done = mixed("kjc,jn->knc", turned, final)
    return done.reshape(factor_one, 2, second, col_count)


def rows_inverse(spec_re, spec_im, length, m_count):
    row_count = spec_re.shape[0]
    second = length // first_radix
    shaped_re = spec_re.reshape(row_count, first_radix, m_count)
    shaped_im = spec_im.reshape(row_count, first_radix, m_count)
    k_idx = jnp.arange(first_radix, dtype=jnp.int32)
    u_idx = jnp.arange(second, dtype=jnp.int32)
    m_idx = jnp.arange(m_count, dtype=jnp.int32)
    section_re, section_im = phase_table(m_idx, u_idx, second, 1.0)
    part_re, part_im = complex_product("rkm,mu->rku", shaped_re, shaped_im, section_re, section_im)
    twist_re, twist_im = phase_table(k_idx, u_idx, length, 1.0)
    turned_re = part_re * twist_re - part_im * twist_im
    turned_im = part_re * twist_im + part_im * twist_re
    final_re, final_im = phase_table(k_idx, k_idx, first_radix, 1.0)
    done_re, done_im = complex_product("rku,kv->rvu", turned_re, turned_im, final_re, final_im)
    return (done_re.reshape(row_count, length), done_im.reshape(row_count, length))


def wavenumbers(indices, length):
    signed = jnp.where(indices < length // 2, indices, indices - length)
    return (two_pi / length * signed.astype(jnp.float32), indices != length // 2)


def folded_spectra(spectrum, col_idx, ray_all):
    k_count, _, m_count, col_count = spectrum.shape
    length = k_count * m_count
    norm_factor = float(length * length)
    wave_col, retain_col = wavenumbers(col_idx, length)
    weight = jnp.where(col_idx == 0, 1.0, 2.0).astype(jnp.float32)
    row_idx = (
        jnp.arange(k_count, dtype=jnp.int32)[:, None]
        + k_count * jnp.arange(m_count, dtype=jnp.int32)[None, :]
    )
    wave_row, retain_row = wavenumbers(row_idx, length)
    wave_row = wave_row[:, None, :, None]
    retain_row = retain_row[:, None, :, None]
    squared = wave_col * wave_col + wave_row * wave_row
    retain = retain_row & retain_col & (squared > 0.0)
    safe_sq = jnp.where(retain, squared, 1.0)
    kernel = jnp.where(retain, -2.0 / (safe_sq * norm_factor), 0.0) * weight
    phi = kernel * spectrum
    terms = jnp.stack([phi, wave_row * phi, (wave_row * wave_row) * phi])
    terms = terms.reshape(3, k_count // ray_all, ray_all, 2, m_count, col_count)
    return jnp.transpose(jnp.sum(terms, axis=(1, 4)), (0, 2, 1, 3))


def per_device(density, lens_weight, plane_count, ray_state):
    sky_count = lax.axis_size("sky")
    sky_index = lax.axis_index("sky")
    ray_split = ray_state.shape[1] // 2
    ray_first = shifted(ray_state[:, :ray_split], "los", HOPS)
    ray_second = shifted(ray_state[:, ray_split:], "los", HOPS)
    plane_cells = density[0]
    length = plane_cells.shape[1]
    second = length // first_radix
    half = second // 2
    ray_dev = ray_state.shape[2]
    ray_all = ray_dev * sky_count
    strength = lens_weight[0] * plane_count[0].astype(jnp.float32)
    rows = rows_forward(plane_cells)
    ray_first, rows = lax.optimization_barrier((ray_first, rows))
    spread = lax.all_to_all(rows, "sky", split_axis=1, concat_axis=0, tiled=True)
    k_local = spread.shape[1]
    spread_re = spread[:, :, :half].reshape(length, k_local * half)
    spread_im = spread[:, :, half:].reshape(length, k_local * half)
    spectrum = columns_forward(spread_re, spread_im)
    ray_second, spectrum = lax.optimization_barrier((ray_second, spectrum))
    position = jnp.arange(k_local * half, dtype=jnp.int32)
    col_idx = sky_index * k_local + position // half + first_radix * (position % half)
    folds = folded_spectra(spectrum, col_idx, ray_all)
    q_idx = jnp.arange(ray_all, dtype=jnp.int32)
    back = block_table(q_idx, q_idx, ray_all, 1.0)
    at_rows = mixed("pjc,jn->pnc", folds.reshape(3, 2 * ray_all, k_local * half), back)
    at_rows = at_rows.reshape(3, 2, ray_all, k_local, half)
    returned = lax.all_to_all(at_rows, "sky", split_axis=2, concat_axis=3, tiled=True)
    k_all = returned.shape[3]
    dense = returned.reshape(3 * 2 * ray_dev, k_all * half) * strength
    arrived = jnp.stack(
        [shifted(dense, "los", HOPS - step_index) for step_index in range(HOPS)]
    ).reshape(HOPS, 3, 2, ray_dev, k_all, half)
    kx_idx = jnp.arange(k_all, dtype=jnp.int32)[:, None] + first_radix * jnp.arange(
        half, dtype=jnp.int32
    )[None, :]
    wave_col = wavenumbers(kx_idx, length)[0]
    f0_re, f0_im = arrived[:, 0, 0], arrived[:, 0, 1]
    f1_re, f1_im = arrived[:, 1, 0], arrived[:, 1, 1]
    f2_re, f2_im = arrived[:, 2, 0], arrived[:, 2, 1]
    col_sq = wave_col * wave_col
    all_re = jnp.stack(
        [-wave_col * f0_im, -f1_im, -col_sq * f0_re, -f2_re, -wave_col * f1_re], axis=1
    )
    all_im = jnp.stack(
        [wave_col * f0_re, f1_re, -col_sq * f0_im, -f2_im, -wave_col * f1_im], axis=1
    )
    flat_re = all_re.reshape(HOPS * 5 * ray_dev, k_all * half)
    flat_im = all_im.reshape(HOPS * 5 * ray_dev, k_all * half)
    field_re, _ = rows_inverse(flat_re, flat_im, length, half)
    fields = field_re.reshape(HOPS, 5, ray_dev, length)
    state = [ray_first[:, i] for i in range(ray_split)]
    state += [ray_second[:, i] for i in range(ray_state.shape[1] - ray_split)]
    for step_index in range(HOPS):
        lens = [fields[step_index][j][None] for j in range(5)]
        state = lens_step(state, lens)
    return jnp.stack(state, axis=1)


def solution(mesh):
    return jax.shard_map(
        per_device,
        mesh=mesh,
        in_specs=(
            P(("real", "los"), "sky", None),
            P(("real", "los")),
            P(("real", "los")),
            P(("real", "los"), None, "sky", None),
        ),
        out_specs=P(("real", "los"), None, "sky", None),
        check_vma=False,
    )
```

```python
import math

import jax
import jax.numpy as jnp
from jax import lax
from jax.sharding import PartitionSpec as P

HOPS = 4


two_pi = 2.0 * math.pi
highest = lax.Precision.HIGH
first_radix = 16


def shifted(block, axis, distance):
    devices = range(lax.axis_size(axis))
    route = [((i - distance) % len(devices), i) for i in devices]
    return lax.ppermute(block, axis, route)


def lens_step(ray_tile, fields):
    disp_x = ray_tile[..., 0, :, :]
    disp_y = ray_tile[..., 1, :, :]
    tilt_x = ray_tile[..., 2, :, :]
    tilt_y = ray_tile[..., 3, :, :]
    jac_xx = ray_tile[..., 4, :, :]
    jac_xy = ray_tile[..., 5, :, :]
    jac_yx = ray_tile[..., 6, :, :]
    jac_yy = ray_tile[..., 7, :, :]
    rate_xx = ray_tile[..., 8, :, :]
    rate_xy = ray_tile[..., 9, :, :]
    rate_yx = ray_tile[..., 10, :, :]
    rate_yy = ray_tile[..., 11, :, :]
    bend_x = fields[..., 0, :, :]
    bend_y = fields[..., 1, :, :]
    hess_xx = fields[..., 2, :, :]
    hess_yy = fields[..., 3, :, :]
    hess_xy = fields[..., 4, :, :]
    push_x = bend_x + hess_xx * disp_x + hess_xy * disp_y
    push_y = bend_y + hess_xy * disp_x + hess_yy * disp_y
    new_tilt_x = tilt_x - push_x
    new_tilt_y = tilt_y - push_y
    new_disp_x = disp_x + new_tilt_x
    new_disp_y = disp_y + new_tilt_y
    new_rate_xx = rate_xx - (hess_xx * jac_xx + hess_xy * jac_yx)
    new_rate_xy = rate_xy - (hess_xx * jac_xy + hess_xy * jac_yy)
    new_rate_yx = rate_yx - (hess_xy * jac_xx + hess_yy * jac_yx)
    new_rate_yy = rate_yy - (hess_xy * jac_xy + hess_yy * jac_yy)
    new_jac_xx = jac_xx + new_rate_xx
    new_jac_xy = jac_xy + new_rate_xy
    new_jac_yx = jac_yx + new_rate_yx
    new_jac_yy = jac_yy + new_rate_yy
    return jnp.stack(
        [
            new_disp_x,
            new_disp_y,
            new_tilt_x,
            new_tilt_y,
            new_jac_xx,
            new_jac_xy,
            new_jac_yx,
            new_jac_yy,
            new_rate_xx,
            new_rate_xy,
            new_rate_yx,
            new_rate_yy,
        ],
        axis=-3,
    )


def phase_table(left_idx, right_idx, modulus, orient):
    product = left_idx[:, None] * right_idx[None, :] % modulus
    angle = orient * two_pi / modulus * product.astype(jnp.float32)
    return (jnp.cos(angle), jnp.sin(angle))


def block_table(left_idx, right_idx, modulus, orient):
    t_re, t_im = phase_table(left_idx, right_idx, modulus, orient)
    top = jnp.concatenate([t_re, t_im], axis=1)
    bottom = jnp.concatenate([-t_im, t_re], axis=1)
    return jnp.concatenate([top, bottom], axis=0)


def mixed(form, left_op, right_op):
    return jnp.einsum(
        form, left_op, right_op, precision=highest, preferred_element_type=jnp.float32
    )


def complex_product(form, real_in, imag_in, table_re, table_im):
    if imag_in is None:
        return (mixed(form, real_in, table_re), mixed(form, real_in, table_im))
    out_re = mixed(form, real_in, table_re) - mixed(form, imag_in, table_im)
    out_im = mixed(form, real_in, table_im) + mixed(form, imag_in, table_re)
    return (out_re, out_im)


def first_factor_of(length):
    factor_one = 1
    while factor_one * factor_one < length and length % (factor_one * 2) == 0:
        factor_one = factor_one * 2
    return factor_one


def rows_forward(cells):
    row_count, length = cells.shape
    second = length // first_radix
    half = second // 2
    shaped = cells.reshape(row_count, first_radix, second)
    v_idx = jnp.arange(first_radix, dtype=jnp.int32)
    u_idx = jnp.arange(second, dtype=jnp.int32)
    m_idx = jnp.arange(half, dtype=jnp.int32)
    section_re, section_im = phase_table(v_idx, v_idx, first_radix, -1.0)
    section = jnp.concatenate([section_re, section_im], axis=1)
    part = mixed("rvu,vk->rku", shaped, section)
    part_re = part[:, :first_radix]
    part_im = part[:, first_radix:]
    twist_re, twist_im = phase_table(v_idx, u_idx, length, -1.0)
    turned_re = part_re * twist_re - part_im * twist_im
    turned_im = part_re * twist_im + part_im * twist_re
    final = block_table(u_idx, m_idx, second, -1.0)
    return mixed("rkj,jn->rkn", turned_re, final[:second]) + mixed(
        "rkj,jn->rkn", turned_im, final[second:]
    )


def columns_forward(spread_re, spread_im):
    length, col_count = spread_re.shape
    factor_one = first_factor_of(length)
    second = length // factor_one
    first_idx = jnp.arange(factor_one, dtype=jnp.int32)
    second_idx = jnp.arange(second, dtype=jnp.int32)
    section = block_table(first_idx, first_idx, factor_one, -1.0)
    part = mixed(
        "jn,jbc->nbc", section[:factor_one], spread_re.reshape(factor_one, second, col_count)
    ) + mixed(
        "jn,jbc->nbc", section[factor_one:], spread_im.reshape(factor_one, second, col_count)
    )
    part = part.reshape(2, factor_one, second, col_count)
    twist_re, twist_im = phase_table(first_idx, second_idx, length, -1.0)
    twist_re = twist_re[:, :, None]
    twist_im = twist_im[:, :, None]
    turned_re = part[0] * twist_re - part[1] * twist_im
    turned_im = part[0] * twist_im + part[1] * twist_re
    turned = jnp.stack([turned_re, turned_im], axis=1).reshape(
        factor_one, 2 * second, col_count
    )
    final = block_table(second_idx, second_idx, second, -1.0)
    done = mixed("kjc,jn->knc", turned, final)
    return done.reshape(factor_one, 2, second, col_count)


def rows_inverse(spec_re, spec_im, length, m_count):
    row_count = spec_re.shape[0]
    second = length // first_radix
    shaped_re = spec_re.reshape(row_count, first_radix, m_count)
    shaped_im = spec_im.reshape(row_count, first_radix, m_count)
    k_idx = jnp.arange(first_radix, dtype=jnp.int32)
    u_idx = jnp.arange(second, dtype=jnp.int32)
    m_idx = jnp.arange(m_count, dtype=jnp.int32)
    section_re, section_im = phase_table(m_idx, u_idx, second, 1.0)
    part_re, part_im = complex_product("rkm,mu->rku", shaped_re, shaped_im, section_re, section_im)
    twist_re, twist_im = phase_table(k_idx, u_idx, length, 1.0)
    turned_re = part_re * twist_re - part_im * twist_im
    turned_im = part_re * twist_im + part_im * twist_re
    final_re, final_im = phase_table(k_idx, k_idx, first_radix, 1.0)
    done_re, done_im = complex_product("rku,kv->rvu", turned_re, turned_im, final_re, final_im)
    return (done_re.reshape(row_count, length), done_im.reshape(row_count, length))


def wavenumbers(indices, length):
    signed = jnp.where(indices < length // 2, indices, indices - length)
    return (two_pi / length * signed.astype(jnp.float32), indices != length // 2)


def folded_spectra(spectrum, col_idx, ray_all):
    k_count, _, m_count, col_count = spectrum.shape
    length = k_count * m_count
    norm_factor = float(length * length)
    wave_col, retain_col = wavenumbers(col_idx, length)
    weight = jnp.where(col_idx == 0, 1.0, 2.0).astype(jnp.float32)
    row_idx = (
        jnp.arange(k_count, dtype=jnp.int32)[:, None]
        + k_count * jnp.arange(m_count, dtype=jnp.int32)[None, :]
    )
    wave_row, retain_row = wavenumbers(row_idx, length)
    wave_row = wave_row[:, None, :, None]
    retain_row = retain_row[:, None, :, None]
    squared = wave_col * wave_col + wave_row * wave_row
    retain = retain_row & retain_col & (squared > 0.0)
    safe_sq = jnp.where(retain, squared, 1.0)
    kernel = jnp.where(retain, -2.0 / (safe_sq * norm_factor), 0.0) * weight
    phi = kernel * spectrum
    terms = jnp.stack([phi, wave_row * phi, (wave_row * wave_row) * phi])
    terms = terms.reshape(3, k_count // ray_all, ray_all, 2, m_count, col_count)
    return jnp.transpose(jnp.sum(terms, axis=(1, 4)), (0, 2, 1, 3))


def per_device(density, lens_weight, plane_count, ray_state):
    sky_count = lax.axis_size("sky")
    sky_index = lax.axis_index("sky")
    ray_split = ray_state.shape[1] // 2
    ray_first = shifted(ray_state[:, :ray_split], "los", HOPS)
    ray_second = shifted(ray_state[:, ray_split:], "los", HOPS)
    plane_cells = density[0]
    length = plane_cells.shape[1]
    second = length // first_radix
    half = second // 2
    ray_dev = ray_state.shape[2]
    ray_all = ray_dev * sky_count
    strength = lens_weight[0] * plane_count[0].astype(jnp.float32)
    rows = rows_forward(plane_cells)
    ray_first, rows = lax.optimization_barrier((ray_first, rows))
    spread = lax.all_to_all(rows, "sky", split_axis=1, concat_axis=0, tiled=True)
    k_local = spread.shape[1]
    spread_re = spread[:, :, :half].reshape(length, k_local * half)
    spread_im = spread[:, :, half:].reshape(length, k_local * half)
    spectrum = columns_forward(spread_re, spread_im)
    ray_second, spectrum = lax.optimization_barrier((ray_second, spectrum))
    position = jnp.arange(k_local * half, dtype=jnp.int32)
    col_idx = sky_index * k_local + position // half + first_radix * (position % half)
    folds = folded_spectra(spectrum, col_idx, ray_all)
    q_idx = jnp.arange(ray_all, dtype=jnp.int32)
    back = block_table(q_idx, q_idx, ray_all, 1.0)
    at_rows = mixed("pjc,jn->pnc", folds.reshape(3, 2 * ray_all, k_local * half), back)
    at_rows = at_rows.reshape(3, 2, ray_all, k_local, half)
    returned = lax.all_to_all(at_rows, "sky", split_axis=2, concat_axis=3, tiled=True)
    k_all = returned.shape[3]
    dense = returned.reshape(3 * 2 * ray_dev, k_all * half) * strength
    arrived = jnp.stack(
        [shifted(dense, "los", HOPS - step_index) for step_index in range(HOPS)]
    ).reshape(HOPS, 3, 2, ray_dev, k_all, half)
    kx_idx = jnp.arange(k_all, dtype=jnp.int32)[:, None] + first_radix * jnp.arange(
        half, dtype=jnp.int32
    )[None, :]
    wave_col = wavenumbers(kx_idx, length)[0]
    f0_re, f0_im = arrived[:, 0, 0], arrived[:, 0, 1]
    f1_re, f1_im = arrived[:, 1, 0], arrived[:, 1, 1]
    f2_re, f2_im = arrived[:, 2, 0], arrived[:, 2, 1]
    col_sq = wave_col * wave_col
    all_re = jnp.stack(
        [-wave_col * f0_im, -f1_im, -col_sq * f0_re, -f2_re, -wave_col * f1_re], axis=1
    )
    all_im = jnp.stack(
        [wave_col * f0_re, f1_re, -col_sq * f0_im, -f2_im, -wave_col * f1_im], axis=1
    )
    flat_re = all_re.reshape(HOPS * 5 * ray_dev, k_all * half)
    flat_im = all_im.reshape(HOPS * 5 * ray_dev, k_all * half)
    field_re, _ = rows_inverse(flat_re, flat_im, length, half)
    fields = field_re.reshape(HOPS, 5, ray_dev, length)
    ray_tile = jnp.concatenate([ray_first, ray_second], axis=1)
    for step_index in range(HOPS):
        ray_tile = lens_step(ray_tile, fields[step_index][None])
    return ray_tile


def solution(mesh):
    return jax.shard_map(
        per_device,
        mesh=mesh,
        in_specs=(
            P(("real", "los"), "sky", None),
            P(("real", "los")),
            P(("real", "los")),
            P(("real", "los"), None, "sky", None),
        ),
        out_specs=P(("real", "los"), None, "sky", None),
        check_vma=False,
    )
```

```python
import math

import jax
import jax.numpy as jnp
from jax import lax
from jax.sharding import PartitionSpec as P

HOPS = 4


two_pi = 2.0 * math.pi
highest = lax.Precision.HIGH
first_radix = 16


def shifted(block, axis, distance):
    devices = range(lax.axis_size(axis))
    route = [((i - distance) % len(devices), i) for i in devices]
    return lax.ppermute(block, axis, route)


def lens_step(ray_tile, fields):
    disp_x = ray_tile[..., 0, :, :]
    disp_y = ray_tile[..., 1, :, :]
    tilt_x = ray_tile[..., 2, :, :]
    tilt_y = ray_tile[..., 3, :, :]
    jac_xx = ray_tile[..., 4, :, :]
    jac_xy = ray_tile[..., 5, :, :]
    jac_yx = ray_tile[..., 6, :, :]
    jac_yy = ray_tile[..., 7, :, :]
    rate_xx = ray_tile[..., 8, :, :]
    rate_xy = ray_tile[..., 9, :, :]
    rate_yx = ray_tile[..., 10, :, :]
    rate_yy = ray_tile[..., 11, :, :]
    bend_x = fields[..., 0, :, :]
    bend_y = fields[..., 1, :, :]
    hess_xx = fields[..., 2, :, :]
    hess_yy = fields[..., 3, :, :]
    hess_xy = fields[..., 4, :, :]
    push_x = bend_x + hess_xx * disp_x + hess_xy * disp_y
    push_y = bend_y + hess_xy * disp_x + hess_yy * disp_y
    new_tilt_x = tilt_x - push_x
    new_tilt_y = tilt_y - push_y
    new_disp_x = disp_x + new_tilt_x
    new_disp_y = disp_y + new_tilt_y
    new_rate_xx = rate_xx - (hess_xx * jac_xx + hess_xy * jac_yx)
    new_rate_xy = rate_xy - (hess_xx * jac_xy + hess_xy * jac_yy)
    new_rate_yx = rate_yx - (hess_xy * jac_xx + hess_yy * jac_yx)
    new_rate_yy = rate_yy - (hess_xy * jac_xy + hess_yy * jac_yy)
    new_jac_xx = jac_xx + new_rate_xx
    new_jac_xy = jac_xy + new_rate_xy
    new_jac_yx = jac_yx + new_rate_yx
    new_jac_yy = jac_yy + new_rate_yy
    return jnp.stack(
        [
            new_disp_x,
            new_disp_y,
            new_tilt_x,
            new_tilt_y,
            new_jac_xx,
            new_jac_xy,
            new_jac_yx,
            new_jac_yy,
            new_rate_xx,
            new_rate_xy,
            new_rate_yx,
            new_rate_yy,
        ],
        axis=-3,
    )


def phase_table(left_idx, right_idx, modulus, orient):
    product = left_idx[:, None] * right_idx[None, :] % modulus
    angle = orient * two_pi / modulus * product.astype(jnp.float32)
    return (jnp.cos(angle), jnp.sin(angle))


def block_table(left_idx, right_idx, modulus, orient):
    t_re, t_im = phase_table(left_idx, right_idx, modulus, orient)
    top = jnp.concatenate([t_re, t_im], axis=1)
    bottom = jnp.concatenate([-t_im, t_re], axis=1)
    return jnp.concatenate([top, bottom], axis=0)


def mixed(form, left_op, right_op):
    return jnp.einsum(
        form, left_op, right_op, precision=highest, preferred_element_type=jnp.float32
    )


def complex_product(form, real_in, imag_in, table_re, table_im):
    if imag_in is None:
        return (mixed(form, real_in, table_re), mixed(form, real_in, table_im))
    out_re = mixed(form, real_in, table_re) - mixed(form, imag_in, table_im)
    out_im = mixed(form, real_in, table_im) + mixed(form, imag_in, table_re)
    return (out_re, out_im)


def first_factor_of(length):
    factor_one = 1
    while factor_one * factor_one < length and length % (factor_one * 2) == 0:
        factor_one = factor_one * 2
    return factor_one


def rows_forward(cells):
    row_count, length = cells.shape
    second = length // first_radix
    half = second // 2
    shaped = cells.reshape(row_count, first_radix, second)
    v_idx = jnp.arange(first_radix, dtype=jnp.int32)
    u_idx = jnp.arange(second, dtype=jnp.int32)
    m_idx = jnp.arange(half, dtype=jnp.int32)
    section_re, section_im = phase_table(v_idx, v_idx, first_radix, -1.0)
    section = jnp.concatenate([section_re, section_im], axis=1)
    part = mixed("rvu,vk->rku", shaped, section)
    part_re = part[:, :first_radix]
    part_im = part[:, first_radix:]
    twist_re, twist_im = phase_table(v_idx, u_idx, length, -1.0)
    turned_re = part_re * twist_re - part_im * twist_im
    turned_im = part_re * twist_im + part_im * twist_re
    final = block_table(u_idx, m_idx, second, -1.0)
    return mixed("rkj,jn->rkn", turned_re, final[:second]) + mixed(
        "rkj,jn->rkn", turned_im, final[second:]
    )


def columns_forward(spread_re, spread_im):
    length, col_count = spread_re.shape
    factor_one = first_factor_of(length)
    second = length // factor_one
    first_idx = jnp.arange(factor_one, dtype=jnp.int32)
    second_idx = jnp.arange(second, dtype=jnp.int32)
    section = block_table(first_idx, first_idx, factor_one, -1.0)
    part = mixed(
        "jn,jbc->nbc", section[:factor_one], spread_re.reshape(factor_one, second, col_count)
    ) + mixed(
        "jn,jbc->nbc", section[factor_one:], spread_im.reshape(factor_one, second, col_count)
    )
    part = part.reshape(2, factor_one, second, col_count)
    twist_re, twist_im = phase_table(first_idx, second_idx, length, -1.0)
    twist_re = twist_re[:, :, None]
    twist_im = twist_im[:, :, None]
    turned_re = part[0] * twist_re - part[1] * twist_im
    turned_im = part[0] * twist_im + part[1] * twist_re
    final = block_table(second_idx, second_idx, second, -1.0)
    done = mixed("kjc,jn->knc", turned_re, final[:second]) + mixed(
        "kjc,jn->knc", turned_im, final[second:]
    )
    return done.reshape(factor_one, 2, second, col_count)


def rows_inverse(spec_re, spec_im, length, m_count):
    row_count = spec_re.shape[0]
    second = length // first_radix
    shaped_re = spec_re.reshape(row_count, first_radix, m_count)
    shaped_im = spec_im.reshape(row_count, first_radix, m_count)
    k_idx = jnp.arange(first_radix, dtype=jnp.int32)
    u_idx = jnp.arange(second, dtype=jnp.int32)
    m_idx = jnp.arange(m_count, dtype=jnp.int32)
    section_re, section_im = phase_table(m_idx, u_idx, second, 1.0)
    part_re, part_im = complex_product("rkm,mu->rku", shaped_re, shaped_im, section_re, section_im)
    twist_re, twist_im = phase_table(k_idx, u_idx, length, 1.0)
    turned_re = part_re * twist_re - part_im * twist_im
    turned_im = part_re * twist_im + part_im * twist_re
    final_re, final_im = phase_table(k_idx, k_idx, first_radix, 1.0)
    done_re, done_im = complex_product("rku,kv->rvu", turned_re, turned_im, final_re, final_im)
    return (done_re.reshape(row_count, length), done_im.reshape(row_count, length))


def wavenumbers(indices, length):
    signed = jnp.where(indices < length // 2, indices, indices - length)
    return (two_pi / length * signed.astype(jnp.float32), indices != length // 2)


def folded_spectra(spectrum, col_idx, ray_all):
    k_count, _, m_count, col_count = spectrum.shape
    length = k_count * m_count
    norm_factor = float(length * length)
    wave_col, retain_col = wavenumbers(col_idx, length)
    weight = jnp.where(col_idx == 0, 1.0, 2.0).astype(jnp.float32)
    row_idx = (
        jnp.arange(k_count, dtype=jnp.int32)[:, None]
        + k_count * jnp.arange(m_count, dtype=jnp.int32)[None, :]
    )
    wave_row, retain_row = wavenumbers(row_idx, length)
    wave_row = wave_row[:, None, :, None]
    retain_row = retain_row[:, None, :, None]
    squared = wave_col * wave_col + wave_row * wave_row
    retain = retain_row & retain_col & (squared > 0.0)
    safe_sq = jnp.where(retain, squared, 1.0)
    kernel = jnp.where(retain, -2.0 / (safe_sq * norm_factor), 0.0) * weight
    phi = kernel * spectrum
    terms = jnp.stack([phi, wave_row * phi, (wave_row * wave_row) * phi])
    terms = terms.reshape(3, k_count // ray_all, ray_all, 2, m_count, col_count)
    return jnp.transpose(jnp.sum(terms, axis=(1, 4)), (0, 2, 1, 3))


def per_device(density, lens_weight, plane_count, ray_state):
    sky_count = lax.axis_size("sky")
    sky_index = lax.axis_index("sky")
    ray_split = ray_state.shape[1] // 2
    ray_first = shifted(ray_state[:, :ray_split], "los", HOPS)
    ray_second = shifted(ray_state[:, ray_split:], "los", HOPS)
    plane_cells = density[0]
    length = plane_cells.shape[1]
    second = length // first_radix
    half = second // 2
    ray_dev = ray_state.shape[2]
    ray_all = ray_dev * sky_count
    strength = lens_weight[0] * plane_count[0].astype(jnp.float32)
    rows = rows_forward(plane_cells)
    ray_first, rows = lax.optimization_barrier((ray_first, rows))
    spread = lax.all_to_all(rows, "sky", split_axis=1, concat_axis=0, tiled=True)
    k_local = spread.shape[1]
    spread_re = spread[:, :, :half].reshape(length, k_local * half)
    spread_im = spread[:, :, half:].reshape(length, k_local * half)
    spectrum = columns_forward(spread_re, spread_im)
    ray_second, spectrum = lax.optimization_barrier((ray_second, spectrum))
    position = jnp.arange(k_local * half, dtype=jnp.int32)
    col_idx = sky_index * k_local + position // half + first_radix * (position % half)
    folds = folded_spectra(spectrum, col_idx, ray_all)
    q_idx = jnp.arange(ray_all, dtype=jnp.int32)
    back = block_table(q_idx, q_idx, ray_all, 1.0)
    at_rows = mixed("pjc,jn->pnc", folds.reshape(3, 2 * ray_all, k_local * half), back)
    at_rows = at_rows.reshape(3, 2, ray_all, k_local, half)
    returned = lax.all_to_all(at_rows, "sky", split_axis=2, concat_axis=3, tiled=True)
    k_all = returned.shape[3]
    dense = returned.reshape(3 * 2 * ray_dev, k_all * half) * strength
    arrived = jnp.stack(
        [shifted(dense, "los", HOPS - step_index) for step_index in range(HOPS)]
    ).reshape(HOPS, 3, 2, ray_dev, k_all, half)
    kx_idx = jnp.arange(k_all, dtype=jnp.int32)[:, None] + first_radix * jnp.arange(
        half, dtype=jnp.int32
    )[None, :]
    wave_col = wavenumbers(kx_idx, length)[0]
    f0_re, f0_im = arrived[:, 0, 0], arrived[:, 0, 1]
    f1_re, f1_im = arrived[:, 1, 0], arrived[:, 1, 1]
    f2_re, f2_im = arrived[:, 2, 0], arrived[:, 2, 1]
    col_sq = wave_col * wave_col
    all_re = jnp.stack(
        [-wave_col * f0_im, -f1_im, -col_sq * f0_re, -f2_re, -wave_col * f1_re], axis=1
    )
    all_im = jnp.stack(
        [wave_col * f0_re, f1_re, -col_sq * f0_im, -f2_im, -wave_col * f1_im], axis=1
    )
    flat_re = all_re.reshape(HOPS * 5 * ray_dev, k_all * half)
    flat_im = all_im.reshape(HOPS * 5 * ray_dev, k_all * half)
    field_re, _ = rows_inverse(flat_re, flat_im, length, half)
    fields = field_re.reshape(HOPS, 5, ray_dev, length)
    ray_tile = jnp.concatenate([ray_first, ray_second], axis=1)
    for step_index in range(HOPS):
        ray_tile = lens_step(ray_tile, fields[step_index][None])
    return ray_tile


def solution(mesh):
    return jax.shard_map(
        per_device,
        mesh=mesh,
        in_specs=(
            P(("real", "los"), "sky", None),
            P(("real", "los")),
            P(("real", "los")),
            P(("real", "los"), None, "sky", None),
        ),
        out_specs=P(("real", "los"), None, "sky", None),
        check_vma=False,
    )
```

```python
import math

import jax
import jax.numpy as jnp
from jax import lax
from jax.sharding import PartitionSpec as P

HOPS = 4


two_pi = 2.0 * math.pi
highest = lax.Precision.HIGH
first_radix = 16


def shifted(block, axis, distance):
    devices = range(lax.axis_size(axis))
    route = [((i - distance) % len(devices), i) for i in devices]
    return lax.ppermute(block, axis, route)


def lens_step(ray_tile, fields):
    disp_x = ray_tile[..., 0, :, :]
    disp_y = ray_tile[..., 1, :, :]
    tilt_x = ray_tile[..., 2, :, :]
    tilt_y = ray_tile[..., 3, :, :]
    jac_xx = ray_tile[..., 4, :, :]
    jac_xy = ray_tile[..., 5, :, :]
    jac_yx = ray_tile[..., 6, :, :]
    jac_yy = ray_tile[..., 7, :, :]
    rate_xx = ray_tile[..., 8, :, :]
    rate_xy = ray_tile[..., 9, :, :]
    rate_yx = ray_tile[..., 10, :, :]
    rate_yy = ray_tile[..., 11, :, :]
    bend_x = fields[..., 0, :, :]
    bend_y = fields[..., 1, :, :]
    hess_xx = fields[..., 2, :, :]
    hess_yy = fields[..., 3, :, :]
    hess_xy = fields[..., 4, :, :]
    push_x = bend_x + hess_xx * disp_x + hess_xy * disp_y
    push_y = bend_y + hess_xy * disp_x + hess_yy * disp_y
    new_tilt_x = tilt_x - push_x
    new_tilt_y = tilt_y - push_y
    new_disp_x = disp_x + new_tilt_x
    new_disp_y = disp_y + new_tilt_y
    new_rate_xx = rate_xx - (hess_xx * jac_xx + hess_xy * jac_yx)
    new_rate_xy = rate_xy - (hess_xx * jac_xy + hess_xy * jac_yy)
    new_rate_yx = rate_yx - (hess_xy * jac_xx + hess_yy * jac_yx)
    new_rate_yy = rate_yy - (hess_xy * jac_xy + hess_yy * jac_yy)
    new_jac_xx = jac_xx + new_rate_xx
    new_jac_xy = jac_xy + new_rate_xy
    new_jac_yx = jac_yx + new_rate_yx
    new_jac_yy = jac_yy + new_rate_yy
    return jnp.stack(
        [
            new_disp_x,
            new_disp_y,
            new_tilt_x,
            new_tilt_y,
            new_jac_xx,
            new_jac_xy,
            new_jac_yx,
            new_jac_yy,
            new_rate_xx,
            new_rate_xy,
            new_rate_yx,
            new_rate_yy,
        ],
        axis=-3,
    )


def phase_table(left_idx, right_idx, modulus, orient):
    product = left_idx[:, None] * right_idx[None, :] % modulus
    angle = orient * two_pi / modulus * product.astype(jnp.float32)
    return (jnp.cos(angle), jnp.sin(angle))


def block_table(left_idx, right_idx, modulus, orient):
    t_re, t_im = phase_table(left_idx, right_idx, modulus, orient)
    top = jnp.concatenate([t_re, t_im], axis=1)
    bottom = jnp.concatenate([-t_im, t_re], axis=1)
    return jnp.concatenate([top, bottom], axis=0)


def mixed(form, left_op, right_op):
    return jnp.einsum(
        form, left_op, right_op, precision=highest, preferred_element_type=jnp.float32
    )


def complex_product(form, real_in, imag_in, table_re, table_im):
    if imag_in is None:
        return (mixed(form, real_in, table_re), mixed(form, real_in, table_im))
    out_re = mixed(form, real_in, table_re) - mixed(form, imag_in, table_im)
    out_im = mixed(form, real_in, table_im) + mixed(form, imag_in, table_re)
    return (out_re, out_im)


def first_factor_of(length):
    factor_one = 1
    while factor_one * factor_one < length and length % (factor_one * 2) == 0:
        factor_one = factor_one * 2
    return factor_one


def rows_forward(cells):
    row_count, length = cells.shape
    second = length // first_radix
    half = second // 2
    shaped = cells.reshape(row_count, first_radix, second)
    v_idx = jnp.arange(first_radix, dtype=jnp.int32)
    u_idx = jnp.arange(second, dtype=jnp.int32)
    m_idx = jnp.arange(half, dtype=jnp.int32)
    section_re, section_im = phase_table(v_idx, v_idx, first_radix, -1.0)
    section = jnp.concatenate([section_re, section_im], axis=1)
    part = mixed("rvu,vk->rku", shaped, section)
    part_re = part[:, :first_radix]
    part_im = part[:, first_radix:]
    twist_re, twist_im = phase_table(v_idx, u_idx, length, -1.0)
    turned_re = part_re * twist_re - part_im * twist_im
    turned_im = part_re * twist_im + part_im * twist_re
    final = block_table(u_idx, m_idx, second, -1.0)
    return mixed("rkj,jn->rkn", turned_re, final[:second]) + mixed(
        "rkj,jn->rkn", turned_im, final[second:]
    )


def columns_forward(spread_re, spread_im):
    length, col_count = spread_re.shape
    factor_one = first_factor_of(length)
    second = length // factor_one
    first_idx = jnp.arange(factor_one, dtype=jnp.int32)
    second_idx = jnp.arange(second, dtype=jnp.int32)
    section = block_table(first_idx, first_idx, factor_one, -1.0)
    part = mixed(
        "jn,jbc->nbc", section[:factor_one], spread_re.reshape(factor_one, second, col_count)
    ) + mixed(
        "jn,jbc->nbc", section[factor_one:], spread_im.reshape(factor_one, second, col_count)
    )
    part = part.reshape(2, factor_one, second, col_count)
    twist_re, twist_im = phase_table(first_idx, second_idx, length, -1.0)
    twist_re = twist_re[:, :, None]
    twist_im = twist_im[:, :, None]
    turned_re = part[0] * twist_re - part[1] * twist_im
    turned_im = part[0] * twist_im + part[1] * twist_re
    turned = jnp.stack([turned_re, turned_im], axis=1).reshape(
        factor_one, 2 * second, col_count
    )
    final = block_table(second_idx, second_idx, second, -1.0)
    done = mixed("kjc,jn->knc", turned, final)
    return done.reshape(factor_one, 2, second, col_count)


def rows_inverse(spec_re, spec_im, length, m_count):
    row_count = spec_re.shape[0]
    second = length // first_radix
    shaped_re = spec_re.reshape(row_count, first_radix, m_count)
    shaped_im = spec_im.reshape(row_count, first_radix, m_count)
    k_idx = jnp.arange(first_radix, dtype=jnp.int32)
    u_idx = jnp.arange(second, dtype=jnp.int32)
    m_idx = jnp.arange(m_count, dtype=jnp.int32)
    section_re, section_im = phase_table(m_idx, u_idx, second, 1.0)
    part_re, part_im = complex_product("rkm,mu->rku", shaped_re, shaped_im, section_re, section_im)
    twist_re, twist_im = phase_table(k_idx, u_idx, length, 1.0)
    turned_re = part_re * twist_re - part_im * twist_im
    turned_im = part_re * twist_im + part_im * twist_re
    final_re, final_im = phase_table(k_idx, k_idx, first_radix, 1.0)
    done_re, done_im = complex_product("rku,kv->rvu", turned_re, turned_im, final_re, final_im)
    return (done_re.reshape(row_count, length), done_im.reshape(row_count, length))


def wavenumbers(indices, length):
    signed = jnp.where(indices < length // 2, indices, indices - length)
    return (two_pi / length * signed.astype(jnp.float32), indices != length // 2)


def folded_spectra(spectrum, col_idx, ray_all):
    k_count, _, m_count, col_count = spectrum.shape
    length = k_count * m_count
    norm_factor = float(length * length)
    wave_col, retain_col = wavenumbers(col_idx, length)
    weight = jnp.where(col_idx == 0, 1.0, 2.0).astype(jnp.float32)
    row_idx = (
        jnp.arange(k_count, dtype=jnp.int32)[:, None]
        + k_count * jnp.arange(m_count, dtype=jnp.int32)[None, :]
    )
    wave_row, retain_row = wavenumbers(row_idx, length)
    wave_row = wave_row[:, None, :, None]
    retain_row = retain_row[:, None, :, None]
    squared = wave_col * wave_col + wave_row * wave_row
    retain = retain_row & retain_col & (squared > 0.0)
    safe_sq = jnp.where(retain, squared, 1.0)
    kernel = jnp.where(retain, -2.0 / (safe_sq * norm_factor), 0.0) * weight
    phi = kernel * spectrum
    terms = jnp.stack([phi, wave_row * phi, (wave_row * wave_row) * phi])
    terms = terms.reshape(3, k_count // ray_all, ray_all, 2, m_count, col_count)
    return jnp.transpose(jnp.sum(terms, axis=(1, 4)), (0, 2, 1, 3))


def per_device(density, lens_weight, plane_count, ray_state):
    sky_count = lax.axis_size("sky")
    sky_index = lax.axis_index("sky")
    ray_split = ray_state.shape[1] // 3
    ray_first = shifted(ray_state[:, :ray_split], "los", HOPS)
    ray_second = shifted(ray_state[:, ray_split:], "los", HOPS)
    plane_cells = density[0]
    length = plane_cells.shape[1]
    second = length // first_radix
    half = second // 2
    ray_dev = ray_state.shape[2]
    ray_all = ray_dev * sky_count
    strength = lens_weight[0] * plane_count[0].astype(jnp.float32)
    rows = rows_forward(plane_cells)
    ray_first, rows = lax.optimization_barrier((ray_first, rows))
    spread = lax.all_to_all(rows, "sky", split_axis=1, concat_axis=0, tiled=True)
    k_local = spread.shape[1]
    spread_re = spread[:, :, :half].reshape(length, k_local * half)
    spread_im = spread[:, :, half:].reshape(length, k_local * half)
    spectrum = columns_forward(spread_re, spread_im)
    ray_second, spectrum = lax.optimization_barrier((ray_second, spectrum))
    position = jnp.arange(k_local * half, dtype=jnp.int32)
    col_idx = sky_index * k_local + position // half + first_radix * (position % half)
    folds = folded_spectra(spectrum, col_idx, ray_all)
    q_idx = jnp.arange(ray_all, dtype=jnp.int32)
    back = block_table(q_idx, q_idx, ray_all, 1.0)
    at_rows = mixed("pjc,jn->pnc", folds.reshape(3, 2 * ray_all, k_local * half), back)
    at_rows = at_rows.reshape(3, 2, ray_all, k_local, half)
    returned = lax.all_to_all(at_rows, "sky", split_axis=2, concat_axis=3, tiled=True)
    k_all = returned.shape[3]
    dense = returned.reshape(3 * 2 * ray_dev, k_all * half) * strength
    arrived = jnp.stack(
        [shifted(dense, "los", HOPS - step_index) for step_index in range(HOPS)]
    ).reshape(HOPS, 3, 2, ray_dev, k_all, half)
    kx_idx = jnp.arange(k_all, dtype=jnp.int32)[:, None] + first_radix * jnp.arange(
        half, dtype=jnp.int32
    )[None, :]
    wave_col = wavenumbers(kx_idx, length)[0]
    f0_re, f0_im = arrived[:, 0, 0], arrived[:, 0, 1]
    f1_re, f1_im = arrived[:, 1, 0], arrived[:, 1, 1]
    f2_re, f2_im = arrived[:, 2, 0], arrived[:, 2, 1]
    col_sq = wave_col * wave_col
    all_re = jnp.stack(
        [-wave_col * f0_im, -f1_im, -col_sq * f0_re, -f2_re, -wave_col * f1_re], axis=1
    )
    all_im = jnp.stack(
        [wave_col * f0_re, f1_re, -col_sq * f0_im, -f2_im, -wave_col * f1_im], axis=1
    )
    flat_re = all_re.reshape(HOPS * 5 * ray_dev, k_all * half)
    flat_im = all_im.reshape(HOPS * 5 * ray_dev, k_all * half)
    field_re, _ = rows_inverse(flat_re, flat_im, length, half)
    fields = field_re.reshape(HOPS, 5, ray_dev, length)
    ray_tile = jnp.concatenate([ray_first, ray_second], axis=1)
    for step_index in range(HOPS):
        ray_tile = lens_step(ray_tile, fields[step_index][None])
    return ray_tile


def solution(mesh):
    return jax.shard_map(
        per_device,
        mesh=mesh,
        in_specs=(
            P(("real", "los"), "sky", None),
            P(("real", "los")),
            P(("real", "los")),
            P(("real", "los"), None, "sky", None),
        ),
        out_specs=P(("real", "los"), None, "sky", None),
        check_vma=False,
    )
```

```python
import math

import jax
import jax.numpy as jnp
from jax import lax
from jax.sharding import PartitionSpec as P

HOPS = 4


two_pi = 2.0 * math.pi
highest = lax.Precision.HIGH
first_radix = 16


def shifted(block, axis, distance):
    devices = range(lax.axis_size(axis))
    route = [((i - distance) % len(devices), i) for i in devices]
    return lax.ppermute(block, axis, route)


def lens_step(ray_tile, fields):
    disp_x = ray_tile[..., 0, :, :]
    disp_y = ray_tile[..., 1, :, :]
    tilt_x = ray_tile[..., 2, :, :]
    tilt_y = ray_tile[..., 3, :, :]
    jac_xx = ray_tile[..., 4, :, :]
    jac_xy = ray_tile[..., 5, :, :]
    jac_yx = ray_tile[..., 6, :, :]
    jac_yy = ray_tile[..., 7, :, :]
    rate_xx = ray_tile[..., 8, :, :]
    rate_xy = ray_tile[..., 9, :, :]
    rate_yx = ray_tile[..., 10, :, :]
    rate_yy = ray_tile[..., 11, :, :]
    bend_x = fields[..., 0, :, :]
    bend_y = fields[..., 1, :, :]
    hess_xx = fields[..., 2, :, :]
    hess_yy = fields[..., 3, :, :]
    hess_xy = fields[..., 4, :, :]
    push_x = bend_x + hess_xx * disp_x + hess_xy * disp_y
    push_y = bend_y + hess_xy * disp_x + hess_yy * disp_y
    new_tilt_x = tilt_x - push_x
    new_tilt_y = tilt_y - push_y
    new_disp_x = disp_x + new_tilt_x
    new_disp_y = disp_y + new_tilt_y
    new_rate_xx = rate_xx - (hess_xx * jac_xx + hess_xy * jac_yx)
    new_rate_xy = rate_xy - (hess_xx * jac_xy + hess_xy * jac_yy)
    new_rate_yx = rate_yx - (hess_xy * jac_xx + hess_yy * jac_yx)
    new_rate_yy = rate_yy - (hess_xy * jac_xy + hess_yy * jac_yy)
    new_jac_xx = jac_xx + new_rate_xx
    new_jac_xy = jac_xy + new_rate_xy
    new_jac_yx = jac_yx + new_rate_yx
    new_jac_yy = jac_yy + new_rate_yy
    return jnp.stack(
        [
            new_disp_x,
            new_disp_y,
            new_tilt_x,
            new_tilt_y,
            new_jac_xx,
            new_jac_xy,
            new_jac_yx,
            new_jac_yy,
            new_rate_xx,
            new_rate_xy,
            new_rate_yx,
            new_rate_yy,
        ],
        axis=-3,
    )


def phase_table(left_idx, right_idx, modulus, orient):
    product = left_idx[:, None] * right_idx[None, :] % modulus
    angle = orient * two_pi / modulus * product.astype(jnp.float32)
    return (jnp.cos(angle), jnp.sin(angle))


def block_table(left_idx, right_idx, modulus, orient):
    t_re, t_im = phase_table(left_idx, right_idx, modulus, orient)
    top = jnp.concatenate([t_re, t_im], axis=1)
    bottom = jnp.concatenate([-t_im, t_re], axis=1)
    return jnp.concatenate([top, bottom], axis=0)


def mixed(form, left_op, right_op):
    return jnp.einsum(
        form, left_op, right_op, precision=highest, preferred_element_type=jnp.float32
    )


def complex_product(form, real_in, imag_in, table_re, table_im):
    if imag_in is None:
        return (mixed(form, real_in, table_re), mixed(form, real_in, table_im))
    out_re = mixed(form, real_in, table_re) - mixed(form, imag_in, table_im)
    out_im = mixed(form, real_in, table_im) + mixed(form, imag_in, table_re)
    return (out_re, out_im)


def first_factor_of(length):
    factor_one = 1
    while factor_one * factor_one < length and length % (factor_one * 2) == 0:
        factor_one = factor_one * 2
    return factor_one


def rows_forward(cells):
    row_count, length = cells.shape
    second = length // first_radix
    half = second // 2
    shaped = cells.reshape(row_count, first_radix, second)
    v_idx = jnp.arange(first_radix, dtype=jnp.int32)
    u_idx = jnp.arange(second, dtype=jnp.int32)
    m_idx = jnp.arange(half, dtype=jnp.int32)
    section_re, section_im = phase_table(v_idx, v_idx, first_radix, -1.0)
    section = jnp.concatenate([section_re, section_im], axis=1)
    part = mixed("rvu,vk->rku", shaped, section)
    part_re = part[:, :first_radix]
    part_im = part[:, first_radix:]
    twist_re, twist_im = phase_table(v_idx, u_idx, length, -1.0)
    turned_re = part_re * twist_re - part_im * twist_im
    turned_im = part_re * twist_im + part_im * twist_re
    final = block_table(u_idx, m_idx, second, -1.0)
    return mixed("rkj,jn->rkn", turned_re, final[:second]) + mixed(
        "rkj,jn->rkn", turned_im, final[second:]
    )


def columns_forward(spread_re, spread_im):
    length, col_count = spread_re.shape
    factor_one = first_factor_of(length)
    second = length // factor_one
    first_idx = jnp.arange(factor_one, dtype=jnp.int32)
    second_idx = jnp.arange(second, dtype=jnp.int32)
    section = block_table(first_idx, first_idx, factor_one, -1.0)
    part = mixed(
        "jn,jbc->nbc", section[:factor_one], spread_re.reshape(factor_one, second, col_count)
    ) + mixed(
        "jn,jbc->nbc", section[factor_one:], spread_im.reshape(factor_one, second, col_count)
    )
    part = part.reshape(2, factor_one, second, col_count)
    twist_re, twist_im = phase_table(first_idx, second_idx, length, -1.0)
    twist_re = twist_re[:, :, None]
    twist_im = twist_im[:, :, None]
    turned_re = part[0] * twist_re - part[1] * twist_im
    turned_im = part[0] * twist_im + part[1] * twist_re
    turned = jnp.stack([turned_re, turned_im], axis=1).reshape(
        factor_one, 2 * second, col_count
    )
    final = block_table(second_idx, second_idx, second, -1.0)
    done = mixed("kjc,jn->knc", turned, final)
    return done.reshape(factor_one, 2, second, col_count)


def rows_inverse(spec_re, spec_im, length, m_count):
    row_count = spec_re.shape[0]
    second = length // first_radix
    shaped_re = spec_re.reshape(row_count, first_radix, m_count)
    shaped_im = spec_im.reshape(row_count, first_radix, m_count)
    k_idx = jnp.arange(first_radix, dtype=jnp.int32)
    u_idx = jnp.arange(second, dtype=jnp.int32)
    m_idx = jnp.arange(m_count, dtype=jnp.int32)
    section_re, section_im = phase_table(m_idx, u_idx, second, 1.0)
    part_re, part_im = complex_product("rkm,mu->rku", shaped_re, shaped_im, section_re, section_im)
    twist_re, twist_im = phase_table(k_idx, u_idx, length, 1.0)
    turned_re = part_re * twist_re - part_im * twist_im
    turned_im = part_re * twist_im + part_im * twist_re
    final_re, final_im = phase_table(k_idx, k_idx, first_radix, 1.0)
    done_re, done_im = complex_product("rku,kv->rvu", turned_re, turned_im, final_re, final_im)
    return (done_re.reshape(row_count, length), done_im.reshape(row_count, length))


def wavenumbers(indices, length):
    signed = jnp.where(indices < length // 2, indices, indices - length)
    return (two_pi / length * signed.astype(jnp.float32), indices != length // 2)


def folded_spectra(spectrum, col_idx, ray_all):
    k_count, _, m_count, col_count = spectrum.shape
    length = k_count * m_count
    norm_factor = float(length * length)
    wave_col, retain_col = wavenumbers(col_idx, length)
    weight = jnp.where(col_idx == 0, 1.0, 2.0).astype(jnp.float32)
    row_idx = (
        jnp.arange(k_count, dtype=jnp.int32)[:, None]
        + k_count * jnp.arange(m_count, dtype=jnp.int32)[None, :]
    )
    wave_row, retain_row = wavenumbers(row_idx, length)
    wave_row = wave_row[:, None, :, None]
    retain_row = retain_row[:, None, :, None]
    squared = wave_col * wave_col + wave_row * wave_row
    retain = retain_row & retain_col & (squared > 0.0)
    safe_sq = jnp.where(retain, squared, 1.0)
    kernel = jnp.where(retain, -2.0 / (safe_sq * norm_factor), 0.0) * weight
    shape = (k_count // ray_all, ray_all, 2, m_count, col_count)
    spread = spectrum.reshape(shape)
    sums = [
        jnp.sum((factor * kernel).reshape(shape[:2] + (1,) + shape[3:]) * spread, axis=(0, 3))
        for factor in (1.0, wave_row, wave_row * wave_row)
    ]
    return jnp.transpose(jnp.stack(sums), (0, 2, 1, 3))


def per_device(density, lens_weight, plane_count, ray_state):
    sky_count = lax.axis_size("sky")
    sky_index = lax.axis_index("sky")
    ray_split = ray_state.shape[1] // 3
    ray_first = shifted(ray_state[:, :ray_split], "los", HOPS)
    ray_second = shifted(ray_state[:, ray_split:], "los", HOPS)
    plane_cells = density[0]
    length = plane_cells.shape[1]
    second = length // first_radix
    half = second // 2
    ray_dev = ray_state.shape[2]
    ray_all = ray_dev * sky_count
    strength = lens_weight[0] * plane_count[0].astype(jnp.float32)
    rows = rows_forward(plane_cells)
    ray_first, rows = lax.optimization_barrier((ray_first, rows))
    spread = lax.all_to_all(rows, "sky", split_axis=1, concat_axis=0, tiled=True)
    k_local = spread.shape[1]
    spread_re = spread[:, :, :half].reshape(length, k_local * half)
    spread_im = spread[:, :, half:].reshape(length, k_local * half)
    spectrum = columns_forward(spread_re, spread_im)
    ray_second, spectrum = lax.optimization_barrier((ray_second, spectrum))
    position = jnp.arange(k_local * half, dtype=jnp.int32)
    col_idx = sky_index * k_local + position // half + first_radix * (position % half)
    folds = folded_spectra(spectrum, col_idx, ray_all)
    q_idx = jnp.arange(ray_all, dtype=jnp.int32)
    back = block_table(q_idx, q_idx, ray_all, 1.0)
    at_rows = mixed("pjc,jn->pnc", folds.reshape(3, 2 * ray_all, k_local * half), back)
    at_rows = at_rows.reshape(3, 2, ray_all, k_local, half)
    returned = lax.all_to_all(at_rows, "sky", split_axis=2, concat_axis=3, tiled=True)
    k_all = returned.shape[3]
    dense = returned.reshape(3 * 2 * ray_dev, k_all * half) * strength
    arrived = jnp.stack(
        [shifted(dense, "los", HOPS - step_index) for step_index in range(HOPS)]
    ).reshape(HOPS, 3, 2, ray_dev, k_all, half)
    kx_idx = jnp.arange(k_all, dtype=jnp.int32)[:, None] + first_radix * jnp.arange(
        half, dtype=jnp.int32
    )[None, :]
    wave_col = wavenumbers(kx_idx, length)[0]
    f0_re, f0_im = arrived[:, 0, 0], arrived[:, 0, 1]
    f1_re, f1_im = arrived[:, 1, 0], arrived[:, 1, 1]
    f2_re, f2_im = arrived[:, 2, 0], arrived[:, 2, 1]
    col_sq = wave_col * wave_col
    all_re = jnp.stack(
        [-wave_col * f0_im, -f1_im, -col_sq * f0_re, -f2_re, -wave_col * f1_re], axis=1
    )
    all_im = jnp.stack(
        [wave_col * f0_re, f1_re, -col_sq * f0_im, -f2_im, -wave_col * f1_im], axis=1
    )
    flat_re = all_re.reshape(HOPS * 5 * ray_dev, k_all * half)
    flat_im = all_im.reshape(HOPS * 5 * ray_dev, k_all * half)
    field_re, _ = rows_inverse(flat_re, flat_im, length, half)
    fields = field_re.reshape(HOPS, 5, ray_dev, length)
    ray_tile = jnp.concatenate([ray_first, ray_second], axis=1)
    for step_index in range(HOPS):
        ray_tile = lens_step(ray_tile, fields[step_index][None])
    return ray_tile


def solution(mesh):
    return jax.shard_map(
        per_device,
        mesh=mesh,
        in_specs=(
            P(("real", "los"), "sky", None),
            P(("real", "los")),
            P(("real", "los")),
            P(("real", "los"), None, "sky", None),
        ),
        out_specs=P(("real", "los"), None, "sky", None),
        check_vma=False,
    )
```

```python
import math

import jax
import jax.numpy as jnp
from jax import lax
from jax.sharding import PartitionSpec as P

HOPS = 4


two_pi = 2.0 * math.pi
highest = lax.Precision.HIGH
first_radix = 16


def shifted(block, axis, distance):
    devices = range(lax.axis_size(axis))
    route = [((i - distance) % len(devices), i) for i in devices]
    return lax.ppermute(block, axis, route)


def lens_step(ray_tile, fields):
    disp_x = ray_tile[..., 0, :, :]
    disp_y = ray_tile[..., 1, :, :]
    tilt_x = ray_tile[..., 2, :, :]
    tilt_y = ray_tile[..., 3, :, :]
    jac_xx = ray_tile[..., 4, :, :]
    jac_xy = ray_tile[..., 5, :, :]
    jac_yx = ray_tile[..., 6, :, :]
    jac_yy = ray_tile[..., 7, :, :]
    rate_xx = ray_tile[..., 8, :, :]
    rate_xy = ray_tile[..., 9, :, :]
    rate_yx = ray_tile[..., 10, :, :]
    rate_yy = ray_tile[..., 11, :, :]
    bend_x = fields[..., 0, :, :]
    bend_y = fields[..., 1, :, :]
    hess_xx = fields[..., 2, :, :]
    hess_yy = fields[..., 3, :, :]
    hess_xy = fields[..., 4, :, :]
    push_x = bend_x + hess_xx * disp_x + hess_xy * disp_y
    push_y = bend_y + hess_xy * disp_x + hess_yy * disp_y
    new_tilt_x = tilt_x - push_x
    new_tilt_y = tilt_y - push_y
    new_disp_x = disp_x + new_tilt_x
    new_disp_y = disp_y + new_tilt_y
    new_rate_xx = rate_xx - (hess_xx * jac_xx + hess_xy * jac_yx)
    new_rate_xy = rate_xy - (hess_xx * jac_xy + hess_xy * jac_yy)
    new_rate_yx = rate_yx - (hess_xy * jac_xx + hess_yy * jac_yx)
    new_rate_yy = rate_yy - (hess_xy * jac_xy + hess_yy * jac_yy)
    new_jac_xx = jac_xx + new_rate_xx
    new_jac_xy = jac_xy + new_rate_xy
    new_jac_yx = jac_yx + new_rate_yx
    new_jac_yy = jac_yy + new_rate_yy
    return jnp.stack(
        [
            new_disp_x,
            new_disp_y,
            new_tilt_x,
            new_tilt_y,
            new_jac_xx,
            new_jac_xy,
            new_jac_yx,
            new_jac_yy,
            new_rate_xx,
            new_rate_xy,
            new_rate_yx,
            new_rate_yy,
        ],
        axis=-3,
    )


def phase_table(left_idx, right_idx, modulus, orient):
    product = left_idx[:, None] * right_idx[None, :] % modulus
    angle = orient * two_pi / modulus * product.astype(jnp.float32)
    return (jnp.cos(angle), jnp.sin(angle))


def block_table(left_idx, right_idx, modulus, orient):
    t_re, t_im = phase_table(left_idx, right_idx, modulus, orient)
    top = jnp.concatenate([t_re, t_im], axis=1)
    bottom = jnp.concatenate([-t_im, t_re], axis=1)
    return jnp.concatenate([top, bottom], axis=0)


def mixed(form, left_op, right_op):
    return jnp.einsum(
        form, left_op, right_op, precision=highest, preferred_element_type=jnp.float32
    )


def complex_product(form, real_in, imag_in, table_re, table_im):
    if imag_in is None:
        return (mixed(form, real_in, table_re), mixed(form, real_in, table_im))
    out_re = mixed(form, real_in, table_re) - mixed(form, imag_in, table_im)
    out_im = mixed(form, real_in, table_im) + mixed(form, imag_in, table_re)
    return (out_re, out_im)


def first_factor_of(length):
    factor_one = 1
    while factor_one * factor_one < length and length % (factor_one * 2) == 0:
        factor_one = factor_one * 2
    return factor_one


def rows_forward(cells):
    row_count, length = cells.shape
    second = length // first_radix
    half = second // 2
    shaped = cells.reshape(row_count, first_radix, second)
    v_idx = jnp.arange(first_radix, dtype=jnp.int32)
    u_idx = jnp.arange(second, dtype=jnp.int32)
    m_idx = jnp.arange(half, dtype=jnp.int32)
    section_re, section_im = phase_table(v_idx, v_idx, first_radix, -1.0)
    part_re = mixed("rvu,vk->rku", shaped, section_re)
    part_im = mixed("rvu,vk->rku", shaped, section_im)
    twist_re, twist_im = phase_table(v_idx, u_idx, length, -1.0)
    turned_re = part_re * twist_re - part_im * twist_im
    turned_im = part_re * twist_im + part_im * twist_re
    final = block_table(u_idx, m_idx, second, -1.0)
    return mixed("rkj,jn->rkn", turned_re, final[:second]) + mixed(
        "rkj,jn->rkn", turned_im, final[second:]
    )


def columns_forward(spread_re, spread_im):
    length, col_count = spread_re.shape
    factor_one = first_factor_of(length)
    second = length // factor_one
    first_idx = jnp.arange(factor_one, dtype=jnp.int32)
    second_idx = jnp.arange(second, dtype=jnp.int32)
    section = block_table(first_idx, first_idx, factor_one, -1.0)
    part = mixed(
        "jn,jbc->nbc", section[:factor_one], spread_re.reshape(factor_one, second, col_count)
    ) + mixed(
        "jn,jbc->nbc", section[factor_one:], spread_im.reshape(factor_one, second, col_count)
    )
    part = part.reshape(2, factor_one, second, col_count)
    twist_re, twist_im = phase_table(first_idx, second_idx, length, -1.0)
    twist_re = twist_re[:, :, None]
    twist_im = twist_im[:, :, None]
    turned_re = part[0] * twist_re - part[1] * twist_im
    turned_im = part[0] * twist_im + part[1] * twist_re
    turned = jnp.stack([turned_re, turned_im], axis=1).reshape(
        factor_one, 2 * second, col_count
    )
    final = block_table(second_idx, second_idx, second, -1.0)
    done = mixed("kjc,jn->knc", turned, final)
    return done.reshape(factor_one, 2, second, col_count)


def rows_inverse(spec_re, spec_im, length, m_count):
    row_count = spec_re.shape[0]
    second = length // first_radix
    shaped_re = spec_re.reshape(row_count, first_radix, m_count)
    shaped_im = spec_im.reshape(row_count, first_radix, m_count)
    k_idx = jnp.arange(first_radix, dtype=jnp.int32)
    u_idx = jnp.arange(second, dtype=jnp.int32)
    m_idx = jnp.arange(m_count, dtype=jnp.int32)
    section_re, section_im = phase_table(m_idx, u_idx, second, 1.0)
    part_re, part_im = complex_product("rkm,mu->rku", shaped_re, shaped_im, section_re, section_im)
    twist_re, twist_im = phase_table(k_idx, u_idx, length, 1.0)
    turned_re = part_re * twist_re - part_im * twist_im
    turned_im = part_re * twist_im + part_im * twist_re
    final_re, final_im = phase_table(k_idx, k_idx, first_radix, 1.0)
    done_re, done_im = complex_product("rku,kv->rvu", turned_re, turned_im, final_re, final_im)
    return (done_re.reshape(row_count, length), done_im.reshape(row_count, length))


def wavenumbers(indices, length):
    signed = jnp.where(indices < length // 2, indices, indices - length)
    return (two_pi / length * signed.astype(jnp.float32), indices != length // 2)


def folded_spectra(spectrum, col_idx, ray_all):
    k_count, _, m_count, col_count = spectrum.shape
    length = k_count * m_count
    norm_factor = float(length * length)
    wave_col, retain_col = wavenumbers(col_idx, length)
    weight = jnp.where(col_idx == 0, 1.0, 2.0).astype(jnp.float32)
    row_idx = (
        jnp.arange(k_count, dtype=jnp.int32)[:, None]
        + k_count * jnp.arange(m_count, dtype=jnp.int32)[None, :]
    )
    wave_row, retain_row = wavenumbers(row_idx, length)
    wave_row = wave_row[:, None, :, None]
    retain_row = retain_row[:, None, :, None]
    squared = wave_col * wave_col + wave_row * wave_row
    retain = retain_row & retain_col & (squared > 0.0)
    safe_sq = jnp.where(retain, squared, 1.0)
    kernel = jnp.where(retain, -2.0 / (safe_sq * norm_factor), 0.0) * weight
    phi = kernel * spectrum
    terms = jnp.stack([phi, wave_row * phi, (wave_row * wave_row) * phi])
    terms = terms.reshape(3, k_count // ray_all, ray_all, 2, m_count, col_count)
    return jnp.transpose(jnp.sum(terms, axis=(1, 4)), (0, 2, 1, 3))


def per_device(density, lens_weight, plane_count, ray_state):
    sky_count = lax.axis_size("sky")
    sky_index = lax.axis_index("sky")
    ray_split = ray_state.shape[1] // 3
    ray_first = shifted(ray_state[:, :ray_split], "los", HOPS)
    ray_second = shifted(ray_state[:, ray_split:], "los", HOPS)
    plane_cells = density[0]
    length = plane_cells.shape[1]
    second = length // first_radix
    half = second // 2
    ray_dev = ray_state.shape[2]
    ray_all = ray_dev * sky_count
    strength = lens_weight[0] * plane_count[0].astype(jnp.float32)
    rows = rows_forward(plane_cells)
    ray_first, rows = lax.optimization_barrier((ray_first, rows))
    spread = lax.all_to_all(rows, "sky", split_axis=1, concat_axis=0, tiled=True)
    k_local = spread.shape[1]
    spread_re = spread[:, :, :half].reshape(length, k_local * half)
    spread_im = spread[:, :, half:].reshape(length, k_local * half)
    spectrum = columns_forward(spread_re, spread_im)
    ray_second, spectrum = lax.optimization_barrier((ray_second, spectrum))
    position = jnp.arange(k_local * half, dtype=jnp.int32)
    col_idx = sky_index * k_local + position // half + first_radix * (position % half)
    folds = folded_spectra(spectrum, col_idx, ray_all)
    q_idx = jnp.arange(ray_all, dtype=jnp.int32)
    back = block_table(q_idx, q_idx, ray_all, 1.0)
    at_rows = mixed("pjc,jn->pnc", folds.reshape(3, 2 * ray_all, k_local * half), back)
    at_rows = at_rows.reshape(3, 2, ray_all, k_local, half)
    returned = lax.all_to_all(at_rows, "sky", split_axis=2, concat_axis=3, tiled=True)
    k_all = returned.shape[3]
    dense = returned.reshape(3 * 2 * ray_dev, k_all * half) * strength
    arrived = jnp.stack(
        [shifted(dense, "los", HOPS - step_index) for step_index in range(HOPS)]
    ).reshape(HOPS, 3, 2, ray_dev, k_all, half)
    kx_idx = jnp.arange(k_all, dtype=jnp.int32)[:, None] + first_radix * jnp.arange(
        half, dtype=jnp.int32
    )[None, :]
    wave_col = wavenumbers(kx_idx, length)[0]
    f0_re, f0_im = arrived[:, 0, 0], arrived[:, 0, 1]
    f1_re, f1_im = arrived[:, 1, 0], arrived[:, 1, 1]
    f2_re, f2_im = arrived[:, 2, 0], arrived[:, 2, 1]
    col_sq = wave_col * wave_col
    all_re = jnp.stack(
        [-wave_col * f0_im, -f1_im, -col_sq * f0_re, -f2_re, -wave_col * f1_re], axis=1
    )
    all_im = jnp.stack(
        [wave_col * f0_re, f1_re, -col_sq * f0_im, -f2_im, -wave_col * f1_im], axis=1
    )
    flat_re = all_re.reshape(HOPS * 5 * ray_dev, k_all * half)
    flat_im = all_im.reshape(HOPS * 5 * ray_dev, k_all * half)
    field_re, _ = rows_inverse(flat_re, flat_im, length, half)
    fields = field_re.reshape(HOPS, 5, ray_dev, length)
    ray_tile = jnp.concatenate([ray_first, ray_second], axis=1)
    for step_index in range(HOPS):
        ray_tile = lens_step(ray_tile, fields[step_index][None])
    return ray_tile


def solution(mesh):
    return jax.shard_map(
        per_device,
        mesh=mesh,
        in_specs=(
            P(("real", "los"), "sky", None),
            P(("real", "los")),
            P(("real", "los")),
            P(("real", "los"), None, "sky", None),
        ),
        out_specs=P(("real", "los"), None, "sky", None),
        check_vma=False,
    )
```

```python
import math

import jax
import jax.numpy as jnp
from jax import lax
from jax.sharding import PartitionSpec as P

HOPS = 4


two_pi = 2.0 * math.pi
highest = lax.Precision.HIGH
first_radix = 16


def shifted(block, axis, distance):
    devices = range(lax.axis_size(axis))
    route = [((i - distance) % len(devices), i) for i in devices]
    return lax.ppermute(block, axis, route)


def lens_step(ray_tile, fields):
    disp_x = ray_tile[..., 0, :, :]
    disp_y = ray_tile[..., 1, :, :]
    tilt_x = ray_tile[..., 2, :, :]
    tilt_y = ray_tile[..., 3, :, :]
    jac_xx = ray_tile[..., 4, :, :]
    jac_xy = ray_tile[..., 5, :, :]
    jac_yx = ray_tile[..., 6, :, :]
    jac_yy = ray_tile[..., 7, :, :]
    rate_xx = ray_tile[..., 8, :, :]
    rate_xy = ray_tile[..., 9, :, :]
    rate_yx = ray_tile[..., 10, :, :]
    rate_yy = ray_tile[..., 11, :, :]
    bend_x = fields[..., 0, :, :]
    bend_y = fields[..., 1, :, :]
    hess_xx = fields[..., 2, :, :]
    hess_yy = fields[..., 3, :, :]
    hess_xy = fields[..., 4, :, :]
    push_x = bend_x + hess_xx * disp_x + hess_xy * disp_y
    push_y = bend_y + hess_xy * disp_x + hess_yy * disp_y
    new_tilt_x = tilt_x - push_x
    new_tilt_y = tilt_y - push_y
    new_disp_x = disp_x + new_tilt_x
    new_disp_y = disp_y + new_tilt_y
    new_rate_xx = rate_xx - (hess_xx * jac_xx + hess_xy * jac_yx)
    new_rate_xy = rate_xy - (hess_xx * jac_xy + hess_xy * jac_yy)
    new_rate_yx = rate_yx - (hess_xy * jac_xx + hess_yy * jac_yx)
    new_rate_yy = rate_yy - (hess_xy * jac_xy + hess_yy * jac_yy)
    new_jac_xx = jac_xx + new_rate_xx
    new_jac_xy = jac_xy + new_rate_xy
    new_jac_yx = jac_yx + new_rate_yx
    new_jac_yy = jac_yy + new_rate_yy
    return jnp.stack(
        [
            new_disp_x,
            new_disp_y,
            new_tilt_x,
            new_tilt_y,
            new_jac_xx,
            new_jac_xy,
            new_jac_yx,
            new_jac_yy,
            new_rate_xx,
            new_rate_xy,
            new_rate_yx,
            new_rate_yy,
        ],
        axis=-3,
    )


def phase_table(left_idx, right_idx, modulus, orient):
    product = left_idx[:, None] * right_idx[None, :] % modulus
    angle = orient * two_pi / modulus * product.astype(jnp.float32)
    return (jnp.cos(angle), jnp.sin(angle))


def block_table(left_idx, right_idx, modulus, orient):
    t_re, t_im = phase_table(left_idx, right_idx, modulus, orient)
    top = jnp.concatenate([t_re, t_im], axis=1)
    bottom = jnp.concatenate([-t_im, t_re], axis=1)
    return jnp.concatenate([top, bottom], axis=0)


def mixed(form, left_op, right_op):
    return jnp.einsum(
        form, left_op, right_op, precision=highest, preferred_element_type=jnp.float32
    )


def complex_product(form, real_in, imag_in, table_re, table_im):
    if imag_in is None:
        return (mixed(form, real_in, table_re), mixed(form, real_in, table_im))
    out_re = mixed(form, real_in, table_re) - mixed(form, imag_in, table_im)
    out_im = mixed(form, real_in, table_im) + mixed(form, imag_in, table_re)
    return (out_re, out_im)


def first_factor_of(length):
    factor_one = 1
    while factor_one * factor_one < length and length % (factor_one * 2) == 0:
        factor_one = factor_one * 2
    return factor_one


def rows_forward(cells):
    row_count, length = cells.shape
    second = length // first_radix
    half = second // 2
    shaped = cells.reshape(row_count, first_radix, second)
    v_idx = jnp.arange(first_radix, dtype=jnp.int32)
    u_idx = jnp.arange(second, dtype=jnp.int32)
    m_idx = jnp.arange(half, dtype=jnp.int32)
    section_re, section_im = phase_table(v_idx, v_idx, first_radix, -1.0)
    part_re = mixed("rvu,vk->rku", shaped, section_re)
    part_im = mixed("rvu,vk->rku", shaped, section_im)
    twist_re, twist_im = phase_table(v_idx, u_idx, length, -1.0)
    turned_re = part_re * twist_re - part_im * twist_im
    turned_im = part_re * twist_im + part_im * twist_re
    final = block_table(u_idx, m_idx, second, -1.0)
    return mixed("rkj,jn->rkn", turned_re, final[:second]) + mixed(
        "rkj,jn->rkn", turned_im, final[second:]
    )


def columns_forward(spread):
    length, k_local, width = spread.shape
    half = width // 2
    col_count = k_local * half
    factor_one = first_factor_of(length)
    second = length // factor_one
    first_idx = jnp.arange(factor_one, dtype=jnp.int32)
    second_idx = jnp.arange(second, dtype=jnp.int32)
    section_re, section_im = phase_table(first_idx, first_idx, factor_one, -1.0)
    shaped = spread.reshape(factor_one, second, k_local, width)
    cos_part = mixed("ja,jbcl->abcl", section_re, shaped)
    sin_part = mixed("ja,jbcl->abcl", section_im, shaped)
    part = [
        (cos_part[..., :half] - sin_part[..., half:]).reshape(factor_one, second, col_count),
        (cos_part[..., half:] + sin_part[..., :half]).reshape(factor_one, second, col_count),
    ]
    twist_re, twist_im = phase_table(first_idx, second_idx, length, -1.0)
    twist_re = twist_re[:, :, None]
    twist_im = twist_im[:, :, None]
    turned_re = part[0] * twist_re - part[1] * twist_im
    turned_im = part[0] * twist_im + part[1] * twist_re
    turned = jnp.stack([turned_re, turned_im], axis=1).reshape(
        factor_one, 2 * second, col_count
    )
    final = block_table(second_idx, second_idx, second, -1.0)
    done = mixed("kjc,jn->knc", turned, final)
    return done.reshape(factor_one, 2, second, col_count)


def rows_inverse(spec_re, spec_im, length, m_count):
    row_count = spec_re.shape[0]
    second = length // first_radix
    shaped_re = spec_re.reshape(row_count, first_radix, m_count)
    shaped_im = spec_im.reshape(row_count, first_radix, m_count)
    k_idx = jnp.arange(first_radix, dtype=jnp.int32)
    u_idx = jnp.arange(second, dtype=jnp.int32)
    m_idx = jnp.arange(m_count, dtype=jnp.int32)
    section_re, section_im = phase_table(m_idx, u_idx, second, 1.0)
    part_re, part_im = complex_product("rkm,mu->rku", shaped_re, shaped_im, section_re, section_im)
    twist_re, twist_im = phase_table(k_idx, u_idx, length, 1.0)
    turned_re = part_re * twist_re - part_im * twist_im
    turned_im = part_re * twist_im + part_im * twist_re
    final_re, final_im = phase_table(k_idx, k_idx, first_radix, 1.0)
    done_re, done_im = complex_product("rku,kv->rvu", turned_re, turned_im, final_re, final_im)
    return (done_re.reshape(row_count, length), done_im.reshape(row_count, length))


def wavenumbers(indices, length):
    signed = jnp.where(indices < length // 2, indices, indices - length)
    return (two_pi / length * signed.astype(jnp.float32), indices != length // 2)


def folded_spectra(spectrum, col_idx, ray_all):
    k_count, _, m_count, col_count = spectrum.shape
    length = k_count * m_count
    norm_factor = float(length * length)
    wave_col, retain_col = wavenumbers(col_idx, length)
    weight = jnp.where(col_idx == 0, 1.0, 2.0).astype(jnp.float32)
    row_idx = (
        jnp.arange(k_count, dtype=jnp.int32)[:, None]
        + k_count * jnp.arange(m_count, dtype=jnp.int32)[None, :]
    )
    wave_row, retain_row = wavenumbers(row_idx, length)
    wave_row = wave_row[:, None, :, None]
    retain_row = retain_row[:, None, :, None]
    squared = wave_col * wave_col + wave_row * wave_row
    retain = retain_row & retain_col & (squared > 0.0)
    safe_sq = jnp.where(retain, squared, 1.0)
    kernel = jnp.where(retain, -2.0 / (safe_sq * norm_factor), 0.0) * weight
    phi = kernel * spectrum
    terms = jnp.stack([phi, wave_row * phi, (wave_row * wave_row) * phi])
    terms = terms.reshape(3, k_count // ray_all, ray_all, 2, m_count, col_count)
    return jnp.transpose(jnp.sum(terms, axis=(1, 4)), (0, 2, 1, 3))


def per_device(density, lens_weight, plane_count, ray_state):
    sky_count = lax.axis_size("sky")
    sky_index = lax.axis_index("sky")
    ray_split = ray_state.shape[1] // 3
    ray_first = shifted(ray_state[:, :ray_split], "los", HOPS)
    ray_second = shifted(ray_state[:, ray_split:], "los", HOPS)
    plane_cells = density[0]
    length = plane_cells.shape[1]
    second = length // first_radix
    half = second // 2
    ray_dev = ray_state.shape[2]
    ray_all = ray_dev * sky_count
    strength = lens_weight[0] * plane_count[0].astype(jnp.float32)
    rows = rows_forward(plane_cells)
    ray_first, rows = lax.optimization_barrier((ray_first, rows))
    spread = lax.all_to_all(rows, "sky", split_axis=1, concat_axis=0, tiled=True)
    k_local = spread.shape[1]
    spectrum = columns_forward(spread)
    ray_second, spectrum = lax.optimization_barrier((ray_second, spectrum))
    position = jnp.arange(k_local * half, dtype=jnp.int32)
    col_idx = sky_index * k_local + position // half + first_radix * (position % half)
    folds = folded_spectra(spectrum, col_idx, ray_all)
    q_idx = jnp.arange(ray_all, dtype=jnp.int32)
    back = block_table(q_idx, q_idx, ray_all, 1.0)
    at_rows = mixed("pjc,jn->pnc", folds.reshape(3, 2 * ray_all, k_local * half), back)
    at_rows = at_rows.reshape(3, 2, ray_all, k_local, half)
    returned = lax.all_to_all(at_rows, "sky", split_axis=2, concat_axis=3, tiled=True)
    k_all = returned.shape[3]
    dense = returned.reshape(3 * 2 * ray_dev, k_all * half) * strength
    arrived = jnp.stack(
        [shifted(dense, "los", HOPS - step_index) for step_index in range(HOPS)]
    ).reshape(HOPS, 3, 2, ray_dev, k_all, half)
    kx_idx = jnp.arange(k_all, dtype=jnp.int32)[:, None] + first_radix * jnp.arange(
        half, dtype=jnp.int32
    )[None, :]
    wave_col = wavenumbers(kx_idx, length)[0]
    f0_re, f0_im = arrived[:, 0, 0], arrived[:, 0, 1]
    f1_re, f1_im = arrived[:, 1, 0], arrived[:, 1, 1]
    f2_re, f2_im = arrived[:, 2, 0], arrived[:, 2, 1]
    col_sq = wave_col * wave_col
    all_re = jnp.stack(
        [-wave_col * f0_im, -f1_im, -col_sq * f0_re, -f2_re, -wave_col * f1_re], axis=1
    )
    all_im = jnp.stack(
        [wave_col * f0_re, f1_re, -col_sq * f0_im, -f2_im, -wave_col * f1_im], axis=1
    )
    flat_re = all_re.reshape(HOPS * 5 * ray_dev, k_all * half)
    flat_im = all_im.reshape(HOPS * 5 * ray_dev, k_all * half)
    field_re, _ = rows_inverse(flat_re, flat_im, length, half)
    fields = field_re.reshape(HOPS, 5, ray_dev, length)
    ray_tile = jnp.concatenate([ray_first, ray_second], axis=1)
    for step_index in range(HOPS):
        ray_tile = lens_step(ray_tile, fields[step_index][None])
    return ray_tile


def solution(mesh):
    return jax.shard_map(
        per_device,
        mesh=mesh,
        in_specs=(
            P(("real", "los"), "sky", None),
            P(("real", "los")),
            P(("real", "los")),
            P(("real", "los"), None, "sky", None),
        ),
        out_specs=P(("real", "los"), None, "sky", None),
        check_vma=False,
    )
```

```python
import math

import jax
import jax.numpy as jnp
from jax import lax
from jax.sharding import PartitionSpec as P

HOPS = 4


two_pi = 2.0 * math.pi
highest = lax.Precision.HIGH
first_radix = 16


def shifted(block, axis, distance):
    devices = range(lax.axis_size(axis))
    route = [((i - distance) % len(devices), i) for i in devices]
    return lax.ppermute(block, axis, route)


def lens_step(ray_tile, fields):
    disp_x = ray_tile[..., 0, :, :]
    disp_y = ray_tile[..., 1, :, :]
    tilt_x = ray_tile[..., 2, :, :]
    tilt_y = ray_tile[..., 3, :, :]
    jac_xx = ray_tile[..., 4, :, :]
    jac_xy = ray_tile[..., 5, :, :]
    jac_yx = ray_tile[..., 6, :, :]
    jac_yy = ray_tile[..., 7, :, :]
    rate_xx = ray_tile[..., 8, :, :]
    rate_xy = ray_tile[..., 9, :, :]
    rate_yx = ray_tile[..., 10, :, :]
    rate_yy = ray_tile[..., 11, :, :]
    bend_x = fields[..., 0, :, :]
    bend_y = fields[..., 1, :, :]
    hess_xx = fields[..., 2, :, :]
    hess_yy = fields[..., 3, :, :]
    hess_xy = fields[..., 4, :, :]
    push_x = bend_x + hess_xx * disp_x + hess_xy * disp_y
    push_y = bend_y + hess_xy * disp_x + hess_yy * disp_y
    new_tilt_x = tilt_x - push_x
    new_tilt_y = tilt_y - push_y
    new_disp_x = disp_x + new_tilt_x
    new_disp_y = disp_y + new_tilt_y
    new_rate_xx = rate_xx - (hess_xx * jac_xx + hess_xy * jac_yx)
    new_rate_xy = rate_xy - (hess_xx * jac_xy + hess_xy * jac_yy)
    new_rate_yx = rate_yx - (hess_xy * jac_xx + hess_yy * jac_yx)
    new_rate_yy = rate_yy - (hess_xy * jac_xy + hess_yy * jac_yy)
    new_jac_xx = jac_xx + new_rate_xx
    new_jac_xy = jac_xy + new_rate_xy
    new_jac_yx = jac_yx + new_rate_yx
    new_jac_yy = jac_yy + new_rate_yy
    return jnp.stack(
        [
            new_disp_x,
            new_disp_y,
            new_tilt_x,
            new_tilt_y,
            new_jac_xx,
            new_jac_xy,
            new_jac_yx,
            new_jac_yy,
            new_rate_xx,
            new_rate_xy,
            new_rate_yx,
            new_rate_yy,
        ],
        axis=-3,
    )


def phase_table(left_idx, right_idx, modulus, orient):
    product = left_idx[:, None] * right_idx[None, :] % modulus
    angle = orient * two_pi / modulus * product.astype(jnp.float32)
    return (jnp.cos(angle), jnp.sin(angle))


def block_table(left_idx, right_idx, modulus, orient):
    t_re, t_im = phase_table(left_idx, right_idx, modulus, orient)
    top = jnp.concatenate([t_re, t_im], axis=1)
    bottom = jnp.concatenate([-t_im, t_re], axis=1)
    return jnp.concatenate([top, bottom], axis=0)


def mixed(form, left_op, right_op):
    return jnp.einsum(
        form, left_op, right_op, precision=highest, preferred_element_type=jnp.float32
    )


def complex_product(form, real_in, imag_in, table_re, table_im):
    if imag_in is None:
        return (mixed(form, real_in, table_re), mixed(form, real_in, table_im))
    out_re = mixed(form, real_in, table_re) - mixed(form, imag_in, table_im)
    out_im = mixed(form, real_in, table_im) + mixed(form, imag_in, table_re)
    return (out_re, out_im)


def first_factor_of(length):
    factor_one = 1
    while factor_one * factor_one < length and length % (factor_one * 2) == 0:
        factor_one = factor_one * 2
    return factor_one


def rows_forward(cells):
    row_count, length = cells.shape
    second = length // first_radix
    half = second // 2
    shaped = cells.reshape(row_count, first_radix, second)
    v_idx = jnp.arange(first_radix, dtype=jnp.int32)
    u_idx = jnp.arange(second, dtype=jnp.int32)
    m_idx = jnp.arange(half, dtype=jnp.int32)
    section_re, section_im = phase_table(v_idx, v_idx, first_radix, -1.0)
    part_re = mixed("rvu,vk->rku", shaped, section_re)
    part_im = mixed("rvu,vk->rku", shaped, section_im)
    twist_re, twist_im = phase_table(v_idx, u_idx, length, -1.0)
    turned_re = part_re * twist_re - part_im * twist_im
    turned_im = part_re * twist_im + part_im * twist_re
    final = block_table(u_idx, m_idx, second, -1.0)
    return mixed("rkj,jn->rkn", turned_re, final[:second]) + mixed(
        "rkj,jn->rkn", turned_im, final[second:]
    )


def columns_forward(spread_re, spread_im):
    length, col_count = spread_re.shape
    factor_one = first_factor_of(length)
    second = length // factor_one
    first_idx = jnp.arange(factor_one, dtype=jnp.int32)
    second_idx = jnp.arange(second, dtype=jnp.int32)
    section = block_table(first_idx, first_idx, factor_one, -1.0)
    part = mixed(
        "jn,jbc->nbc", section[:factor_one], spread_re.reshape(factor_one, second, col_count)
    ) + mixed(
        "jn,jbc->nbc", section[factor_one:], spread_im.reshape(factor_one, second, col_count)
    )
    part = part.reshape(2, factor_one, second, col_count)
    twist_re, twist_im = phase_table(first_idx, second_idx, length, -1.0)
    twist_re = twist_re[:, :, None]
    twist_im = twist_im[:, :, None]
    turned_re = part[0] * twist_re - part[1] * twist_im
    turned_im = part[0] * twist_im + part[1] * twist_re
    turned = jnp.stack([turned_re, turned_im], axis=1).reshape(
        factor_one, 2 * second, col_count
    )
    final = block_table(second_idx, second_idx, second, -1.0)
    done = mixed("kjc,jn->knc", turned, final)
    return done.reshape(factor_one, 2, second, col_count)


def rows_inverse(spec_re, spec_im, length, m_count):
    row_count = spec_re.shape[0]
    second = length // first_radix
    shaped_re = spec_re.reshape(row_count, first_radix, m_count)
    shaped_im = spec_im.reshape(row_count, first_radix, m_count)
    k_idx = jnp.arange(first_radix, dtype=jnp.int32)
    u_idx = jnp.arange(second, dtype=jnp.int32)
    m_idx = jnp.arange(m_count, dtype=jnp.int32)
    section_re, section_im = phase_table(m_idx, u_idx, second, 1.0)
    part_re, part_im = complex_product("rkm,mu->rku", shaped_re, shaped_im, section_re, section_im)
    twist_re, twist_im = phase_table(k_idx, u_idx, length, 1.0)
    turned_re = part_re * twist_re - part_im * twist_im
    turned_im = part_re * twist_im + part_im * twist_re
    final_re, final_im = phase_table(k_idx, k_idx, first_radix, 1.0)
    done_re, done_im = complex_product("rku,kv->rvu", turned_re, turned_im, final_re, final_im)
    return (done_re.reshape(row_count, length), done_im.reshape(row_count, length))


def wavenumbers(indices, length):
    signed = jnp.where(indices < length // 2, indices, indices - length)
    return (two_pi / length * signed.astype(jnp.float32), indices != length // 2)


def folded_spectra(spectrum, col_idx, ray_all):
    k_count, _, m_count, col_count = spectrum.shape
    length = k_count * m_count
    norm_factor = float(length * length)
    wave_col, retain_col = wavenumbers(col_idx, length)
    weight = jnp.where(col_idx == 0, 1.0, 2.0).astype(jnp.float32)
    row_idx = (
        jnp.arange(k_count, dtype=jnp.int32)[:, None]
        + k_count * jnp.arange(m_count, dtype=jnp.int32)[None, :]
    )
    wave_row, retain_row = wavenumbers(row_idx, length)
    wave_row = wave_row[:, None, :, None]
    retain_row = retain_row[:, None, :, None]
    squared = wave_col * wave_col + wave_row * wave_row
    retain = retain_row & retain_col & (squared > 0.0)
    safe_sq = jnp.where(retain, squared, 1.0)
    kernel = jnp.where(retain, -2.0 / (safe_sq * norm_factor), 0.0) * weight
    phi = kernel * spectrum
    terms = jnp.stack([phi, wave_row * phi, (wave_row * wave_row) * phi])
    terms = terms.reshape(3, k_count // ray_all, ray_all, 2, m_count, col_count)
    return jnp.transpose(jnp.sum(terms, axis=(1, 4)), (0, 2, 1, 3))


def per_device(density, lens_weight, plane_count, ray_state):
    sky_count = lax.axis_size("sky")
    sky_index = lax.axis_index("sky")
    ray_split = ray_state.shape[1] // 3
    ray_first = shifted(ray_state[:, :ray_split], "los", HOPS)
    ray_second = shifted(ray_state[:, ray_split:], "los", HOPS)
    plane_cells = density[0]
    length = plane_cells.shape[1]
    second = length // first_radix
    half = second // 2
    ray_dev = ray_state.shape[2]
    ray_all = ray_dev * sky_count
    strength = lens_weight[0] * plane_count[0].astype(jnp.float32)
    rows = rows_forward(plane_cells)
    ray_first, rows = lax.optimization_barrier((ray_first, rows))
    spread = lax.all_to_all(rows, "sky", split_axis=1, concat_axis=0, tiled=True)
    k_local = spread.shape[1]
    spread_re = spread[:, :, :half].reshape(length, k_local * half)
    spread_im = spread[:, :, half:].reshape(length, k_local * half)
    spectrum = columns_forward(spread_re, spread_im)
    ray_second, spectrum = lax.optimization_barrier((ray_second, spectrum))
    position = jnp.arange(k_local * half, dtype=jnp.int32)
    col_idx = sky_index * k_local + position // half + first_radix * (position % half)
    folds = folded_spectra(spectrum, col_idx, ray_all)
    q_idx = jnp.arange(ray_all, dtype=jnp.int32)
    back = block_table(q_idx, q_idx, ray_all, 1.0)
    at_rows = mixed("pjc,jn->pnc", folds[:, 0], back[:ray_all]) + mixed(
        "pjc,jn->pnc", folds[:, 1], back[ray_all:]
    )
    at_rows = at_rows.reshape(3, 2, ray_all, k_local, half)
    returned = lax.all_to_all(at_rows, "sky", split_axis=2, concat_axis=3, tiled=True)
    k_all = returned.shape[3]
    dense = returned.reshape(3 * 2 * ray_dev, k_all * half) * strength
    arrived = jnp.stack(
        [shifted(dense, "los", HOPS - step_index) for step_index in range(HOPS)]
    ).reshape(HOPS, 3, 2, ray_dev, k_all, half)
    kx_idx = jnp.arange(k_all, dtype=jnp.int32)[:, None] + first_radix * jnp.arange(
        half, dtype=jnp.int32
    )[None, :]
    wave_col = wavenumbers(kx_idx, length)[0]
    f0_re, f0_im = arrived[:, 0, 0], arrived[:, 0, 1]
    f1_re, f1_im = arrived[:, 1, 0], arrived[:, 1, 1]
    f2_re, f2_im = arrived[:, 2, 0], arrived[:, 2, 1]
    col_sq = wave_col * wave_col
    all_re = jnp.stack(
        [-wave_col * f0_im, -f1_im, -col_sq * f0_re, -f2_re, -wave_col * f1_re], axis=1
    )
    all_im = jnp.stack(
        [wave_col * f0_re, f1_re, -col_sq * f0_im, -f2_im, -wave_col * f1_im], axis=1
    )
    flat_re = all_re.reshape(HOPS * 5 * ray_dev, k_all * half)
    flat_im = all_im.reshape(HOPS * 5 * ray_dev, k_all * half)
    field_re, _ = rows_inverse(flat_re, flat_im, length, half)
    fields = field_re.reshape(HOPS, 5, ray_dev, length)
    ray_tile = jnp.concatenate([ray_first, ray_second], axis=1)
    for step_index in range(HOPS):
        ray_tile = lens_step(ray_tile, fields[step_index][None])
    return ray_tile


def solution(mesh):
    return jax.shard_map(
        per_device,
        mesh=mesh,
        in_specs=(
            P(("real", "los"), "sky", None),
            P(("real", "los")),
            P(("real", "los")),
            P(("real", "los"), None, "sky", None),
        ),
        out_specs=P(("real", "los"), None, "sky", None),
        check_vma=False,
    )
```
